32 devices in a mesh: ja: 4 (over x, core), ia: 8 (over z, y).
Axes of the slice: x: 2, y: 2, z: 4, core: 2. Of those that a mesh axis runs over, the one named last changes fastest.
Arguments:
- field: bfloat16 [64, 256, 384], P('ja', 'ia'), may hold values from -6 to 6
- cotangent: bfloat16 [64, 256, 384], P('ja', 'ia'), may hold values from -6 to 6
- conv_weight: float32 [7, 7, 384], replicated, may hold values from -0.875 to 0.875
- conv_bias: float32 [384], replicated, may hold values from -3 to 3
- norm_gain: float32 [384], replicated, may hold values from 0.1 to 1.9
- norm_bias: float32 [384], replicated, may hold values from -3 to 3
- up_weight: bfloat16 [384, 1536], replicated, may hold values from -0.3125 to 0.3125
- up_bias: float32 [1536], replicated, may hold values from -3 to 3
- down_weight: bfloat16 [1536, 384], replicated, may hold values from -0.15625 to 0.15625
- down_bias: float32 [384], replicated, may hold values from -3 to 3
- layer_scale: float32 [384], replicated, may hold values from 0.3 to 1.5
- ocean_mask: int32 [64, 256], P('ja', 'ia'), may hold values 0 or 1
- fold_partner: int32 [256], P('ia'), may hold values from 0 to 255, as said below
- row_owner: int32 [4], P('ja'), may hold values from 0 to 7
- up_projector_copies: float32 [384, 1024], P('ja', 'ia'), may hold values from -0.3125 to 0.3125
- down_projector_copies: float32 [384, 1024], P('ja', 'ia'), may hold values from -0.3125 to 0.3125
Outputs:
- grad_field: bfloat16 [64, 256, 384], P('ja', 'ia')
- grad_kernel: float32 [7, 7, 384], replicated
- grad_vectors: float32 [5, 384], replicated
- proj_up: float32 [128, 1536], P(None, ('ja', 'ia'))
- proj_down: float32 [1536, 128], P(('ja', 'ia'))
The draws below stay inside these ranges and needn't reach their ends.
Inputs may be any that keep to these rules, and one draw needn't show every extreme that they name: fold_partner pairs every column with another one (fold_partner[fold_partner[i]] = i, never i itself); a column of the block q * 32 to q * 32 + 31 is paired with a column of the block 8 - 1 - q.
All inputs are finite; a program needn't handle non-finite values. No bound on the sum of `ocean_mask` on one device may be relied on, other than what follows from the above.
Results may differ from the reference program's by a relative error of at most 0.0062.
Values may be sent and summed in bfloat16 or wider, within the bound.
No kernel may reach another device: no remote copies, remote signals or barrier semaphores. Data moves between devices by JAX's collectives and lax.ppermute only.
A program may use at most 64 MiB of HBM per device.

```python
import math
import jax
import jax.numpy as jnp
from jax import lax

C = 384
HID = 1536
RANK = 128
K = 7
CJ = 16
CI = 32
J = 64
I = 256
N_JA = 4
N_IA = 8


def draw_fold_partner(key, part):
    block_keys = jax.random.split(jax.random.fold_in(key, 17), N_IA)
    perms = jax.vmap(lambda one_key: jax.random.permutation(one_key, CI))(block_keys).astype(jnp.int32)
    inverse = jnp.argsort(perms, axis=1).astype(jnp.int32)
    block_ids = jnp.arange(N_IA, dtype=jnp.int32)
    mirror = N_IA - 1 - block_ids
    lower_half = block_ids < N_IA // 2
    local = jnp.where(lower_half[:, None], perms, inverse[mirror])
    return (mirror[:, None] * CI + local).reshape(-1).astype(jnp.int32)


def plant(values, rng, least, largest):
    extent = values.shape
    spot = [jax.random.randint(jax.random.fold_in(rng, axis), (), 0, extent[axis]) for axis in range(len(extent))]
    values = values.at[tuple(spot)].set(least)
    longest = extent.index(max(extent))
    spot[longest] = (spot[longest] + 1) % extent[longest]
    return values.at[tuple(spot)].set(largest)


def shard_levels(rng, shape, shards, smallest, top_value):
    loudness = 1.0
    for axis_at, shards_of in shards:
        steps = jax.random.uniform(jax.random.fold_in(jax.random.fold_in(rng, 6), axis_at), (shards_of,), jnp.float32, smallest / len(shards), top_value / len(shards))
        loudness = loudness * jnp.repeat(jnp.exp(steps), shape[axis_at] // shards_of).reshape((-1,) + (1,) * (len(shape) - 1 - axis_at))
    return loudness


def normal_values(key, extent, width, most, pieces=(), held_as=jnp.bfloat16):
    array = jax.random.normal(key, extent, jnp.float32) * width
    if len(pieces) > 0:
        array = shard_levels(key, extent, pieces, -0.22, 0.18) * array
    return jnp.clip(array, min=-most, max=most).astype(held_as)


def setup_inputs(seed: int = 0) -> dict:
    arg_keys = jax.random.split(jax.random.key(seed), 17)
    field = normal_values(arg_keys[0], (J, I, C), 1.0, 6.0, ((0, 4), (1, 8)))
    cotangent = normal_values(arg_keys[1], (J, I, C), 1.0, 6.0, ((0, 4), (1, 8)))
    conv_weight = normal_values(arg_keys[2], (K, K, C), (K * K) ** -0.5, 0.875, (), jnp.float32)
    conv_bias = normal_values(arg_keys[3], (C,), 0.5, 3.0, (), jnp.float32)
    norm_gain = jnp.clip(1.0 + 0.18 * jax.random.normal(arg_keys[4], (C,), jnp.float32), 0.1, 1.9)
    norm_bias = normal_values(arg_keys[5], (C,), 0.5, 3.0, (), jnp.float32)
    up_weight = normal_values(arg_keys[6], (C, HID), C ** -0.5, 0.3125)
    up_bias = normal_values(arg_keys[7], (HID,), 0.5, 3.0, (), jnp.float32)
    down_weight = normal_values(arg_keys[8], (HID, C), HID ** -0.5, 0.15625)
    down_bias = normal_values(arg_keys[9], (C,), 0.5, 3.0, (), jnp.float32)
    layer_scale = jnp.clip(jnp.exp(jax.random.uniform(arg_keys[10], (C,), jnp.float32, math.log(0.3), math.log(1.5))), 0.3, 1.5)
    ocean_mask = plant((jax.random.randint(arg_keys[11], (J, I), 0, 4) < 3).astype(jnp.int32), jax.random.fold_in(arg_keys[11], 1), 0, 1)
    fold_partner = draw_fold_partner(jax.random.fold_in(arg_keys[16], 71), 0)
    row_owner = plant(jax.random.randint(arg_keys[13], (N_JA,), 0, N_IA), jax.random.fold_in(arg_keys[13], 1), 0, N_IA - 1).astype(jnp.int32)
    up_projector_copies = normal_values(arg_keys[14], (C, N_IA * RANK), C ** -0.5, 0.3125, ((0, 4), (1, 8)), jnp.float32)
    down_projector_copies = normal_values(arg_keys[15], (C, N_IA * RANK), C ** -0.5, 0.3125, ((0, 4), (1, 8)), jnp.float32)
    return dict(field=field, cotangent=cotangent, conv_weight=conv_weight, conv_bias=conv_bias, norm_gain=norm_gain, norm_bias=norm_bias, up_weight=up_weight, up_bias=up_bias, down_weight=down_weight, down_bias=down_bias, layer_scale=layer_scale, ocean_mask=ocean_mask, fold_partner=fold_partner, row_owner=row_owner, up_projector_copies=up_projector_copies, down_projector_copies=down_projector_copies)


epsilon = 1e-06

def gelu_parts(pre_act):
    cdf = 0.5 * (1.0 + jax.scipy.special.erf(pre_act * 0.7071067811865476))
    dens = jnp.exp(-0.5 * pre_act * pre_act) * 0.3989422804014327
    return (pre_act * cdf, cdf + pre_act * dens)

def reference(field, cotangent, conv_weight, conv_bias, norm_gain, norm_bias, up_weight, up_bias, down_weight, down_bias, layer_scale, ocean_mask, fold_partner, row_owner, up_projector_copies, down_projector_copies):
    fold_top = field[J - 3:][::-1][:, fold_partner]
    zero_rows = jnp.zeros((3, I, C), field.dtype)
    extended = jnp.concatenate([zero_rows, field, fold_top], axis=0)
    widened = jnp.concatenate([extended[:, I - 3:], extended, extended[:, :3]], axis=1).astype(jnp.float32)
    conv_out = jnp.zeros((J, I, C), jnp.float32) + conv_bias
    for tap_row in range(K):
        for tap_col in range(K):
            conv_out = conv_out + conv_weight[tap_row, tap_col] * widened[tap_row:tap_row + J, tap_col:tap_col + I]
    block_count = J // CJ

    def one_block(carry, block_idx):
        acc_up, acc_down, acc_vec = carry
        start = (block_idx * CJ).astype(jnp.int32)
        hidden_in = lax.dynamic_slice_in_dim(conv_out, start, CJ, 0).reshape(-1, C)
        grad_out = lax.dynamic_slice_in_dim(cotangent, start, CJ, 0).reshape(-1, C).astype(jnp.float32)
        wet_cells = lax.dynamic_slice_in_dim(ocean_mask, start, CJ, 0).reshape(-1, 1).astype(jnp.float32)
        mean_val = lax.optimization_barrier(jnp.mean(hidden_in, axis=-1, keepdims=True))
        centered = hidden_in - mean_val
        variance = lax.optimization_barrier(jnp.mean(centered * centered, axis=-1, keepdims=True))
        inv_std = 1.0 / jnp.sqrt(variance + epsilon)
        normed = centered * inv_std
        mlp_in = (normed * norm_gain + norm_bias).astype(jnp.bfloat16)
        pre_act = jnp.dot(mlp_in, up_weight, preferred_element_type=jnp.float32) + up_bias
        act_val, slope = gelu_parts(pre_act)
        activated = act_val.astype(jnp.bfloat16)
        branch = jnp.dot(activated, down_weight, preferred_element_type=jnp.float32) + down_bias
        out_grad = grad_out * wet_cells * layer_scale
        out_grad_low = out_grad.astype(jnp.bfloat16)
        act_grad = jnp.dot(out_grad_low, down_weight.T, preferred_element_type=jnp.float32)
        pre_grad = (act_grad * slope).astype(jnp.bfloat16)
        in_grad = jnp.dot(pre_grad, up_weight.T, preferred_element_type=jnp.float32)
        scaled_grad = in_grad * norm_gain
        conv_grad = inv_std * (scaled_grad - lax.optimization_barrier(jnp.mean(scaled_grad, axis=-1, keepdims=True)) - normed * lax.optimization_barrier(jnp.mean(scaled_grad * normed, axis=-1, keepdims=True)))
        vec_terms = jnp.stack([lax.optimization_barrier(jnp.sum(conv_grad, 0)), lax.optimization_barrier(jnp.sum(in_grad * normed, 0)), lax.optimization_barrier(jnp.sum(in_grad, 0)), lax.optimization_barrier(jnp.sum(out_grad, 0)), lax.optimization_barrier(jnp.sum(grad_out * wet_cells * branch, 0))])
        acc_up = acc_up + jnp.dot(mlp_in.T, pre_grad, preferred_element_type=jnp.float32)
        acc_down = acc_down + jnp.dot(activated.T, out_grad_low, preferred_element_type=jnp.float32)
        return ((acc_up, acc_down, acc_vec + vec_terms), conv_grad.reshape(CJ, I, C))
    init = (jnp.zeros((C, HID), jnp.float32), jnp.zeros((HID, C), jnp.float32), jnp.zeros((5, C), jnp.float32))
    (weight_up, weight_down, vec_sum), grad_blocks = lax.scan(one_block, init, jnp.arange(block_count, dtype=jnp.int32))
    conv_grad = grad_blocks.reshape(J, I, C)
    scale = 1.0 / math.sqrt(J * I)
    kernel_rows = []
    for tap_row in range(K):
        kernel_cols = []
        for tap_col in range(K):
            kernel_cols.append(lax.optimization_barrier(jnp.sum(conv_grad * widened[tap_row:tap_row + J, tap_col:tap_col + I], axis=(0, 1))))
        kernel_rows.append(jnp.stack(kernel_cols))
    grad_kernel = jnp.stack(kernel_rows) * scale
    wrapped = jnp.concatenate([conv_grad[:, I - 3:], conv_grad, conv_grad[:, :3]], axis=1)
    padded = jnp.pad(wrapped, ((6, 6), (0, 0), (0, 0)))
    spread = jnp.zeros((J + 6, I, C), jnp.float32)
    for tap_row in range(K):
        for tap_col in range(K):
            spread = spread + conv_weight[tap_row, tap_col] * padded[6 - tap_row:6 - tap_row + J + 6, 6 - tap_col:6 - tap_col + I]
    grad_sum = cotangent.astype(jnp.float32) + spread[3:J + 3]
    grad_sum = grad_sum.at[J - 3:].add(spread[J + 3:][::-1][:, fold_partner])
    grad_field = grad_sum.astype(jnp.bfloat16)

    def assemble(copies):
        shaped = copies.reshape(N_JA, C // N_JA, N_IA, RANK)
        picked = shaped[jnp.arange(N_JA), :, row_owner]
        return picked.reshape(C, RANK)
    up_proj = assemble(up_projector_copies)
    down_proj = assemble(down_projector_copies)
    proj_up = jnp.dot(up_proj.T, weight_up, precision=lax.Precision.HIGHEST) * scale
    proj_down = jnp.dot(weight_down, down_proj, precision=lax.Precision.HIGHEST) * scale
    return (grad_field, grad_kernel, vec_sum * scale, proj_up, proj_down)
```

```python
import math

import jax
import jax.numpy as jnp
from jax import lax
from jax.sharding import PartitionSpec as P

K = 7


epsilon = 1e-06


def across_fold(block, axis):
    count = lax.axis_size(axis)
    return lax.ppermute(block, axis, [(i, count - 1 - i) for i in range(count)])


def xor_swap(block, axis, bit):
    count = lax.axis_size(axis)
    return lax.ppermute(block, axis, [(i, i ^ (1 << bit)) for i in range(count)])


def axis_bits(axis):
    count = lax.axis_size(axis)
    bits = count.bit_length() - 1
    assert 1 << bits == count
    return bits


def sum_over(block, axis):
    for bit in range(axis_bits(axis)):
        block = block + xor_swap(block, axis, bit)
    return block


def gather_over(block, axis):
    pos = lax.axis_index(axis)
    for bit in range(axis_bits(axis)):
        other = xor_swap(block, axis, bit)
        low = (pos >> bit) % 2 == 0
        block = jnp.where(low, jnp.concatenate([block, other]), jnp.concatenate([other, block]))
    return block


def scatter_sum(chunks, shared):
    ja_bits, ia_bits = axis_bits("ja"), axis_bits("ia")
    total = ja_bits + ia_bits
    rest = chunks.shape[1:]
    block = chunks.reshape((2,) * total + rest)
    steps = [("ja", b, ja_bits - 1 - b) for b in range(ja_bits)]
    steps += [("ia", b, total - 1 - b) for b in range(ia_bits)]
    for axis, bit, dim in steps:
        mine = (lax.axis_index(axis) >> bit) % 2
        keep = lax.dynamic_index_in_dim(block, mine, axis=dim, keepdims=True)
        send = lax.dynamic_index_in_dim(block, 1 - mine, axis=dim, keepdims=True)
        message = jnp.concatenate([send.reshape(-1), shared.reshape(-1)])
        got = xor_swap(message, axis, bit)
        block = keep + got[: send.size].reshape(send.shape)
        shared = shared + got[send.size :].reshape(shared.shape)
    return block.reshape(rest), shared


def with_halo(block, sides, width, periodic):
    for axis, dim in sides:
        count = lax.axis_size(axis)
        forward = [(i, i + 1) for i in range(count - 1)]
        if periodic:
            forward.append((count - 1, 0))
        backward = [(target, source) for source, target in forward]
        low = lax.ppermute(
            lax.slice_in_dim(block, block.shape[dim] - width, None, axis=dim), axis, forward
        )
        high = lax.ppermute(lax.slice_in_dim(block, 0, width, axis=dim), axis, backward)
        block = jnp.concatenate([low, block, high], axis=dim)
    return block


def gelu_parts(pre_act):
    cdf = 0.5 * (1.0 + jax.scipy.special.erf(pre_act * 0.7071067811865476))
    dens = jnp.exp(-0.5 * pre_act * pre_act) * 0.3989422804014327
    return (pre_act * cdf, cdf + pre_act * dens)


def on_device(
    field,
    cotangent,
    conv_weight,
    conv_bias,
    norm_gain,
    norm_bias,
    up_weight,
    up_bias,
    down_weight,
    down_bias,
    layer_scale,
    ocean_mask,
    fold_partner,
    row_owner,
    up_projector_copies,
    down_projector_copies,
):
    height, breadth, channels = field.shape
    row_count = lax.axis_size("ja")
    col_count = lax.axis_size("ia")
    row_pos = lax.axis_index("ja")
    col_pos = lax.axis_index("ia")
    at_top = row_pos == row_count - 1
    mirror_local = fold_partner - (col_count - 1 - col_pos) * breadth
    scale = 1.0 / math.sqrt(height * row_count * breadth * col_count)
    top_rows = field[height - 3 :][::-1]
    moved = across_fold(top_rows, "ia")
    fold_in = jnp.take(moved, mirror_local, axis=1)
    stacked = with_halo(field, (("ja", 0),), 3, False)
    upper_rows = jnp.where(at_top, fold_in, stacked[height + 3 :])
    extended = jnp.concatenate([stacked[: height + 3], upper_rows], axis=0)
    widened = with_halo(extended, (("ia", 1),), 3, True).astype(jnp.float32)
    conv_out = jnp.zeros((height, breadth, channels), jnp.float32) + conv_bias
    for tap_row in range(K):
        for tap_col in range(K):
            conv_out = (
                conv_out
                + conv_weight[tap_row, tap_col]
                * widened[tap_row : tap_row + height, tap_col : tap_col + breadth]
            )
    hidden_in = conv_out.reshape(-1, channels)
    grad_out = cotangent.reshape(-1, channels).astype(jnp.float32)
    wet_cells = ocean_mask.reshape(-1, 1).astype(jnp.float32)
    mean_val = jnp.mean(hidden_in, axis=-1, keepdims=True)
    centered = hidden_in - mean_val
    variance = jnp.mean(centered * centered, axis=-1, keepdims=True)
    inv_std = 1.0 / jnp.sqrt(variance + epsilon)
    normed = centered * inv_std
    mlp_in = (normed * norm_gain + norm_bias).astype(jnp.bfloat16)
    pre_act = jnp.dot(mlp_in, up_weight, preferred_element_type=jnp.float32) + up_bias
    act_val, slope = gelu_parts(pre_act)
    activated = act_val.astype(jnp.bfloat16)
    branch = jnp.dot(activated, down_weight, preferred_element_type=jnp.float32) + down_bias
    out_grad = grad_out * wet_cells * layer_scale
    out_grad_low = out_grad.astype(jnp.bfloat16)
    act_grad = jnp.dot(out_grad_low, down_weight.T, preferred_element_type=jnp.float32)
    pre_grad = (act_grad * slope).astype(jnp.bfloat16)
    in_grad = jnp.dot(pre_grad, up_weight.T, preferred_element_type=jnp.float32)
    scaled_grad = in_grad * norm_gain
    flat_grad = inv_std * (
        scaled_grad
        - jnp.mean(scaled_grad, axis=-1, keepdims=True)
        - normed * jnp.mean(scaled_grad * normed, axis=-1, keepdims=True)
    )
    vec_terms = jnp.stack(
        [
            jnp.sum(flat_grad, 0),
            jnp.sum(in_grad * normed, 0),
            jnp.sum(in_grad, 0),
            jnp.sum(out_grad, 0),
            jnp.sum(grad_out * wet_cells * branch, 0),
        ]
    )
    conv_grad = flat_grad.reshape(height, breadth, channels)
    kernel_rows = []
    for tap_row in range(K):
        kernel_cols = []
        for tap_col in range(K):
            kernel_cols.append(
                jnp.sum(
                    conv_grad * widened[tap_row : tap_row + height, tap_col : tap_col + breadth],
                    axis=(0, 1),
                )
            )
        kernel_rows.append(jnp.stack(kernel_cols))
    kernel_terms = jnp.stack(kernel_rows)
    padded = jnp.pad(conv_grad, ((6, 6), (6, 6), (0, 0)))
    spread = jnp.zeros((height + 6, breadth + 6, channels), jnp.float32)
    for tap_row in range(K):
        for tap_col in range(K):
            spread = (
                spread
                + conv_weight[tap_row, tap_col]
                * padded[
                    6 - tap_row : 6 - tap_row + height + 6, 6 - tap_col : 6 - tap_col + breadth + 6
                ]
            )
    rim_cols = jnp.concatenate([spread[:, :3], spread[:, breadth + 3 :]], axis=1)
    rim_cycle = with_halo(rim_cols.astype(jnp.bfloat16), (("ia", 1),), 3, True).astype(
        rim_cols.dtype
    )
    center = spread[:, 3 : breadth + 3]
    center = center.at[:, :3].add(rim_cycle[:, :3])
    center = center.at[:, breadth - 3 :].add(rim_cycle[:, 9:])
    edge_rows = jnp.concatenate([center[:3], center[height + 3 :]], axis=0)
    edge_cycle = with_halo(edge_rows.astype(jnp.bfloat16), (("ja", 0),), 3, False).astype(
        edge_rows.dtype
    )
    top_grad = center[height + 3 :]
    carried = across_fold(top_grad.astype(jnp.bfloat16), "ia").astype(top_grad.dtype)
    fold_out = jnp.take(carried, mirror_local, axis=1)
    interior = center[3 : height + 3]
    interior = interior.at[:3].add(edge_cycle[:3])
    fold_part = jnp.where(at_top, fold_out[::-1], jnp.zeros_like(fold_out))
    interior = interior.at[height - 3 :].add(edge_cycle[9:] + fold_part)
    grad_field = (cotangent.astype(jnp.float32) + interior).astype(jnp.bfloat16)
    copies_both = jnp.stack([up_projector_copies, down_projector_copies])
    mine = col_pos == row_owner[0]
    owned = sum_over(jnp.where(mine, copies_both, jnp.zeros_like(copies_both)), "ia")
    full_both = gather_over(owned[None], "ja")
    up_proj = full_both[:, 0].reshape(-1, full_both.shape[-1])
    down_proj = full_both[:, 1].reshape(-1, full_both.shape[-1])
    weight_up = jnp.dot(mlp_in.T, pre_grad, preferred_element_type=jnp.float32)
    weight_down = jnp.dot(activated.T, out_grad_low, preferred_element_type=jnp.float32)
    reduced_up = jnp.dot(up_proj.T, weight_up, precision=lax.Precision.HIGHEST)
    reduced_down = jnp.dot(weight_down, down_proj, precision=lax.Precision.HIGHEST)
    devices = row_count * col_count
    rank, hidden = reduced_up.shape
    width = hidden // devices
    up_chunks = reduced_up.reshape(rank, devices, width).transpose(1, 0, 2).reshape(devices, -1)
    down_chunks = reduced_down.reshape(devices, -1)
    shared = jnp.concatenate([vec_terms.reshape(-1), kernel_terms.reshape(-1)])
    mine_chunk, shared = scatter_sum(jnp.concatenate([up_chunks, down_chunks], axis=1), shared)
    proj_up = mine_chunk[: rank * width].reshape(rank, width) * scale
    proj_down = mine_chunk[rank * width :].reshape(width, rank) * scale
    vec_total = shared[: vec_terms.size].reshape(vec_terms.shape) * scale
    kernel_total = shared[vec_terms.size :].reshape(kernel_terms.shape) * scale
    return (grad_field, kernel_total, vec_total, proj_up, proj_down)


def solution(mesh):
    placed = (
        P("ja", "ia", None),
        P("ja", "ia", None),
        P(),
        P(),
        P(),
        P(),
        P(),
        P(),
        P(),
        P(),
        P(),
        P("ja", "ia"),
        P("ia"),
        P("ja"),
        P("ja", "ia"),
        P("ja", "ia"),
    )
    return jax.shard_map(
        on_device,
        mesh=mesh,
        in_specs=placed,
        out_specs=(P("ja", "ia", None), P(), P(), P(None, ("ja", "ia")), P(("ja", "ia"), None)),
        check_vma=False,
    )
```

```python
import math

import jax
import jax.numpy as jnp
from jax import lax
from jax.sharding import PartitionSpec as P

K = 7


epsilon = 1e-06


def across_fold(block, axis):
    count = lax.axis_size(axis)
    return lax.ppermute(block, axis, [(i, count - 1 - i) for i in range(count)])


def xor_swap(block, axis, bit):
    count = lax.axis_size(axis)
    return lax.ppermute(block, axis, [(i, i ^ (1 << bit)) for i in range(count)])


def axis_bits(axis):
    count = lax.axis_size(axis)
    bits = count.bit_length() - 1
    assert 1 << bits == count
    return bits


def sum_over(block, axis):
    for bit in range(axis_bits(axis)):
        block = block + xor_swap(block, axis, bit)
    return block


def gather_over(block, axis):
    pos = lax.axis_index(axis)
    for bit in range(axis_bits(axis)):
        other = xor_swap(block, axis, bit)
        low = (pos >> bit) % 2 == 0
        block = jnp.where(low, jnp.concatenate([block, other]), jnp.concatenate([other, block]))
    return block


def scatter_sum(chunks):
    ja_bits, ia_bits = axis_bits("ja"), axis_bits("ia")
    total = ja_bits + ia_bits
    rest = chunks.shape[1:]
    block = chunks.reshape((2,) * total + rest)
    steps = [("ja", b, ja_bits - 1 - b) for b in range(ja_bits)]
    steps += [("ia", b, total - 1 - b) for b in range(ia_bits)]
    for axis, bit, dim in steps:
        mine = (lax.axis_index(axis) >> bit) % 2
        keep = lax.dynamic_index_in_dim(block, mine, axis=dim, keepdims=True)
        send = lax.dynamic_index_in_dim(block, 1 - mine, axis=dim, keepdims=True)
        block = keep + xor_swap(send, axis, bit)
    return block.reshape(rest)


def with_halo(block, sides, width, periodic):
    for axis, dim in sides:
        count = lax.axis_size(axis)
        forward = [(i, i + 1) for i in range(count - 1)]
        if periodic:
            forward.append((count - 1, 0))
        backward = [(target, source) for source, target in forward]
        low = lax.ppermute(
            lax.slice_in_dim(block, block.shape[dim] - width, None, axis=dim), axis, forward
        )
        high = lax.ppermute(lax.slice_in_dim(block, 0, width, axis=dim), axis, backward)
        block = jnp.concatenate([low, block, high], axis=dim)
    return block


def gelu_parts(pre_act):
    cdf = 0.5 * (1.0 + jax.scipy.special.erf(pre_act * 0.7071067811865476))
    dens = jnp.exp(-0.5 * pre_act * pre_act) * 0.3989422804014327
    return (pre_act * cdf, cdf + pre_act * dens)


def on_device(
    field,
    cotangent,
    conv_weight,
    conv_bias,
    norm_gain,
    norm_bias,
    up_weight,
    up_bias,
    down_weight,
    down_bias,
    layer_scale,
    ocean_mask,
    fold_partner,
    row_owner,
    up_projector_copies,
    down_projector_copies,
):
    height, breadth, channels = field.shape
    row_count = lax.axis_size("ja")
    col_count = lax.axis_size("ia")
    row_pos = lax.axis_index("ja")
    col_pos = lax.axis_index("ia")
    at_top = row_pos == row_count - 1
    mirror_local = fold_partner - (col_count - 1 - col_pos) * breadth
    scale = 1.0 / math.sqrt(height * row_count * breadth * col_count)
    top_rows = field[height - 3 :][::-1]
    moved = across_fold(top_rows, "ia")
    fold_in = jnp.take(moved, mirror_local, axis=1)
    stacked = with_halo(field, (("ja", 0),), 3, False)
    upper_rows = jnp.where(at_top, fold_in, stacked[height + 3 :])
    extended = jnp.concatenate([stacked[: height + 3], upper_rows], axis=0)
    widened = with_halo(extended, (("ia", 1),), 3, True).astype(jnp.float32)
    conv_out = jnp.zeros((height, breadth, channels), jnp.float32) + conv_bias
    for tap_row in range(K):
        for tap_col in range(K):
            conv_out = (
                conv_out
                + conv_weight[tap_row, tap_col]
                * widened[tap_row : tap_row + height, tap_col : tap_col + breadth]
            )
    hidden_in = conv_out.reshape(-1, channels)
    grad_out = cotangent.reshape(-1, channels).astype(jnp.float32)
    wet_cells = ocean_mask.reshape(-1, 1).astype(jnp.float32)
    mean_val = jnp.mean(hidden_in, axis=-1, keepdims=True)
    centered = hidden_in - mean_val
    variance = jnp.mean(centered * centered, axis=-1, keepdims=True)
    inv_std = 1.0 / jnp.sqrt(variance + epsilon)
    normed = centered * inv_std
    mlp_in = (normed * norm_gain + norm_bias).astype(jnp.bfloat16)
    pre_act = jnp.dot(mlp_in, up_weight, preferred_element_type=jnp.float32) + up_bias
    act_val, slope = gelu_parts(pre_act)
    activated = act_val.astype(jnp.bfloat16)
    branch = jnp.dot(activated, down_weight, preferred_element_type=jnp.float32) + down_bias
    out_grad = grad_out * wet_cells * layer_scale
    out_grad_low = out_grad.astype(jnp.bfloat16)
    act_grad = jnp.dot(out_grad_low, down_weight.T, preferred_element_type=jnp.float32)
    pre_grad = (act_grad * slope).astype(jnp.bfloat16)
    in_grad = jnp.dot(pre_grad, up_weight.T, preferred_element_type=jnp.float32)
    scaled_grad = in_grad * norm_gain
    flat_grad = inv_std * (
        scaled_grad
        - jnp.mean(scaled_grad, axis=-1, keepdims=True)
        - normed * jnp.mean(scaled_grad * normed, axis=-1, keepdims=True)
    )
    vec_terms = jnp.stack(
        [
            jnp.sum(flat_grad, 0),
            jnp.sum(in_grad * normed, 0),
            jnp.sum(in_grad, 0),
            jnp.sum(out_grad, 0),
            jnp.sum(grad_out * wet_cells * branch, 0),
        ]
    )
    conv_grad = flat_grad.reshape(height, breadth, channels)
    kernel_terms = lax.conv_general_dilated(
        widened[None],
        conv_grad[:, :, None, :],
        (1, 1),
        "VALID",
        dimension_numbers=("NHWC", "HWIO", "NHWC"),
        feature_group_count=channels,
        precision=lax.Precision.HIGHEST,
    )[0]
    padded = jnp.pad(conv_grad, ((6, 6), (6, 6), (0, 0)))
    spread = jnp.zeros((height + 6, breadth + 6, channels), jnp.float32)
    for tap_row in range(K):
        for tap_col in range(K):
            spread = (
                spread
                + conv_weight[tap_row, tap_col]
                * padded[
                    6 - tap_row : 6 - tap_row + height + 6, 6 - tap_col : 6 - tap_col + breadth + 6
                ]
            )
    rim_cols = jnp.concatenate([spread[:, :3], spread[:, breadth + 3 :]], axis=1)
    rim_cycle = with_halo(rim_cols.astype(jnp.bfloat16), (("ia", 1),), 3, True).astype(
        rim_cols.dtype
    )
    center = spread[:, 3 : breadth + 3]
    center = center.at[:, :3].add(rim_cycle[:, :3])
    center = center.at[:, breadth - 3 :].add(rim_cycle[:, 9:])
    edge_rows = jnp.concatenate([center[:3], center[height + 3 :]], axis=0)
    edge_cycle = with_halo(edge_rows.astype(jnp.bfloat16), (("ja", 0),), 3, False).astype(
        edge_rows.dtype
    )
    top_grad = center[height + 3 :]
    carried = across_fold(top_grad.astype(jnp.bfloat16), "ia").astype(top_grad.dtype)
    fold_out = jnp.take(carried, mirror_local, axis=1)
    interior = center[3 : height + 3]
    interior = interior.at[:3].add(edge_cycle[:3])
    fold_part = jnp.where(at_top, fold_out[::-1], jnp.zeros_like(fold_out))
    interior = interior.at[height - 3 :].add(edge_cycle[9:] + fold_part)
    grad_field = (cotangent.astype(jnp.float32) + interior).astype(jnp.bfloat16)
    copies_both = jnp.stack([up_projector_copies, down_projector_copies])
    mine = col_pos == row_owner[0]
    owned = sum_over(jnp.where(mine, copies_both, jnp.zeros_like(copies_both)), "ia")
    full_both = gather_over(owned[None], "ja")
    up_proj = full_both[:, 0].reshape(-1, full_both.shape[-1])
    down_proj = full_both[:, 1].reshape(-1, full_both.shape[-1])
    weight_up = jnp.dot(mlp_in.T, pre_grad, preferred_element_type=jnp.float32)
    weight_down = jnp.dot(activated.T, out_grad_low, preferred_element_type=jnp.float32)
    reduced_up = jnp.dot(weight_up.T, up_proj, precision=lax.Precision.HIGHEST)
    reduced_down = jnp.dot(weight_down, down_proj, precision=lax.Precision.HIGHEST)
    devices = row_count * col_count
    hidden, rank = reduced_up.shape
    width = hidden // devices
    up_chunks = reduced_up.reshape(devices, -1)
    down_chunks = reduced_down.reshape(devices, -1)
    mine_chunk = scatter_sum(jnp.concatenate([up_chunks, down_chunks], axis=1))
    shared = jnp.concatenate([vec_terms.reshape(-1), kernel_terms.reshape(-1)])
    shared = sum_over(sum_over(shared, "ja"), "ia")
    proj_up = mine_chunk[: rank * width].reshape(width, rank).T * scale
    proj_down = mine_chunk[rank * width :].reshape(width, rank) * scale
    vec_total = shared[: vec_terms.size].reshape(vec_terms.shape) * scale
    kernel_total = shared[vec_terms.size :].reshape(kernel_terms.shape) * scale
    return (grad_field, kernel_total, vec_total, proj_up, proj_down)


def solution(mesh):
    placed = (
        P("ja", "ia", None),
        P("ja", "ia", None),
        P(),
        P(),
        P(),
        P(),
        P(),
        P(),
        P(),
        P(),
        P(),
        P("ja", "ia"),
        P("ia"),
        P("ja"),
        P("ja", "ia"),
        P("ja", "ia"),
    )
    return jax.shard_map(
        on_device,
        mesh=mesh,
        in_specs=placed,
        out_specs=(P("ja", "ia", None), P(), P(), P(None, ("ja", "ia")), P(("ja", "ia"), None)),
        check_vma=False,
    )
```

```python
import math

import jax
import jax.numpy as jnp
from jax import lax
from jax.sharding import PartitionSpec as P

K = 7


epsilon = 1e-06


def across_fold(block, axis):
    count = lax.axis_size(axis)
    return lax.ppermute(block, axis, [(i, count - 1 - i) for i in range(count)])


def xor_swap(block, axis, bit):
    count = lax.axis_size(axis)
    return lax.ppermute(block, axis, [(i, i ^ (1 << bit)) for i in range(count)])


def axis_bits(axis):
    count = lax.axis_size(axis)
    bits = count.bit_length() - 1
    assert 1 << bits == count
    return bits


def sum_over(block, axis):
    for bit in range(axis_bits(axis)):
        block = block + xor_swap(block, axis, bit)
    return block


def gather_over(block, axis):
    pos = lax.axis_index(axis)
    for bit in range(axis_bits(axis)):
        other = xor_swap(block, axis, bit)
        low = (pos >> bit) % 2 == 0
        block = jnp.where(low, jnp.concatenate([block, other]), jnp.concatenate([other, block]))
    return block


def scatter_sum(chunks, shared):
    ja_bits, ia_bits = axis_bits("ja"), axis_bits("ia")
    total = ja_bits + ia_bits
    rest = chunks.shape[1:]
    block = chunks.reshape((2,) * total + rest)
    steps = [("ja", b, ja_bits - 1 - b) for b in range(ja_bits)]
    steps += [("ia", b, total - 1 - b) for b in range(ia_bits)]
    for axis, bit, dim in steps:
        mine = (lax.axis_index(axis) >> bit) % 2
        keep = lax.dynamic_index_in_dim(block, mine, axis=dim, keepdims=True)
        send = lax.dynamic_index_in_dim(block, 1 - mine, axis=dim, keepdims=True)
        message = jnp.concatenate([send.reshape(-1), shared.reshape(-1)])
        got = xor_swap(message, axis, bit)
        block = keep + got[: send.size].reshape(send.shape)
        shared = shared + got[send.size :].reshape(shared.shape)
    return block.reshape(rest), shared


def with_halo(block, sides, width, periodic):
    for axis, dim in sides:
        count = lax.axis_size(axis)
        forward = [(i, i + 1) for i in range(count - 1)]
        if periodic:
            forward.append((count - 1, 0))
        backward = [(target, source) for source, target in forward]
        low = lax.ppermute(
            lax.slice_in_dim(block, block.shape[dim] - width, None, axis=dim), axis, forward
        )
        high = lax.ppermute(lax.slice_in_dim(block, 0, width, axis=dim), axis, backward)
        block = jnp.concatenate([low, block, high], axis=dim)
    return block


def gelu_parts(pre_act):
    cdf = 0.5 * (1.0 + jax.scipy.special.erf(pre_act * 0.7071067811865476))
    dens = jnp.exp(-0.5 * pre_act * pre_act) * 0.3989422804014327
    return (pre_act * cdf, cdf + pre_act * dens)


def on_device(
    field,
    cotangent,
    conv_weight,
    conv_bias,
    norm_gain,
    norm_bias,
    up_weight,
    up_bias,
    down_weight,
    down_bias,
    layer_scale,
    ocean_mask,
    fold_partner,
    row_owner,
    up_projector_copies,
    down_projector_copies,
):
    height, breadth, channels = field.shape
    row_count = lax.axis_size("ja")
    col_count = lax.axis_size("ia")
    row_pos = lax.axis_index("ja")
    col_pos = lax.axis_index("ia")
    at_top = row_pos == row_count - 1
    mirror_local = fold_partner - (col_count - 1 - col_pos) * breadth
    scale = 1.0 / math.sqrt(height * row_count * breadth * col_count)
    top_rows = field[height - 3 :][::-1]
    moved = across_fold(top_rows, "ia")
    fold_in = jnp.take(moved, mirror_local, axis=1)
    stacked = with_halo(field, (("ja", 0),), 3, False)
    upper_rows = jnp.where(at_top, fold_in, stacked[height + 3 :])
    extended = jnp.concatenate([stacked[: height + 3], upper_rows], axis=0)
    widened = with_halo(extended, (("ia", 1),), 3, True).astype(jnp.float32)
    conv_out = jnp.zeros((height, breadth, channels), jnp.float32) + conv_bias
    for tap_row in range(K):
        for tap_col in range(K):
            conv_out = (
                conv_out
                + conv_weight[tap_row, tap_col]
                * widened[tap_row : tap_row + height, tap_col : tap_col + breadth]
            )
    hidden_in = conv_out.reshape(-1, channels)
    grad_out = cotangent.reshape(-1, channels).astype(jnp.float32)
    wet_cells = ocean_mask.reshape(-1, 1).astype(jnp.float32)
    mean_val = jnp.mean(hidden_in, axis=-1, keepdims=True)
    centered = hidden_in - mean_val
    variance = jnp.mean(centered * centered, axis=-1, keepdims=True)
    inv_std = 1.0 / jnp.sqrt(variance + epsilon)
    normed = centered * inv_std
    mlp_in = (normed * norm_gain + norm_bias).astype(jnp.bfloat16)
    pre_act = jnp.dot(mlp_in, up_weight, preferred_element_type=jnp.float32) + up_bias
    act_val, slope = gelu_parts(pre_act)
    activated = act_val.astype(jnp.bfloat16)
    copies_both = jnp.stack([up_projector_copies, down_projector_copies])
    mine = col_pos == row_owner[0]
    owned = sum_over(jnp.where(mine, copies_both, jnp.zeros_like(copies_both)), "ia")
    full_both = gather_over(owned[None], "ja")
    full_both, activated = lax.optimization_barrier((full_both, activated))
    branch = jnp.dot(activated, down_weight, preferred_element_type=jnp.float32) + down_bias
    out_grad = grad_out * wet_cells * layer_scale
    out_grad_low = out_grad.astype(jnp.bfloat16)
    act_grad = jnp.dot(out_grad_low, down_weight.T, preferred_element_type=jnp.float32)
    pre_grad = (act_grad * slope).astype(jnp.bfloat16)
    in_grad = jnp.dot(pre_grad, up_weight.T, preferred_element_type=jnp.float32)
    scaled_grad = in_grad * norm_gain
    flat_grad = inv_std * (
        scaled_grad
        - jnp.mean(scaled_grad, axis=-1, keepdims=True)
        - normed * jnp.mean(scaled_grad * normed, axis=-1, keepdims=True)
    )
    vec_terms = jnp.stack(
        [
            jnp.sum(flat_grad, 0),
            jnp.sum(in_grad * normed, 0),
            jnp.sum(in_grad, 0),
            jnp.sum(out_grad, 0),
            jnp.sum(grad_out * wet_cells * branch, 0),
        ]
    )
    conv_grad = flat_grad.reshape(height, breadth, channels)
    kernel_terms = lax.conv_general_dilated(
        widened[None],
        conv_grad[:, :, None, :],
        (1, 1),
        "VALID",
        dimension_numbers=("NHWC", "HWIO", "NHWC"),
        feature_group_count=channels,
        precision=lax.Precision.HIGHEST,
    )[0]
    padded = jnp.pad(conv_grad, ((6, 6), (6, 6), (0, 0)))
    spread = jnp.zeros((height + 6, breadth + 6, channels), jnp.float32)
    for tap_row in range(K):
        for tap_col in range(K):
            spread = (
                spread
                + conv_weight[tap_row, tap_col]
                * padded[
                    6 - tap_row : 6 - tap_row + height + 6, 6 - tap_col : 6 - tap_col + breadth + 6
                ]
            )
    rim_cols = jnp.concatenate([spread[:, :3], spread[:, breadth + 3 :]], axis=1)
    rim_cycle = with_halo(rim_cols.astype(jnp.bfloat16), (("ia", 1),), 3, True).astype(
        rim_cols.dtype
    )
    center = spread[:, 3 : breadth + 3]
    center = center.at[:, :3].add(rim_cycle[:, :3])
    center = center.at[:, breadth - 3 :].add(rim_cycle[:, 9:])
    edge_rows = jnp.concatenate([center[:3], center[height + 3 :]], axis=0)
    edge_cycle = with_halo(edge_rows.astype(jnp.bfloat16), (("ja", 0),), 3, False).astype(
        edge_rows.dtype
    )
    top_grad = center[height + 3 :]
    carried = across_fold(top_grad.astype(jnp.bfloat16), "ia").astype(top_grad.dtype)
    fold_out = jnp.take(carried, mirror_local, axis=1)
    interior = center[3 : height + 3]
    interior = interior.at[:3].add(edge_cycle[:3])
    fold_part = jnp.where(at_top, fold_out[::-1], jnp.zeros_like(fold_out))
    interior = interior.at[height - 3 :].add(edge_cycle[9:] + fold_part)
    grad_field = (cotangent.astype(jnp.float32) + interior).astype(jnp.bfloat16)
    up_proj = full_both[:, 0].reshape(-1, full_both.shape[-1])
    down_proj = full_both[:, 1].reshape(-1, full_both.shape[-1])
    weight_up = jnp.dot(mlp_in.T, pre_grad, preferred_element_type=jnp.float32)
    weight_down = jnp.dot(activated.T, out_grad_low, preferred_element_type=jnp.float32)
    reduced_up = jnp.dot(weight_up.T, up_proj, precision=lax.Precision.HIGHEST)
    reduced_down = jnp.dot(weight_down, down_proj, precision=lax.Precision.HIGHEST)
    devices = row_count * col_count
    hidden, rank = reduced_up.shape
    width = hidden // devices
    up_chunks = reduced_up.reshape(devices, -1)
    down_chunks = reduced_down.reshape(devices, -1)
    shared = jnp.concatenate([vec_terms.reshape(-1), kernel_terms.reshape(-1)])
    payload = jnp.concatenate([up_chunks, down_chunks], axis=1)
    payload, shared, grad_field = lax.optimization_barrier((payload, shared, grad_field))
    mine_chunk, shared = scatter_sum(payload, shared)
    proj_up = mine_chunk[: rank * width].reshape(width, rank).T * scale
    proj_down = mine_chunk[rank * width :].reshape(width, rank) * scale
    vec_total = shared[: vec_terms.size].reshape(vec_terms.shape) * scale
    kernel_total = shared[vec_terms.size :].reshape(kernel_terms.shape) * scale
    return (grad_field, kernel_total, vec_total, proj_up, proj_down)


def solution(mesh):
    placed = (
        P("ja", "ia", None),
        P("ja", "ia", None),
        P(),
        P(),
        P(),
        P(),
        P(),
        P(),
        P(),
        P(),
        P(),
        P("ja", "ia"),
        P("ia"),
        P("ja"),
        P("ja", "ia"),
        P("ja", "ia"),
    )
    return jax.shard_map(
        on_device,
        mesh=mesh,
        in_specs=placed,
        out_specs=(P("ja", "ia", None), P(), P(), P(None, ("ja", "ia")), P(("ja", "ia"), None)),
        check_vma=False,
    )
```

```python
import math

import jax
import jax.numpy as jnp
from jax import lax
from jax.sharding import PartitionSpec as P

K = 7


epsilon = 1e-06


def across_fold(block, axis):
    count = lax.axis_size(axis)
    return lax.ppermute(block, axis, [(i, count - 1 - i) for i in range(count)])


def xor_swap(block, axis, bit):
    count = lax.axis_size(axis)
    return lax.ppermute(block, axis, [(i, i ^ (1 << bit)) for i in range(count)])


def axis_bits(axis):
    count = lax.axis_size(axis)
    bits = count.bit_length() - 1
    assert 1 << bits == count
    return bits


def sum_over(block, axis):
    for bit in range(axis_bits(axis)):
        block = block + xor_swap(block, axis, bit)
    return block


def gather_over(block, axis):
    pos = lax.axis_index(axis)
    for bit in range(axis_bits(axis)):
        other = xor_swap(block, axis, bit)
        low = (pos >> bit) % 2 == 0
        block = jnp.where(low, jnp.concatenate([block, other]), jnp.concatenate([other, block]))
    return block


def scatter_sum(chunks, shared):
    ja_bits, ia_bits = axis_bits("ja"), axis_bits("ia")
    total = ja_bits + ia_bits
    col_count = lax.axis_size("ia")
    rest = chunks.shape[1:]
    block = chunks.reshape((2,) * total + rest)
    dims = {("ja", b): ja_bits - 1 - b for b in range(ja_bits)}
    dims.update({("ia", b): total - 1 - b for b in range(ia_bits)})
    first = [("ja", b) for b in range(ja_bits)][:1]
    later = [("ja", b) for b in range(1, ja_bits)] + [("ia", b) for b in range(ia_bits)]
    order0 = first + later
    order1 = first + (later[1:2] + later[:1] + later[2:] if len(later) >= 2 else later)
    core = lax.axis_index("ja") % 2
    mask = lambda step: (1 << step[1]) * (col_count if step[0] == "ja" else 1)
    mine_bit = lambda step: (lax.axis_index(step[0]) >> step[1]) % 2
    devices = 1 << total
    for at, (step0, step1) in enumerate(zip(order0, order1)):
        if at == 1 and step0 != step1:
            swapped = jnp.swapaxes(block, dims[step0], dims[step1])
            block = jnp.where(core == 0, block, swapped)
        dim = dims[step0]
        mine = jnp.where(core == 0, mine_bit(step0), mine_bit(step1))
        keep = lax.dynamic_index_in_dim(block, mine, axis=dim, keepdims=True)
        send = lax.dynamic_index_in_dim(block, 1 - mine, axis=dim, keepdims=True)
        message = jnp.concatenate([send.reshape(-1), shared.reshape(-1)])
        pairs = []
        for d in range(devices):
            step = step0 if (d // col_count) % 2 == 0 else step1
            pairs.append((d, d ^ mask(step)))
        got = lax.ppermute(message, ("ja", "ia"), pairs)
        block = keep + got[: send.size].reshape(send.shape)
        shared = shared + got[send.size :].reshape(shared.shape)
    return block.reshape(rest), shared


def with_halo(block, sides, width, periodic):
    for axis, dim in sides:
        count = lax.axis_size(axis)
        forward = [(i, i + 1) for i in range(count - 1)]
        if periodic:
            forward.append((count - 1, 0))
        backward = [(target, source) for source, target in forward]
        low = lax.ppermute(
            lax.slice_in_dim(block, block.shape[dim] - width, None, axis=dim), axis, forward
        )
        high = lax.ppermute(lax.slice_in_dim(block, 0, width, axis=dim), axis, backward)
        block = jnp.concatenate([low, block, high], axis=dim)
    return block


def gelu_parts(pre_act):
    cdf = 0.5 * (1.0 + jax.scipy.special.erf(pre_act * 0.7071067811865476))
    dens = jnp.exp(-0.5 * pre_act * pre_act) * 0.3989422804014327
    return (pre_act * cdf, cdf + pre_act * dens)


def on_device(
    field,
    cotangent,
    conv_weight,
    conv_bias,
    norm_gain,
    norm_bias,
    up_weight,
    up_bias,
    down_weight,
    down_bias,
    layer_scale,
    ocean_mask,
    fold_partner,
    row_owner,
    up_projector_copies,
    down_projector_copies,
):
    height, breadth, channels = field.shape
    row_count = lax.axis_size("ja")
    col_count = lax.axis_size("ia")
    row_pos = lax.axis_index("ja")
    col_pos = lax.axis_index("ia")
    at_top = row_pos == row_count - 1
    mirror_local = fold_partner - (col_count - 1 - col_pos) * breadth
    scale = 1.0 / math.sqrt(height * row_count * breadth * col_count)
    top_rows = field[height - 3 :][::-1]
    moved = across_fold(top_rows, "ia")
    fold_in = jnp.take(moved, mirror_local, axis=1)
    stacked = with_halo(field, (("ja", 0),), 3, False)
    upper_rows = jnp.where(at_top, fold_in, stacked[height + 3 :])
    extended = jnp.concatenate([stacked[: height + 3], upper_rows], axis=0)
    widened = with_halo(extended, (("ia", 1),), 3, True).astype(jnp.float32)
    conv_out = jnp.zeros((height, breadth, channels), jnp.float32) + conv_bias
    for tap_row in range(K):
        for tap_col in range(K):
            conv_out = (
                conv_out
                + conv_weight[tap_row, tap_col]
                * widened[tap_row : tap_row + height, tap_col : tap_col + breadth]
            )
    hidden_in = conv_out.reshape(-1, channels)
    grad_out = cotangent.reshape(-1, channels).astype(jnp.float32)
    wet_cells = ocean_mask.reshape(-1, 1).astype(jnp.float32)
    mean_val = jnp.mean(hidden_in, axis=-1, keepdims=True)
    centered = hidden_in - mean_val
    variance = jnp.mean(centered * centered, axis=-1, keepdims=True)
    inv_std = 1.0 / jnp.sqrt(variance + epsilon)
    normed = centered * inv_std
    mlp_in = (normed * norm_gain + norm_bias).astype(jnp.bfloat16)
    pre_act = jnp.dot(mlp_in, up_weight, preferred_element_type=jnp.float32) + up_bias
    act_val, slope = gelu_parts(pre_act)
    activated = act_val.astype(jnp.bfloat16)
    copies_both = jnp.stack([up_projector_copies, down_projector_copies])
    mine = col_pos == row_owner[0]
    owned = sum_over(jnp.where(mine, copies_both, jnp.zeros_like(copies_both)), "ia")
    full_both = gather_over(owned[None], "ja")
    full_both, activated = lax.optimization_barrier((full_both, activated))
    branch = jnp.dot(activated, down_weight, preferred_element_type=jnp.float32) + down_bias
    out_grad = grad_out * wet_cells * layer_scale
    out_grad_low = out_grad.astype(jnp.bfloat16)
    act_grad = jnp.dot(out_grad_low, down_weight.T, preferred_element_type=jnp.float32)
    pre_grad = (act_grad * slope).astype(jnp.bfloat16)
    in_grad = jnp.dot(pre_grad, up_weight.T, preferred_element_type=jnp.float32)
    scaled_grad = in_grad * norm_gain
    flat_grad = inv_std * (
        scaled_grad
        - jnp.mean(scaled_grad, axis=-1, keepdims=True)
        - normed * jnp.mean(scaled_grad * normed, axis=-1, keepdims=True)
    )
    vec_terms = jnp.stack(
        [
            jnp.sum(flat_grad, 0),
            jnp.sum(in_grad * normed, 0),
            jnp.sum(in_grad, 0),
            jnp.sum(out_grad, 0),
            jnp.sum(grad_out * wet_cells * branch, 0),
        ]
    )
    conv_grad = flat_grad.reshape(height, breadth, channels)
    kernel_terms = lax.conv_general_dilated(
        widened[None],
        conv_grad[:, :, None, :],
        (1, 1),
        "VALID",
        dimension_numbers=("NHWC", "HWIO", "NHWC"),
        feature_group_count=channels,
        precision=lax.Precision.HIGHEST,
    )[0]
    padded = jnp.pad(conv_grad, ((6, 6), (6, 6), (0, 0)))
    spread = jnp.zeros((height + 6, breadth + 6, channels), jnp.float32)
    for tap_row in range(K):
        for tap_col in range(K):
            spread = (
                spread
                + conv_weight[tap_row, tap_col]
                * padded[
                    6 - tap_row : 6 - tap_row + height + 6, 6 - tap_col : 6 - tap_col + breadth + 6
                ]
            )
    rim_cols = jnp.concatenate([spread[:, :3], spread[:, breadth + 3 :]], axis=1)
    rim_cycle = with_halo(rim_cols.astype(jnp.bfloat16), (("ia", 1),), 3, True).astype(
        rim_cols.dtype
    )
    center = spread[:, 3 : breadth + 3]
    center = center.at[:, :3].add(rim_cycle[:, :3])
    center = center.at[:, breadth - 3 :].add(rim_cycle[:, 9:])
    edge_rows = jnp.concatenate([center[:3], center[height + 3 :]], axis=0)
    edge_cycle = with_halo(edge_rows.astype(jnp.bfloat16), (("ja", 0),), 3, False).astype(
        edge_rows.dtype
    )
    top_grad = center[height + 3 :]
    carried = across_fold(top_grad.astype(jnp.bfloat16), "ia").astype(top_grad.dtype)
    fold_out = jnp.take(carried, mirror_local, axis=1)
    interior = center[3 : height + 3]
    interior = interior.at[:3].add(edge_cycle[:3])
    fold_part = jnp.where(at_top, fold_out[::-1], jnp.zeros_like(fold_out))
    interior = interior.at[height - 3 :].add(edge_cycle[9:] + fold_part)
    grad_field = (cotangent.astype(jnp.float32) + interior).astype(jnp.bfloat16)
    up_proj = full_both[:, 0].reshape(-1, full_both.shape[-1])
    down_proj = full_both[:, 1].reshape(-1, full_both.shape[-1])
    weight_up = jnp.dot(mlp_in.T, pre_grad, preferred_element_type=jnp.float32)
    weight_down = jnp.dot(activated.T, out_grad_low, preferred_element_type=jnp.float32)
    reduced_up = jnp.dot(weight_up.T, up_proj, precision=lax.Precision.HIGHEST)
    reduced_down = jnp.dot(weight_down, down_proj, precision=lax.Precision.HIGHEST)
    devices = row_count * col_count
    hidden, rank = reduced_up.shape
    width = hidden // devices
    up_chunks = reduced_up.reshape(devices, -1)
    down_chunks = reduced_down.reshape(devices, -1)
    shared = jnp.concatenate([vec_terms.reshape(-1), kernel_terms.reshape(-1)])
    payload = jnp.concatenate([up_chunks, down_chunks], axis=1)
    payload, shared, grad_field = lax.optimization_barrier((payload, shared, grad_field))
    mine_chunk, shared = scatter_sum(payload, shared)
    proj_up = mine_chunk[: rank * width].reshape(width, rank).T * scale
    proj_down = mine_chunk[rank * width :].reshape(width, rank) * scale
    vec_total = shared[: vec_terms.size].reshape(vec_terms.shape) * scale
    kernel_total = shared[vec_terms.size :].reshape(kernel_terms.shape) * scale
    return (grad_field, kernel_total, vec_total, proj_up, proj_down)


def solution(mesh):
    placed = (
        P("ja", "ia", None),
        P("ja", "ia", None),
        P(),
        P(),
        P(),
        P(),
        P(),
        P(),
        P(),
        P(),
        P(),
        P("ja", "ia"),
        P("ia"),
        P("ja"),
        P("ja", "ia"),
        P("ja", "ia"),
    )
    return jax.shard_map(
        on_device,
        mesh=mesh,
        in_specs=placed,
        out_specs=(P("ja", "ia", None), P(), P(), P(None, ("ja", "ia")), P(("ja", "ia"), None)),
        check_vma=False,
    )
```

```python
import math

import jax
import jax.numpy as jnp
from jax import lax
from jax.sharding import PartitionSpec as P

K = 7


epsilon = 1e-06


def across_fold(block, axis):
    count = lax.axis_size(axis)
    return lax.ppermute(block, axis, [(i, count - 1 - i) for i in range(count)])


def xor_swap(block, axis, bit):
    count = lax.axis_size(axis)
    return lax.ppermute(block, axis, [(i, i ^ (1 << bit)) for i in range(count)])


def axis_bits(axis):
    count = lax.axis_size(axis)
    bits = count.bit_length() - 1
    assert 1 << bits == count
    return bits


def sum_over(block, axis):
    for bit in range(axis_bits(axis)):
        block = block + xor_swap(block, axis, bit)
    return block


def gather_over(block, axis):
    pos = lax.axis_index(axis)
    for bit in range(axis_bits(axis)):
        other = xor_swap(block, axis, bit)
        low = (pos >> bit) % 2 == 0
        block = jnp.where(low, jnp.concatenate([block, other]), jnp.concatenate([other, block]))
    return block


def scatter_sum(chunks, shared):
    ja_bits, ia_bits = axis_bits("ja"), axis_bits("ia")
    total = ja_bits + ia_bits
    col_count = lax.axis_size("ia")
    rest = chunks.shape[1:]
    block = chunks.reshape((2,) * total + rest)
    dims = {("ja", b): ja_bits - 1 - b for b in range(ja_bits)}
    dims.update({("ia", b): total - 1 - b for b in range(ia_bits)})
    first = [("ja", b) for b in range(ja_bits)][:1]
    later = [("ja", b) for b in range(1, ja_bits)] + [("ia", b) for b in range(ia_bits)]
    order0 = first + later
    order1 = first + (later[1:2] + later[:1] + later[2:] if len(later) >= 2 else later)
    core = lax.axis_index("ja") % 2
    mask = lambda step: (1 << step[1]) * (col_count if step[0] == "ja" else 1)
    mine_bit = lambda step: (lax.axis_index(step[0]) >> step[1]) % 2
    devices = 1 << total
    lanes = rest[-1]
    count = -(-shared.size // lanes)
    count = -(-count // 8) * 8
    rows = jnp.pad(shared.reshape(-1), (0, count * lanes - shared.size)).reshape(count, lanes)
    for at, (step0, step1) in enumerate(zip(order0, order1)):
        if at == 1 and step0 != step1:
            swapped = jnp.swapaxes(block, dims[step0], dims[step1])
            block = jnp.where(core == 0, block, swapped)
        dim = dims[step0]
        mine = jnp.where(core == 0, mine_bit(step0), mine_bit(step1))
        keep = lax.dynamic_index_in_dim(block, mine, axis=dim, keepdims=True)
        send = lax.dynamic_index_in_dim(block, 1 - mine, axis=dim, keepdims=True)
        pairs = []
        for d in range(devices):
            step = step0 if (d // col_count) % 2 == 0 else step1
            pairs.append((d, d ^ mask(step)))
        lanes = send.shape[-1]
        message = jnp.concatenate([send.reshape(-1, lanes), rows], axis=0)
        got = lax.ppermute(message, ("ja", "ia"), pairs)
        block = keep + got[: send.size // lanes].reshape(send.shape)
        rows = rows + got[send.size // lanes :]
    flat = rows.reshape(-1)[: shared.size]
    return block.reshape(rest), flat.reshape(shared.shape)


def with_halo(block, sides, width, periodic):
    for axis, dim in sides:
        count = lax.axis_size(axis)
        forward = [(i, i + 1) for i in range(count - 1)]
        if periodic:
            forward.append((count - 1, 0))
        backward = [(target, source) for source, target in forward]
        low = lax.ppermute(
            lax.slice_in_dim(block, block.shape[dim] - width, None, axis=dim), axis, forward
        )
        high = lax.ppermute(lax.slice_in_dim(block, 0, width, axis=dim), axis, backward)
        block = jnp.concatenate([low, block, high], axis=dim)
    return block


def gelu_parts(pre_act):
    cdf = 0.5 * (1.0 + jax.scipy.special.erf(pre_act * 0.7071067811865476))
    dens = jnp.exp(-0.5 * pre_act * pre_act) * 0.3989422804014327
    return (pre_act * cdf, cdf + pre_act * dens)


def on_device(
    field,
    cotangent,
    conv_weight,
    conv_bias,
    norm_gain,
    norm_bias,
    up_weight,
    up_bias,
    down_weight,
    down_bias,
    layer_scale,
    ocean_mask,
    fold_partner,
    row_owner,
    up_projector_copies,
    down_projector_copies,
):
    height, breadth, channels = field.shape
    row_count = lax.axis_size("ja")
    col_count = lax.axis_size("ia")
    row_pos = lax.axis_index("ja")
    col_pos = lax.axis_index("ia")
    at_top = row_pos == row_count - 1
    mirror_local = fold_partner - (col_count - 1 - col_pos) * breadth
    scale = 1.0 / math.sqrt(height * row_count * breadth * col_count)
    top_rows = field[height - 3 :][::-1]
    moved = across_fold(top_rows, "ia")
    fold_in = jnp.take(moved, mirror_local, axis=1)
    stacked = with_halo(field, (("ja", 0),), 3, False)
    upper_rows = jnp.where(at_top, fold_in, stacked[height + 3 :])
    extended = jnp.concatenate([stacked[: height + 3], upper_rows], axis=0)
    widened = with_halo(extended, (("ia", 1),), 3, True).astype(jnp.float32)
    conv_out = jnp.zeros((height, breadth, channels), jnp.float32) + conv_bias
    for tap_row in range(K):
        for tap_col in range(K):
            conv_out = (
                conv_out
                + conv_weight[tap_row, tap_col]
                * widened[tap_row : tap_row + height, tap_col : tap_col + breadth]
            )
    hidden_in = conv_out.reshape(-1, channels)
    grad_out = cotangent.reshape(-1, channels).astype(jnp.float32)
    wet_cells = ocean_mask.reshape(-1, 1).astype(jnp.float32)
    mean_val = jnp.mean(hidden_in, axis=-1, keepdims=True)
    centered = hidden_in - mean_val
    variance = jnp.mean(centered * centered, axis=-1, keepdims=True)
    inv_std = 1.0 / jnp.sqrt(variance + epsilon)
    normed = centered * inv_std
    mlp_in = (normed * norm_gain + norm_bias).astype(jnp.bfloat16)
    pre_act = jnp.dot(mlp_in, up_weight, preferred_element_type=jnp.float32) + up_bias
    act_val, slope = gelu_parts(pre_act)
    activated = act_val.astype(jnp.bfloat16)
    copies_both = jnp.stack([up_projector_copies, down_projector_copies])
    mine = col_pos == row_owner[0]
    owned = sum_over(jnp.where(mine, copies_both, jnp.zeros_like(copies_both)), "ia")
    full_both = gather_over(owned[None], "ja")
    full_both, activated = lax.optimization_barrier((full_both, activated))
    branch = jnp.dot(activated, down_weight, preferred_element_type=jnp.float32) + down_bias
    out_grad = grad_out * wet_cells * layer_scale
    out_grad_low = out_grad.astype(jnp.bfloat16)
    act_grad = jnp.dot(out_grad_low, down_weight.T, preferred_element_type=jnp.float32)
    pre_grad = (act_grad * slope).astype(jnp.bfloat16)
    in_grad = jnp.dot(pre_grad, up_weight.T, preferred_element_type=jnp.float32)
    scaled_grad = in_grad * norm_gain
    flat_grad = inv_std * (
        scaled_grad
        - jnp.mean(scaled_grad, axis=-1, keepdims=True)
        - normed * jnp.mean(scaled_grad * normed, axis=-1, keepdims=True)
    )
    vec_terms = jnp.stack(
        [
            jnp.sum(flat_grad, 0),
            jnp.sum(in_grad * normed, 0),
            jnp.sum(in_grad, 0),
            jnp.sum(out_grad, 0),
            jnp.sum(grad_out * wet_cells * branch, 0),
        ]
    )
    conv_grad = flat_grad.reshape(height, breadth, channels)
    kernel_terms = lax.conv_general_dilated(
        widened[None],
        conv_grad[:, :, None, :],
        (1, 1),
        "VALID",
        dimension_numbers=("NHWC", "HWIO", "NHWC"),
        feature_group_count=channels,
        precision=lax.Precision.HIGHEST,
    )[0]
    padded = jnp.pad(conv_grad, ((6, 6), (6, 6), (0, 0)))
    spread = jnp.zeros((height + 6, breadth + 6, channels), jnp.float32)
    for tap_row in range(K):
        for tap_col in range(K):
            spread = (
                spread
                + conv_weight[tap_row, tap_col]
                * padded[
                    6 - tap_row : 6 - tap_row + height + 6, 6 - tap_col : 6 - tap_col + breadth + 6
                ]
            )
    rim_cols = jnp.concatenate([spread[:, :3], spread[:, breadth + 3 :]], axis=1)
    rim_cycle = with_halo(rim_cols.astype(jnp.bfloat16), (("ia", 1),), 3, True).astype(
        rim_cols.dtype
    )
    center = spread[:, 3 : breadth + 3]
    center = center.at[:, :3].add(rim_cycle[:, :3])
    center = center.at[:, breadth - 3 :].add(rim_cycle[:, 9:])
    edge_rows = jnp.concatenate([center[:3], center[height + 3 :]], axis=0)
    edge_cycle = with_halo(edge_rows.astype(jnp.bfloat16), (("ja", 0),), 3, False).astype(
        edge_rows.dtype
    )
    top_grad = center[height + 3 :]
    carried = across_fold(top_grad.astype(jnp.bfloat16), "ia").astype(top_grad.dtype)
    fold_out = jnp.take(carried, mirror_local, axis=1)
    interior = center[3 : height + 3]
    interior = interior.at[:3].add(edge_cycle[:3])
    fold_part = jnp.where(at_top, fold_out[::-1], jnp.zeros_like(fold_out))
    interior = interior.at[height - 3 :].add(edge_cycle[9:] + fold_part)
    grad_field = (cotangent.astype(jnp.float32) + interior).astype(jnp.bfloat16)
    up_proj = full_both[:, 0].reshape(-1, full_both.shape[-1])
    down_proj = full_both[:, 1].reshape(-1, full_both.shape[-1])
    weight_up = jnp.dot(mlp_in.T, pre_grad, preferred_element_type=jnp.float32)
    weight_down = jnp.dot(activated.T, out_grad_low, preferred_element_type=jnp.float32)
    reduced_up = jnp.dot(weight_up.T, up_proj, precision=lax.Precision.HIGHEST)
    reduced_down = jnp.dot(weight_down, down_proj, precision=lax.Precision.HIGHEST)
    devices = row_count * col_count
    hidden, rank = reduced_up.shape
    width = hidden // devices
    shared = jnp.concatenate([vec_terms, kernel_terms.reshape(-1, channels)])
    payload = jnp.concatenate([reduced_up, reduced_down], axis=1).reshape(devices, width, 2 * rank)
    payload, shared, grad_field = lax.optimization_barrier((payload, shared, grad_field))
    mine_chunk, shared = scatter_sum(payload, shared)
    proj_up = mine_chunk[:, :rank].T * scale
    proj_down = mine_chunk[:, rank:] * scale
    vec_total = shared[: vec_terms.shape[0]] * scale
    kernel_total = shared[vec_terms.shape[0] :].reshape(kernel_terms.shape) * scale
    return (grad_field, kernel_total, vec_total, proj_up, proj_down)


def solution(mesh):
    placed = (
        P("ja", "ia", None),
        P("ja", "ia", None),
        P(),
        P(),
        P(),
        P(),
        P(),
        P(),
        P(),
        P(),
        P(),
        P("ja", "ia"),
        P("ia"),
        P("ja"),
        P("ja", "ia"),
        P("ja", "ia"),
    )
    return jax.shard_map(
        on_device,
        mesh=mesh,
        in_specs=placed,
        out_specs=(P("ja", "ia", None), P(), P(), P(None, ("ja", "ia")), P(("ja", "ia"), None)),
        check_vma=False,
    )
```

```python
import math

import jax
import jax.numpy as jnp
from jax import lax
from jax.sharding import PartitionSpec as P

K = 7


epsilon = 1e-06


def across_fold(block, axis):
    count = lax.axis_size(axis)
    return lax.ppermute(block, axis, [(i, count - 1 - i) for i in range(count)])


def xor_swap(block, axis, bit):
    count = lax.axis_size(axis)
    return lax.ppermute(block, axis, [(i, i ^ (1 << bit)) for i in range(count)])


def axis_bits(axis):
    count = lax.axis_size(axis)
    bits = count.bit_length() - 1
    assert 1 << bits == count
    return bits


def sum_over(block, axis):
    for bit in range(axis_bits(axis)):
        block = block + xor_swap(block, axis, bit)
    return block


def gather_over(block, axis):
    pos = lax.axis_index(axis)
    for bit in range(axis_bits(axis)):
        other = xor_swap(block, axis, bit)
        low = (pos >> bit) % 2 == 0
        block = jnp.where(low, jnp.concatenate([block, other]), jnp.concatenate([other, block]))
    return block


def scatter_sum(chunks, shared):
    ja_bits, ia_bits = axis_bits("ja"), axis_bits("ia")
    total = ja_bits + ia_bits
    col_count = lax.axis_size("ia")
    rest = chunks.shape[1:]
    block = chunks.reshape((2,) * total + rest)
    dims = {("ja", b): ja_bits - 1 - b for b in range(ja_bits)}
    dims.update({("ia", b): total - 1 - b for b in range(ia_bits)})
    first = [("ja", b) for b in range(ja_bits)][:1]
    later = [("ja", b) for b in range(1, ja_bits)] + [("ia", b) for b in range(ia_bits)]
    order0 = first + later
    order1 = first + (later[1:2] + later[:1] + later[2:] if len(later) >= 2 else later)
    core = lax.axis_index("ja") % 2
    mask = lambda step: (1 << step[1]) * (col_count if step[0] == "ja" else 1)
    mine_bit = lambda step: (lax.axis_index(step[0]) >> step[1]) % 2
    devices = 1 << total
    lanes = rest[-1]
    count = -(-shared.size // lanes)
    count = -(-count // 8) * 8
    rows = jnp.pad(shared.reshape(-1), (0, count * lanes - shared.size)).reshape(count, lanes)
    for at, (step0, step1) in enumerate(zip(order0, order1)):
        if at == 1 and step0 != step1:
            swapped = jnp.swapaxes(block, dims[step0], dims[step1])
            block = jnp.where(core == 0, block, swapped)
        dim = dims[step0]
        mine = jnp.where(core == 0, mine_bit(step0), mine_bit(step1))
        keep = lax.dynamic_index_in_dim(block, mine, axis=dim, keepdims=True)
        send = lax.dynamic_index_in_dim(block, 1 - mine, axis=dim, keepdims=True)
        pairs = []
        for d in range(devices):
            step = step0 if (d // col_count) % 2 == 0 else step1
            pairs.append((d, d ^ mask(step)))
        lanes = send.shape[-1]
        message = jnp.concatenate([send.reshape(-1, lanes), rows], axis=0)
        got = lax.ppermute(message, ("ja", "ia"), pairs)
        block = keep + got[: send.size // lanes].reshape(send.shape)
        rows = rows + got[send.size // lanes :]
    flat = rows.reshape(-1)[: shared.size]
    return block.reshape(rest), flat.reshape(shared.shape)


def with_halo(block, sides, width, periodic):
    for axis, dim in sides:
        count = lax.axis_size(axis)
        forward = [(i, i + 1) for i in range(count - 1)]
        if periodic:
            forward.append((count - 1, 0))
        backward = [(target, source) for source, target in forward]
        low = lax.ppermute(
            lax.slice_in_dim(block, block.shape[dim] - width, None, axis=dim), axis, forward
        )
        high = lax.ppermute(lax.slice_in_dim(block, 0, width, axis=dim), axis, backward)
        block = jnp.concatenate([low, block, high], axis=dim)
    return block


def pick_columns(block, index):
    count = block.shape[1]
    select = (index[:, None] == jnp.arange(count)[None, :]).astype(block.dtype)
    return jnp.einsum("ik,akc->aic", select, block, preferred_element_type=jnp.float32)


def gelu_parts(pre_act):
    cdf = 0.5 * (1.0 + jax.scipy.special.erf(pre_act * 0.7071067811865476))
    dens = jnp.exp(-0.5 * pre_act * pre_act) * 0.3989422804014327
    return (pre_act * cdf, cdf + pre_act * dens)


def on_device(
    field,
    cotangent,
    conv_weight,
    conv_bias,
    norm_gain,
    norm_bias,
    up_weight,
    up_bias,
    down_weight,
    down_bias,
    layer_scale,
    ocean_mask,
    fold_partner,
    row_owner,
    up_projector_copies,
    down_projector_copies,
):
    height, breadth, channels = field.shape
    row_count = lax.axis_size("ja")
    col_count = lax.axis_size("ia")
    row_pos = lax.axis_index("ja")
    col_pos = lax.axis_index("ia")
    at_top = row_pos == row_count - 1
    mirror_local = fold_partner - (col_count - 1 - col_pos) * breadth
    scale = 1.0 / math.sqrt(height * row_count * breadth * col_count)
    top_rows = field[height - 3 :][::-1]
    moved = across_fold(top_rows, "ia")
    fold_in = pick_columns(moved, mirror_local).astype(moved.dtype)
    stacked = with_halo(field, (("ja", 0),), 3, False)
    upper_rows = jnp.where(at_top, fold_in, stacked[height + 3 :])
    extended = jnp.concatenate([stacked[: height + 3], upper_rows], axis=0)
    widened = with_halo(extended, (("ia", 1),), 3, True).astype(jnp.float32)
    conv_out = jnp.zeros((height, breadth, channels), jnp.float32) + conv_bias
    for tap_row in range(K):
        for tap_col in range(K):
            conv_out = (
                conv_out
                + conv_weight[tap_row, tap_col]
                * widened[tap_row : tap_row + height, tap_col : tap_col + breadth]
            )
    hidden_in = conv_out.reshape(-1, channels)
    grad_out = cotangent.reshape(-1, channels).astype(jnp.float32)
    wet_cells = ocean_mask.reshape(-1, 1).astype(jnp.float32)
    mean_val = jnp.mean(hidden_in, axis=-1, keepdims=True)
    centered = hidden_in - mean_val
    variance = jnp.mean(centered * centered, axis=-1, keepdims=True)
    inv_std = 1.0 / jnp.sqrt(variance + epsilon)
    normed = centered * inv_std
    mlp_in = (normed * norm_gain + norm_bias).astype(jnp.bfloat16)
    pre_act = jnp.dot(mlp_in, up_weight, preferred_element_type=jnp.float32) + up_bias
    act_val, slope = gelu_parts(pre_act)
    activated = act_val.astype(jnp.bfloat16)
    copies_both = jnp.stack([up_projector_copies, down_projector_copies])
    mine = col_pos == row_owner[0]
    owned = sum_over(jnp.where(mine, copies_both, jnp.zeros_like(copies_both)), "ia")
    full_both = gather_over(owned[None], "ja")
    full_both, activated = lax.optimization_barrier((full_both, activated))
    branch = jnp.dot(activated, down_weight, preferred_element_type=jnp.float32) + down_bias
    out_grad = grad_out * wet_cells * layer_scale
    out_grad_low = out_grad.astype(jnp.bfloat16)
    act_grad = jnp.dot(out_grad_low, down_weight.T, preferred_element_type=jnp.float32)
    pre_grad = (act_grad * slope).astype(jnp.bfloat16)
    in_grad = jnp.dot(pre_grad, up_weight.T, preferred_element_type=jnp.float32)
    scaled_grad = in_grad * norm_gain
    flat_grad = inv_std * (
        scaled_grad
        - jnp.mean(scaled_grad, axis=-1, keepdims=True)
        - normed * jnp.mean(scaled_grad * normed, axis=-1, keepdims=True)
    )
    vec_terms = jnp.stack(
        [
            jnp.sum(flat_grad, 0),
            jnp.sum(in_grad * normed, 0),
            jnp.sum(in_grad, 0),
            jnp.sum(out_grad, 0),
            jnp.sum(grad_out * wet_cells * branch, 0),
        ]
    )
    conv_grad = flat_grad.reshape(height, breadth, channels)
    kernel_terms = lax.conv_general_dilated(
        widened[None],
        conv_grad[:, :, None, :],
        (1, 1),
        "VALID",
        dimension_numbers=("NHWC", "HWIO", "NHWC"),
        feature_group_count=channels,
        precision=lax.Precision.HIGHEST,
    )[0]
    padded = jnp.pad(conv_grad, ((6, 6), (6, 6), (0, 0)))
    spread = jnp.zeros((height + 6, breadth + 6, channels), jnp.float32)
    for tap_row in range(K):
        for tap_col in range(K):
            spread = (
                spread
                + conv_weight[tap_row, tap_col]
                * padded[
                    6 - tap_row : 6 - tap_row + height + 6, 6 - tap_col : 6 - tap_col + breadth + 6
                ]
            )
    rim_cols = jnp.concatenate([spread[:, :3], spread[:, breadth + 3 :]], axis=1)
    rim_cycle = with_halo(rim_cols.astype(jnp.bfloat16), (("ia", 1),), 3, True).astype(
        rim_cols.dtype
    )
    center = (
        spread[:, 3 : breadth + 3]
        + jnp.pad(rim_cycle[:, :3], ((0, 0), (0, breadth - 3), (0, 0)))
        + jnp.pad(rim_cycle[:, 9:], ((0, 0), (breadth - 3, 0), (0, 0)))
    )
    edge_rows = jnp.concatenate([center[:3], center[height + 3 :]], axis=0)
    edge_cycle = with_halo(edge_rows.astype(jnp.bfloat16), (("ja", 0),), 3, False).astype(
        edge_rows.dtype
    )
    top_grad = center[height + 3 :]
    carried = across_fold(top_grad.astype(jnp.bfloat16), "ia")
    fold_out = pick_columns(carried, mirror_local)
    fold_part = jnp.where(at_top, fold_out[::-1], jnp.zeros_like(fold_out))
    interior = (
        center[3 : height + 3]
        + jnp.pad(edge_cycle[:3], ((0, height - 3), (0, 0), (0, 0)))
        + jnp.pad(edge_cycle[9:] + fold_part, ((height - 3, 0), (0, 0), (0, 0)))
    )
    grad_field = (cotangent.astype(jnp.float32) + interior).astype(jnp.bfloat16)
    up_proj = full_both[:, 0].reshape(-1, full_both.shape[-1])
    down_proj = full_both[:, 1].reshape(-1, full_both.shape[-1])
    weight_up = jnp.dot(mlp_in.T, pre_grad, preferred_element_type=jnp.float32)
    weight_down = jnp.dot(activated.T, out_grad_low, preferred_element_type=jnp.float32)
    reduced_up = jnp.dot(weight_up.T, up_proj, precision=lax.Precision.HIGHEST)
    reduced_down = jnp.dot(weight_down, down_proj, precision=lax.Precision.HIGHEST)
    devices = row_count * col_count
    hidden, rank = reduced_up.shape
    width = hidden // devices
    shared = jnp.concatenate([vec_terms, kernel_terms.reshape(-1, channels)])
    payload = jnp.concatenate([reduced_up, reduced_down], axis=1).reshape(devices, width, 2 * rank)
    payload, shared, grad_field = lax.optimization_barrier((payload, shared, grad_field))
    mine_chunk, shared = scatter_sum(payload, shared)
    proj_up = mine_chunk[:, :rank].T * scale
    proj_down = mine_chunk[:, rank:] * scale
    vec_total = shared[: vec_terms.shape[0]] * scale
    kernel_total = shared[vec_terms.shape[0] :].reshape(kernel_terms.shape) * scale
    return (grad_field, kernel_total, vec_total, proj_up, proj_down)


def solution(mesh):
    placed = (
        P("ja", "ia", None),
        P("ja", "ia", None),
        P(),
        P(),
        P(),
        P(),
        P(),
        P(),
        P(),
        P(),
        P(),
        P("ja", "ia"),
        P("ia"),
        P("ja"),
        P("ja", "ia"),
        P("ja", "ia"),
    )
    return jax.shard_map(
        on_device,
        mesh=mesh,
        in_specs=placed,
        out_specs=(P("ja", "ia", None), P(), P(), P(None, ("ja", "ia")), P(("ja", "ia"), None)),
        check_vma=False,
    )
```

```python
import math

import jax
import jax.numpy as jnp
from jax import lax
from jax.sharding import PartitionSpec as P

K = 7


epsilon = 1e-06


def across_fold(block, axis):
    count = lax.axis_size(axis)
    return lax.ppermute(block, axis, [(i, count - 1 - i) for i in range(count)])


def xor_swap(block, axis, bit):
    count = lax.axis_size(axis)
    return lax.ppermute(block, axis, [(i, i ^ (1 << bit)) for i in range(count)])


def axis_bits(axis):
    count = lax.axis_size(axis)
    bits = count.bit_length() - 1
    assert 1 << bits == count
    return bits


def sum_over(block, axis):
    for bit in range(axis_bits(axis)):
        block = block + xor_swap(block, axis, bit)
    return block


def gather_over(block, axis):
    pos = lax.axis_index(axis)
    for bit in range(axis_bits(axis)):
        other = xor_swap(block, axis, bit)
        low = (pos >> bit) % 2 == 0
        block = jnp.where(low, jnp.concatenate([block, other]), jnp.concatenate([other, block]))
    return block


def scatter_sum(chunks, shared):
    ja_bits, ia_bits = axis_bits("ja"), axis_bits("ia")
    total = ja_bits + ia_bits
    col_count = lax.axis_size("ia")
    rest = chunks.shape[1:]
    block = chunks.reshape((2,) * total + rest)
    dims = {("ja", b): ja_bits - 1 - b for b in range(ja_bits)}
    dims.update({("ia", b): total - 1 - b for b in range(ia_bits)})
    first = [("ja", b) for b in range(ja_bits)][:1]
    later = [("ja", b) for b in range(1, ja_bits)] + [("ia", b) for b in range(ia_bits)]
    order0 = first + later
    order1 = first + (later[1:2] + later[:1] + later[2:] if len(later) >= 2 else later)
    core = lax.axis_index("ja") % 2
    mask = lambda step: (1 << step[1]) * (col_count if step[0] == "ja" else 1)
    mine_bit = lambda step: (lax.axis_index(step[0]) >> step[1]) % 2
    devices = 1 << total
    lanes = rest[-1]
    count = -(-shared.size // lanes)
    count = -(-count // 8) * 8
    rows = jnp.pad(shared.reshape(-1), (0, count * lanes - shared.size)).reshape(count, lanes)
    for at, (step0, step1) in enumerate(zip(order0, order1)):
        if at == 1 and step0 != step1:
            swapped = jnp.swapaxes(block, dims[step0], dims[step1])
            block = jnp.where(core == 0, block, swapped)
        dim = dims[step0]
        mine = jnp.where(core == 0, mine_bit(step0), mine_bit(step1))
        keep = lax.dynamic_index_in_dim(block, mine, axis=dim, keepdims=True)
        send = lax.dynamic_index_in_dim(block, 1 - mine, axis=dim, keepdims=True)
        pairs = []
        for d in range(devices):
            step = step0 if (d // col_count) % 2 == 0 else step1
            pairs.append((d, d ^ mask(step)))
        lanes = send.shape[-1]
        message = jnp.concatenate([send.reshape(-1, lanes), rows], axis=0)
        got = lax.ppermute(message, ("ja", "ia"), pairs)
        block = keep + got[: send.size // lanes].reshape(send.shape)
        rows = rows + got[send.size // lanes :]
    flat = rows.reshape(-1)[: shared.size]
    return block.reshape(rest), flat.reshape(shared.shape)


def with_halo(block, sides, width, periodic):
    for axis, dim in sides:
        count = lax.axis_size(axis)
        forward = [(i, i + 1) for i in range(count - 1)]
        if periodic:
            forward.append((count - 1, 0))
        backward = [(target, source) for source, target in forward]
        low = lax.ppermute(
            lax.slice_in_dim(block, block.shape[dim] - width, None, axis=dim), axis, forward
        )
        high = lax.ppermute(lax.slice_in_dim(block, 0, width, axis=dim), axis, backward)
        block = jnp.concatenate([low, block, high], axis=dim)
    return block


def pick_columns(block, index):
    count = block.shape[1]
    select = (index[:, None] == jnp.arange(count)[None, :]).astype(block.dtype)
    return jnp.einsum("ik,akc->aic", select, block, preferred_element_type=jnp.float32)


def gelu_parts(pre_act):
    cdf = 0.5 * (1.0 + jax.scipy.special.erf(pre_act * 0.7071067811865476))
    dens = jnp.exp(-0.5 * pre_act * pre_act) * 0.3989422804014327
    return (pre_act * cdf, cdf + pre_act * dens)


def on_device(
    field,
    cotangent,
    conv_weight,
    conv_bias,
    norm_gain,
    norm_bias,
    up_weight,
    up_bias,
    down_weight,
    down_bias,
    layer_scale,
    ocean_mask,
    fold_partner,
    row_owner,
    up_projector_copies,
    down_projector_copies,
):
    height, breadth, channels = field.shape
    row_count = lax.axis_size("ja")
    col_count = lax.axis_size("ia")
    row_pos = lax.axis_index("ja")
    col_pos = lax.axis_index("ia")
    at_top = row_pos == row_count - 1
    mirror_local = fold_partner - (col_count - 1 - col_pos) * breadth
    scale = 1.0 / math.sqrt(height * row_count * breadth * col_count)
    top_rows = field[height - 3 :][::-1]
    moved = across_fold(top_rows, "ia")
    fold_in = pick_columns(moved, mirror_local).astype(moved.dtype)
    stacked = with_halo(field, (("ja", 0),), 3, False)
    upper_rows = jnp.where(at_top, fold_in, stacked[height + 3 :])
    extended = jnp.concatenate([stacked[: height + 3], upper_rows], axis=0)
    widened = with_halo(extended, (("ia", 1),), 3, True).astype(jnp.float32)
    conv_out = jnp.zeros((height, breadth, channels), jnp.float32) + conv_bias
    for tap_row in range(K):
        for tap_col in range(K):
            conv_out = (
                conv_out
                + conv_weight[tap_row, tap_col]
                * widened[tap_row : tap_row + height, tap_col : tap_col + breadth]
            )
    hidden_in = conv_out.reshape(-1, channels)
    grad_out = cotangent.reshape(-1, channels).astype(jnp.float32)
    wet_cells = ocean_mask.reshape(-1, 1).astype(jnp.float32)
    mean_val = jnp.mean(hidden_in, axis=-1, keepdims=True)
    centered = hidden_in - mean_val
    variance = jnp.mean(centered * centered, axis=-1, keepdims=True)
    inv_std = 1.0 / jnp.sqrt(variance + epsilon)
    normed = centered * inv_std
    mlp_in = (normed * norm_gain + norm_bias).astype(jnp.bfloat16)
    pre_act = jnp.dot(mlp_in, up_weight, preferred_element_type=jnp.float32) + up_bias
    act_val, slope = gelu_parts(pre_act)
    activated = act_val.astype(jnp.bfloat16)
    copies_both = jnp.stack([up_projector_copies, down_projector_copies])
    mine = col_pos == row_owner[0]
    owned = sum_over(jnp.where(mine, copies_both, jnp.zeros_like(copies_both)), "ia")
    full_both = gather_over(owned[None], "ja")
    full_both, activated = lax.optimization_barrier((full_both, activated))
    branch = jnp.dot(activated, down_weight, preferred_element_type=jnp.float32) + down_bias
    out_grad = grad_out * wet_cells * layer_scale
    out_grad_low = out_grad.astype(jnp.bfloat16)
    act_grad = jnp.dot(out_grad_low, down_weight.T, preferred_element_type=jnp.float32)
    pre_grad = (act_grad * slope).astype(jnp.bfloat16)
    in_grad = jnp.dot(pre_grad, up_weight.T, preferred_element_type=jnp.float32)
    scaled_grad = in_grad * norm_gain
    flat_grad = inv_std * (
        scaled_grad
        - jnp.mean(scaled_grad, axis=-1, keepdims=True)
        - normed * jnp.mean(scaled_grad * normed, axis=-1, keepdims=True)
    )
    vec_terms = jnp.stack(
        [
            jnp.sum(flat_grad, 0),
            jnp.sum(in_grad * normed, 0),
            jnp.sum(in_grad, 0),
            jnp.sum(out_grad, 0),
            jnp.sum(grad_out * wet_cells * branch, 0),
        ]
    )
    conv_grad = flat_grad.reshape(height, breadth, channels)
    kernel_terms = lax.conv_general_dilated(
        widened[None],
        conv_grad[:, :, None, :],
        (1, 1),
        "VALID",
        dimension_numbers=("NHWC", "HWIO", "NHWC"),
        feature_group_count=channels,
        precision=lax.Precision.HIGHEST,
    )[0]
    up_proj = full_both[:, 0].reshape(-1, full_both.shape[-1])
    down_proj = full_both[:, 1].reshape(-1, full_both.shape[-1])
    weight_up = jnp.dot(mlp_in.T, pre_grad, preferred_element_type=jnp.float32)
    weight_down = jnp.dot(activated.T, out_grad_low, preferred_element_type=jnp.float32)
    reduced_up = jnp.dot(weight_up.T, up_proj, precision=lax.Precision.HIGHEST)
    reduced_down = jnp.dot(weight_down, down_proj, precision=lax.Precision.HIGHEST)
    devices = row_count * col_count
    hidden, rank = reduced_up.shape
    width = hidden // devices
    shared = jnp.concatenate([vec_terms, kernel_terms.reshape(-1, channels)])
    payload = jnp.concatenate([reduced_up, reduced_down], axis=1).reshape(devices, width, 2 * rank)
    payload, shared, conv_grad = lax.optimization_barrier((payload, shared, conv_grad))
    padded = jnp.pad(conv_grad, ((6, 6), (6, 6), (0, 0)))
    spread = jnp.zeros((height + 6, breadth + 6, channels), jnp.float32)
    for tap_row in range(K):
        for tap_col in range(K):
            spread = (
                spread
                + conv_weight[tap_row, tap_col]
                * padded[
                    6 - tap_row : 6 - tap_row + height + 6, 6 - tap_col : 6 - tap_col + breadth + 6
                ]
            )
    rim_cols = jnp.concatenate([spread[:, :3], spread[:, breadth + 3 :]], axis=1)
    rim_cycle = with_halo(rim_cols.astype(jnp.bfloat16), (("ia", 1),), 3, True).astype(
        rim_cols.dtype
    )
    center = (
        spread[:, 3 : breadth + 3]
        + jnp.pad(rim_cycle[:, :3], ((0, 0), (0, breadth - 3), (0, 0)))
        + jnp.pad(rim_cycle[:, 9:], ((0, 0), (breadth - 3, 0), (0, 0)))
    )
    edge_rows = jnp.concatenate([center[:3], center[height + 3 :]], axis=0)
    edge_cycle = with_halo(edge_rows.astype(jnp.bfloat16), (("ja", 0),), 3, False).astype(
        edge_rows.dtype
    )
    top_grad = center[height + 3 :]
    carried = across_fold(top_grad.astype(jnp.bfloat16), "ia")
    fold_out = pick_columns(carried, mirror_local)
    fold_part = jnp.where(at_top, fold_out[::-1], jnp.zeros_like(fold_out))
    interior = (
        center[3 : height + 3]
        + jnp.pad(edge_cycle[:3], ((0, height - 3), (0, 0), (0, 0)))
        + jnp.pad(edge_cycle[9:] + fold_part, ((height - 3, 0), (0, 0), (0, 0)))
    )
    grad_field = (cotangent.astype(jnp.float32) + interior).astype(jnp.bfloat16)
    mine_chunk, shared = scatter_sum(payload, shared)
    proj_up = mine_chunk[:, :rank].T * scale
    proj_down = mine_chunk[:, rank:] * scale
    vec_total = shared[: vec_terms.shape[0]] * scale
    kernel_total = shared[vec_terms.shape[0] :].reshape(kernel_terms.shape) * scale
    return (grad_field, kernel_total, vec_total, proj_up, proj_down)


def solution(mesh):
    placed = (
        P("ja", "ia", None),
        P("ja", "ia", None),
        P(),
        P(),
        P(),
        P(),
        P(),
        P(),
        P(),
        P(),
        P(),
        P("ja", "ia"),
        P("ia"),
        P("ja"),
        P("ja", "ia"),
        P("ja", "ia"),
    )
    return jax.shard_map(
        on_device,
        mesh=mesh,
        in_specs=placed,
        out_specs=(P("ja", "ia", None), P(), P(), P(None, ("ja", "ia")), P(("ja", "ia"), None)),
        check_vma=False,
    )
```

```python
import math

import jax
import jax.numpy as jnp
from jax import lax
from jax.sharding import PartitionSpec as P

K = 7


epsilon = 1e-06


def across_fold(block, axis):
    count = lax.axis_size(axis)
    return lax.ppermute(block, axis, [(i, count - 1 - i) for i in range(count)])


def xor_swap(block, axis, bit):
    count = lax.axis_size(axis)
    return lax.ppermute(block, axis, [(i, i ^ (1 << bit)) for i in range(count)])


def axis_bits(axis):
    count = lax.axis_size(axis)
    bits = count.bit_length() - 1
    assert 1 << bits == count
    return bits


def sum_over(block, axis):
    for bit in range(axis_bits(axis)):
        block = block + xor_swap(block, axis, bit)
    return block


def gather_over(block, axis):
    pos = lax.axis_index(axis)
    for bit in range(axis_bits(axis)):
        other = xor_swap(block, axis, bit)
        low = (pos >> bit) % 2 == 0
        block = jnp.where(low, jnp.concatenate([block, other]), jnp.concatenate([other, block]))
    return block


def scatter_sum(chunks, shared):
    ja_bits, ia_bits = axis_bits("ja"), axis_bits("ia")
    total = ja_bits + ia_bits
    col_count = lax.axis_size("ia")
    rest = chunks.shape[1:]
    block = chunks.reshape((2,) * total + rest)
    dims = {("ja", b): ja_bits - 1 - b for b in range(ja_bits)}
    dims.update({("ia", b): total - 1 - b for b in range(ia_bits)})
    first = [("ja", b) for b in range(ja_bits)][:1]
    later = [("ja", b) for b in range(1, ja_bits)] + [("ia", b) for b in range(ia_bits)]
    order0 = first + later
    order1 = first + (later[1:2] + later[:1] + later[2:] if len(later) >= 2 else later)
    core = lax.axis_index("ja") % 2
    mask = lambda step: (1 << step[1]) * (col_count if step[0] == "ja" else 1)
    mine_bit = lambda step: (lax.axis_index(step[0]) >> step[1]) % 2
    devices = 1 << total
    lanes = rest[-1]
    count = -(-shared.size // lanes)
    count = -(-count // 8) * 8
    rows = jnp.pad(shared.reshape(-1), (0, count * lanes - shared.size)).reshape(count, lanes)
    for at, (step0, step1) in enumerate(zip(order0, order1)):
        if at == 1 and step0 != step1:
            swapped = jnp.swapaxes(block, dims[step0], dims[step1])
            block = jnp.where(core == 0, block, swapped)
        dim = dims[step0]
        mine = jnp.where(core == 0, mine_bit(step0), mine_bit(step1))
        keep = lax.dynamic_index_in_dim(block, mine, axis=dim, keepdims=True)
        send = lax.dynamic_index_in_dim(block, 1 - mine, axis=dim, keepdims=True)
        pairs = []
        for d in range(devices):
            step = step0 if (d // col_count) % 2 == 0 else step1
            pairs.append((d, d ^ mask(step)))
        lanes = send.shape[-1]
        message = jnp.concatenate([send.reshape(-1, lanes), rows], axis=0)
        got = lax.ppermute(message, ("ja", "ia"), pairs)
        block = keep + got[: send.size // lanes].reshape(send.shape)
        rows = rows + got[send.size // lanes :]
    flat = rows.reshape(-1)[: shared.size]
    return block.reshape(rest), flat.reshape(shared.shape)


def with_halo(block, sides, width, periodic):
    for axis, dim in sides:
        count = lax.axis_size(axis)
        forward = [(i, i + 1) for i in range(count - 1)]
        if periodic:
            forward.append((count - 1, 0))
        backward = [(target, source) for source, target in forward]
        low = lax.ppermute(
            lax.slice_in_dim(block, block.shape[dim] - width, None, axis=dim), axis, forward
        )
        high = lax.ppermute(lax.slice_in_dim(block, 0, width, axis=dim), axis, backward)
        block = jnp.concatenate([low, block, high], axis=dim)
    return block


def pick_columns(block, index):
    count = block.shape[1]
    select = (index[:, None] == jnp.arange(count)[None, :]).astype(block.dtype)
    return jnp.einsum("ik,akc->aic", select, block, preferred_element_type=jnp.float32)


def gelu_parts(pre_act):
    cdf = 0.5 * (1.0 + jax.scipy.special.erf(pre_act * 0.7071067811865476))
    dens = jnp.exp(-0.5 * pre_act * pre_act) * 0.3989422804014327
    return (pre_act * cdf, cdf + pre_act * dens)


def on_device(
    field,
    cotangent,
    conv_weight,
    conv_bias,
    norm_gain,
    norm_bias,
    up_weight,
    up_bias,
    down_weight,
    down_bias,
    layer_scale,
    ocean_mask,
    fold_partner,
    row_owner,
    up_projector_copies,
    down_projector_copies,
):
    height, breadth, channels = field.shape
    row_count = lax.axis_size("ja")
    col_count = lax.axis_size("ia")
    row_pos = lax.axis_index("ja")
    col_pos = lax.axis_index("ia")
    at_top = row_pos == row_count - 1
    mirror_local = fold_partner - (col_count - 1 - col_pos) * breadth
    scale = 1.0 / math.sqrt(height * row_count * breadth * col_count)
    top_rows = field[height - 3 :][::-1]
    moved = across_fold(top_rows, "ia")
    fold_in = pick_columns(moved, mirror_local).astype(moved.dtype)
    stacked = with_halo(field, (("ja", 0),), 3, False)
    upper_rows = jnp.where(at_top, fold_in, stacked[height + 3 :])
    extended = jnp.concatenate([stacked[: height + 3], upper_rows], axis=0)
    widened = with_halo(extended, (("ia", 1),), 3, True).astype(jnp.float32)
    conv_out = jnp.zeros((height, breadth, channels), jnp.float32) + conv_bias
    for tap_row in range(K):
        for tap_col in range(K):
            conv_out = (
                conv_out
                + conv_weight[tap_row, tap_col]
                * widened[tap_row : tap_row + height, tap_col : tap_col + breadth]
            )
    hidden_in = conv_out.reshape(-1, channels)
    grad_out = cotangent.reshape(-1, channels).astype(jnp.float32)
    wet_cells = ocean_mask.reshape(-1, 1).astype(jnp.float32)
    mean_val = jnp.mean(hidden_in, axis=-1, keepdims=True)
    centered = hidden_in - mean_val
    variance = jnp.mean(centered * centered, axis=-1, keepdims=True)
    inv_std = 1.0 / jnp.sqrt(variance + epsilon)
    normed = centered * inv_std
    mlp_in = (normed * norm_gain + norm_bias).astype(jnp.bfloat16)
    pre_act = jnp.dot(mlp_in, up_weight, preferred_element_type=jnp.float32) + up_bias
    act_val, slope = gelu_parts(pre_act)
    activated = act_val.astype(jnp.bfloat16)
    copies_both = jnp.stack([up_projector_copies, down_projector_copies])
    mine = col_pos == row_owner[0]
    owned = jnp.where(mine, copies_both, jnp.zeros_like(copies_both))
    owned = lax.all_to_all(
        jnp.broadcast_to(owned[None], (col_count,) + owned.shape), "ia", 0, 0, tiled=True
    ).sum(0)
    full_both = lax.all_to_all(
        jnp.broadcast_to(owned[None], (row_count,) + owned.shape), "ja", 0, 0, tiled=True
    )
    full_both, activated = lax.optimization_barrier((full_both, activated))
    branch = jnp.dot(activated, down_weight, preferred_element_type=jnp.float32) + down_bias
    out_grad = grad_out * wet_cells * layer_scale
    out_grad_low = out_grad.astype(jnp.bfloat16)
    act_grad = jnp.dot(out_grad_low, down_weight.T, preferred_element_type=jnp.float32)
    pre_grad = (act_grad * slope).astype(jnp.bfloat16)
    in_grad = jnp.dot(pre_grad, up_weight.T, preferred_element_type=jnp.float32)
    scaled_grad = in_grad * norm_gain
    flat_grad = inv_std * (
        scaled_grad
        - jnp.mean(scaled_grad, axis=-1, keepdims=True)
        - normed * jnp.mean(scaled_grad * normed, axis=-1, keepdims=True)
    )
    vec_terms = jnp.stack(
        [
            jnp.sum(flat_grad, 0),
            jnp.sum(in_grad * normed, 0),
            jnp.sum(in_grad, 0),
            jnp.sum(out_grad, 0),
            jnp.sum(grad_out * wet_cells * branch, 0),
        ]
    )
    conv_grad = flat_grad.reshape(height, breadth, channels)
    kernel_terms = lax.conv_general_dilated(
        widened[None],
        conv_grad[:, :, None, :],
        (1, 1),
        "VALID",
        dimension_numbers=("NHWC", "HWIO", "NHWC"),
        feature_group_count=channels,
        precision=lax.Precision.HIGHEST,
    )[0]
    up_proj = full_both[:, 0].reshape(-1, full_both.shape[-1])
    down_proj = full_both[:, 1].reshape(-1, full_both.shape[-1])
    weight_up = jnp.dot(mlp_in.T, pre_grad, preferred_element_type=jnp.float32)
    weight_down = jnp.dot(activated.T, out_grad_low, preferred_element_type=jnp.float32)
    reduced_up = jnp.dot(weight_up.T, up_proj, precision=lax.Precision.HIGHEST)
    reduced_down = jnp.dot(weight_down, down_proj, precision=lax.Precision.HIGHEST)
    devices = row_count * col_count
    hidden, rank = reduced_up.shape
    width = hidden // devices
    shared = jnp.concatenate([vec_terms, kernel_terms.reshape(-1, channels)])
    payload = jnp.concatenate([reduced_up, reduced_down], axis=1).reshape(devices, width, 2 * rank)
    payload, shared, conv_grad = lax.optimization_barrier((payload, shared, conv_grad))
    padded = jnp.pad(conv_grad, ((6, 6), (6, 6), (0, 0)))
    spread = jnp.zeros((height + 6, breadth + 6, channels), jnp.float32)
    for tap_row in range(K):
        for tap_col in range(K):
            spread = (
                spread
                + conv_weight[tap_row, tap_col]
                * padded[
                    6 - tap_row : 6 - tap_row + height + 6, 6 - tap_col : 6 - tap_col + breadth + 6
                ]
            )
    rim_cols = jnp.concatenate([spread[:, :3], spread[:, breadth + 3 :]], axis=1)
    rim_cycle = with_halo(rim_cols.astype(jnp.bfloat16), (("ia", 1),), 3, True).astype(
        rim_cols.dtype
    )
    center = (
        spread[:, 3 : breadth + 3]
        + jnp.pad(rim_cycle[:, :3], ((0, 0), (0, breadth - 3), (0, 0)))
        + jnp.pad(rim_cycle[:, 9:], ((0, 0), (breadth - 3, 0), (0, 0)))
    )
    edge_rows = jnp.concatenate([center[:3], center[height + 3 :]], axis=0)
    edge_cycle = with_halo(edge_rows.astype(jnp.bfloat16), (("ja", 0),), 3, False).astype(
        edge_rows.dtype
    )
    top_grad = center[height + 3 :]
    carried = across_fold(top_grad.astype(jnp.bfloat16), "ia")
    fold_out = pick_columns(carried, mirror_local)
    fold_part = jnp.where(at_top, fold_out[::-1], jnp.zeros_like(fold_out))
    interior = (
        center[3 : height + 3]
        + jnp.pad(edge_cycle[:3], ((0, height - 3), (0, 0), (0, 0)))
        + jnp.pad(edge_cycle[9:] + fold_part, ((height - 3, 0), (0, 0), (0, 0)))
    )
    grad_field = (cotangent.astype(jnp.float32) + interior).astype(jnp.bfloat16)
    mine_chunk, shared = scatter_sum(payload, shared)
    proj_up = mine_chunk[:, :rank].T * scale
    proj_down = mine_chunk[:, rank:] * scale
    vec_total = shared[: vec_terms.shape[0]] * scale
    kernel_total = shared[vec_terms.shape[0] :].reshape(kernel_terms.shape) * scale
    return (grad_field, kernel_total, vec_total, proj_up, proj_down)


def solution(mesh):
    placed = (
        P("ja", "ia", None),
        P("ja", "ia", None),
        P(),
        P(),
        P(),
        P(),
        P(),
        P(),
        P(),
        P(),
        P(),
        P("ja", "ia"),
        P("ia"),
        P("ja"),
        P("ja", "ia"),
        P("ja", "ia"),
    )
    return jax.shard_map(
        on_device,
        mesh=mesh,
        in_specs=placed,
        out_specs=(P("ja", "ia", None), P(), P(), P(None, ("ja", "ia")), P(("ja", "ia"), None)),
        check_vma=False,
    )
```

```python
import math

import jax
import jax.numpy as jnp
from jax import lax
from jax.sharding import PartitionSpec as P

K = 7


epsilon = 1e-06


def across_fold(block, axis):
    count = lax.axis_size(axis)
    return lax.ppermute(block, axis, [(i, count - 1 - i) for i in range(count)])


def xor_swap(block, axis, bit):
    count = lax.axis_size(axis)
    return lax.ppermute(block, axis, [(i, i ^ (1 << bit)) for i in range(count)])


def axis_bits(axis):
    count = lax.axis_size(axis)
    bits = count.bit_length() - 1
    assert 1 << bits == count
    return bits


def sum_over(block, axis):
    for bit in range(axis_bits(axis)):
        block = block + xor_swap(block, axis, bit)
    return block


def gather_over(block, axis):
    pos = lax.axis_index(axis)
    for bit in range(axis_bits(axis)):
        other = xor_swap(block, axis, bit)
        low = (pos >> bit) % 2 == 0
        block = jnp.where(low, jnp.concatenate([block, other]), jnp.concatenate([other, block]))
    return block


def scatter_sum(chunks, shared):
    ja_bits, ia_bits = axis_bits("ja"), axis_bits("ia")
    total = ja_bits + ia_bits
    col_count = lax.axis_size("ia")
    rest = chunks.shape[1:]
    block = chunks.reshape((2,) * total + rest)
    dims = {("ja", b): ja_bits - 1 - b for b in range(ja_bits)}
    dims.update({("ia", b): total - 1 - b for b in range(ia_bits)})
    first = [("ja", b) for b in range(ja_bits)][:1]
    later = [("ja", b) for b in range(1, ja_bits)] + [("ia", b) for b in range(ia_bits)]
    order0 = first + later
    order1 = first + (later[1:2] + later[:1] + later[2:] if len(later) >= 2 else later)
    core = lax.axis_index("ja") % 2
    mask = lambda step: (1 << step[1]) * (col_count if step[0] == "ja" else 1)
    mine_bit = lambda step: (lax.axis_index(step[0]) >> step[1]) % 2
    devices = 1 << total
    lanes = rest[-1]
    count = -(-shared.size // lanes)
    count = -(-count // 8) * 8
    rows = jnp.pad(shared.reshape(-1), (0, count * lanes - shared.size)).reshape(count, lanes)
    for at, (step0, step1) in enumerate(zip(order0, order1)):
        if at == 1 and step0 != step1:
            swapped = jnp.swapaxes(block, dims[step0], dims[step1])
            block = jnp.where(core == 0, block, swapped)
        dim = dims[step0]
        mine = jnp.where(core == 0, mine_bit(step0), mine_bit(step1))
        keep = lax.dynamic_index_in_dim(block, mine, axis=dim, keepdims=True)
        send = lax.dynamic_index_in_dim(block, 1 - mine, axis=dim, keepdims=True)
        pairs = []
        for d in range(devices):
            step = step0 if (d // col_count) % 2 == 0 else step1
            pairs.append((d, d ^ mask(step)))
        lanes = send.shape[-1]
        message = jnp.concatenate([send.reshape(-1, lanes), rows], axis=0)
        got = lax.ppermute(message, ("ja", "ia"), pairs)
        block = keep + got[: send.size // lanes].reshape(send.shape)
        rows = rows + got[send.size // lanes :]
    flat = rows.reshape(-1)[: shared.size]
    return block.reshape(rest), flat.reshape(shared.shape)


def with_halo(block, sides, width, periodic):
    for axis, dim in sides:
        count = lax.axis_size(axis)
        forward = [(i, i + 1) for i in range(count - 1)]
        if periodic:
            forward.append((count - 1, 0))
        backward = [(target, source) for source, target in forward]
        low = lax.ppermute(
            lax.slice_in_dim(block, block.shape[dim] - width, None, axis=dim), axis, forward
        )
        high = lax.ppermute(lax.slice_in_dim(block, 0, width, axis=dim), axis, backward)
        block = jnp.concatenate([low, block, high], axis=dim)
    return block


def pick_columns(block, index):
    count = block.shape[1]
    select = (index[:, None] == jnp.arange(count)[None, :]).astype(block.dtype)
    return jnp.einsum("ik,akc->aic", select, block, preferred_element_type=jnp.float32)


def gelu_parts(pre_act):
    cdf = 0.5 * (1.0 + jax.scipy.special.erf(pre_act * 0.7071067811865476))
    dens = jnp.exp(-0.5 * pre_act * pre_act) * 0.3989422804014327
    return (pre_act * cdf, cdf + pre_act * dens)


def on_device(
    field,
    cotangent,
    conv_weight,
    conv_bias,
    norm_gain,
    norm_bias,
    up_weight,
    up_bias,
    down_weight,
    down_bias,
    layer_scale,
    ocean_mask,
    fold_partner,
    row_owner,
    up_projector_copies,
    down_projector_copies,
):
    height, breadth, channels = field.shape
    row_count = lax.axis_size("ja")
    col_count = lax.axis_size("ia")
    row_pos = lax.axis_index("ja")
    col_pos = lax.axis_index("ia")
    at_top = row_pos == row_count - 1
    mirror_local = fold_partner - (col_count - 1 - col_pos) * breadth
    scale = 1.0 / math.sqrt(height * row_count * breadth * col_count)
    top_rows = field[height - 3 :][::-1]
    moved = across_fold(top_rows, "ia")
    fold_in = pick_columns(moved, mirror_local).astype(moved.dtype)
    stacked = with_halo(field, (("ja", 0),), 3, False)
    upper_rows = jnp.where(at_top, fold_in, stacked[height + 3 :])
    extended = jnp.concatenate([stacked[: height + 3], upper_rows], axis=0)
    widened = with_halo(extended, (("ia", 1),), 3, True).astype(jnp.float32)
    copies_both = jnp.stack([up_projector_copies, down_projector_copies])
    mine = col_pos == row_owner[0]
    owned = jnp.where(mine, copies_both, jnp.zeros_like(copies_both))
    for bit in range(min(2, axis_bits("ia"))):
        owned = owned + xor_swap(owned, "ia", bit)
    owned, widened = lax.optimization_barrier((owned, widened))
    conv_out = jnp.zeros((height, breadth, channels), jnp.float32) + conv_bias
    for tap_row in range(K):
        for tap_col in range(K):
            conv_out = (
                conv_out
                + conv_weight[tap_row, tap_col]
                * widened[tap_row : tap_row + height, tap_col : tap_col + breadth]
            )
    hidden_in = conv_out.reshape(-1, channels)
    grad_out = cotangent.reshape(-1, channels).astype(jnp.float32)
    wet_cells = ocean_mask.reshape(-1, 1).astype(jnp.float32)
    mean_val = jnp.mean(hidden_in, axis=-1, keepdims=True)
    centered = hidden_in - mean_val
    variance = jnp.mean(centered * centered, axis=-1, keepdims=True)
    inv_std = 1.0 / jnp.sqrt(variance + epsilon)
    normed = centered * inv_std
    mlp_in = (normed * norm_gain + norm_bias).astype(jnp.bfloat16)
    pre_act = jnp.dot(mlp_in, up_weight, preferred_element_type=jnp.float32) + up_bias
    act_val, slope = gelu_parts(pre_act)
    activated = act_val.astype(jnp.bfloat16)
    for bit in range(2, axis_bits("ia")):
        owned = owned + xor_swap(owned, "ia", bit)
    full_both = gather_over(owned[None], "ja")
    full_both, activated = lax.optimization_barrier((full_both, activated))
    branch = jnp.dot(activated, down_weight, preferred_element_type=jnp.float32) + down_bias
    out_grad = grad_out * wet_cells * layer_scale
    out_grad_low = out_grad.astype(jnp.bfloat16)
    act_grad = jnp.dot(out_grad_low, down_weight.T, preferred_element_type=jnp.float32)
    pre_grad = (act_grad * slope).astype(jnp.bfloat16)
    in_grad = jnp.dot(pre_grad, up_weight.T, preferred_element_type=jnp.float32)
    scaled_grad = in_grad * norm_gain
    flat_grad = inv_std * (
        scaled_grad
        - jnp.mean(scaled_grad, axis=-1, keepdims=True)
        - normed * jnp.mean(scaled_grad * normed, axis=-1, keepdims=True)
    )
    vec_terms = jnp.stack(
        [
            jnp.sum(flat_grad, 0),
            jnp.sum(in_grad * normed, 0),
            jnp.sum(in_grad, 0),
            jnp.sum(out_grad, 0),
            jnp.sum(grad_out * wet_cells * branch, 0),
        ]
    )
    conv_grad = flat_grad.reshape(height, breadth, channels)
    kernel_terms = lax.conv_general_dilated(
        widened[None],
        conv_grad[:, :, None, :],
        (1, 1),
        "VALID",
        dimension_numbers=("NHWC", "HWIO", "NHWC"),
        feature_group_count=channels,
        precision=lax.Precision.HIGHEST,
    )[0]
    up_proj = full_both[:, 0].reshape(-1, full_both.shape[-1])
    down_proj = full_both[:, 1].reshape(-1, full_both.shape[-1])
    weight_up = jnp.dot(mlp_in.T, pre_grad, preferred_element_type=jnp.float32)
    weight_down = jnp.dot(activated.T, out_grad_low, preferred_element_type=jnp.float32)
    reduced_up = jnp.dot(weight_up.T, up_proj, precision=lax.Precision.HIGHEST)
    reduced_down = jnp.dot(weight_down, down_proj, precision=lax.Precision.HIGHEST)
    devices = row_count * col_count
    hidden, rank = reduced_up.shape
    width = hidden // devices
    shared = jnp.concatenate([vec_terms, kernel_terms.reshape(-1, channels)])
    payload = jnp.concatenate([reduced_up, reduced_down], axis=1).reshape(devices, width, 2 * rank)
    payload, shared, conv_grad = lax.optimization_barrier((payload, shared, conv_grad))
    padded = jnp.pad(conv_grad, ((6, 6), (6, 6), (0, 0)))
    spread = jnp.zeros((height + 6, breadth + 6, channels), jnp.float32)
    for tap_row in range(K):
        for tap_col in range(K):
            spread = (
                spread
                + conv_weight[tap_row, tap_col]
                * padded[
                    6 - tap_row : 6 - tap_row + height + 6, 6 - tap_col : 6 - tap_col + breadth + 6
                ]
            )
    rim_cols = jnp.concatenate([spread[:, :3], spread[:, breadth + 3 :]], axis=1)
    rim_cycle = with_halo(rim_cols.astype(jnp.bfloat16), (("ia", 1),), 3, True).astype(
        rim_cols.dtype
    )
    center = (
        spread[:, 3 : breadth + 3]
        + jnp.pad(rim_cycle[:, :3], ((0, 0), (0, breadth - 3), (0, 0)))
        + jnp.pad(rim_cycle[:, 9:], ((0, 0), (breadth - 3, 0), (0, 0)))
    )
    edge_rows = jnp.concatenate([center[:3], center[height + 3 :]], axis=0)
    edge_cycle = with_halo(edge_rows.astype(jnp.bfloat16), (("ja", 0),), 3, False).astype(
        edge_rows.dtype
    )
    top_grad = center[height + 3 :]
    carried = across_fold(top_grad.astype(jnp.bfloat16), "ia")
    fold_out = pick_columns(carried, mirror_local)
    fold_part = jnp.where(at_top, fold_out[::-1], jnp.zeros_like(fold_out))
    interior = (
        center[3 : height + 3]
        + jnp.pad(edge_cycle[:3], ((0, height - 3), (0, 0), (0, 0)))
        + jnp.pad(edge_cycle[9:] + fold_part, ((height - 3, 0), (0, 0), (0, 0)))
    )
    grad_field = (cotangent.astype(jnp.float32) + interior).astype(jnp.bfloat16)
    mine_chunk, shared = scatter_sum(payload, shared)
    proj_up = mine_chunk[:, :rank].T * scale
    proj_down = mine_chunk[:, rank:] * scale
    vec_total = shared[: vec_terms.shape[0]] * scale
    kernel_total = shared[vec_terms.shape[0] :].reshape(kernel_terms.shape) * scale
    return (grad_field, kernel_total, vec_total, proj_up, proj_down)


def solution(mesh):
    placed = (
        P("ja", "ia", None),
        P("ja", "ia", None),
        P(),
        P(),
        P(),
        P(),
        P(),
        P(),
        P(),
        P(),
        P(),
        P("ja", "ia"),
        P("ia"),
        P("ja"),
        P("ja", "ia"),
        P("ja", "ia"),
    )
    return jax.shard_map(
        on_device,
        mesh=mesh,
        in_specs=placed,
        out_specs=(P("ja", "ia", None), P(), P(), P(None, ("ja", "ia")), P(("ja", "ia"), None)),
        check_vma=False,
    )
```

```python
import math

import jax
import jax.numpy as jnp
from jax import lax
from jax.sharding import PartitionSpec as P

K = 7


epsilon = 1e-06


def across_fold(block, axis):
    count = lax.axis_size(axis)
    return lax.ppermute(block, axis, [(i, count - 1 - i) for i in range(count)])


def xor_swap(block, axis, bit):
    count = lax.axis_size(axis)
    return lax.ppermute(block, axis, [(i, i ^ (1 << bit)) for i in range(count)])


def axis_bits(axis):
    count = lax.axis_size(axis)
    bits = count.bit_length() - 1
    assert 1 << bits == count
    return bits


def sum_over(block, axis):
    for bit in range(axis_bits(axis)):
        block = block + xor_swap(block, axis, bit)
    return block


def gather_over(block, axis):
    pos = lax.axis_index(axis)
    for bit in range(axis_bits(axis)):
        other = xor_swap(block, axis, bit)
        low = (pos >> bit) % 2 == 0
        block = jnp.where(low, jnp.concatenate([block, other]), jnp.concatenate([other, block]))
    return block


def scatter_sum(chunks, shared):
    ja_bits, ia_bits = axis_bits("ja"), axis_bits("ia")
    total = ja_bits + ia_bits
    col_count = lax.axis_size("ia")
    rest = chunks.shape[1:]
    block = chunks.reshape((2,) * total + rest)
    dims = {("ja", b): ja_bits - 1 - b for b in range(ja_bits)}
    dims.update({("ia", b): total - 1 - b for b in range(ia_bits)})
    first = [("ja", b) for b in range(ja_bits)][:1]
    later = [("ja", b) for b in range(1, ja_bits)] + [("ia", b) for b in range(ia_bits)]
    order0 = first + later
    order1 = first + (later[1:2] + later[:1] + later[2:] if len(later) >= 2 else later)
    core = lax.axis_index("ja") % 2
    mask = lambda step: (1 << step[1]) * (col_count if step[0] == "ja" else 1)
    mine_bit = lambda step: (lax.axis_index(step[0]) >> step[1]) % 2
    devices = 1 << total
    lanes = rest[-1]
    count = -(-shared.size // lanes)
    count = -(-count // 8) * 8
    rows = jnp.pad(shared.reshape(-1), (0, count * lanes - shared.size)).reshape(count, lanes)
    for at, (step0, step1) in enumerate(zip(order0, order1)):
        if at == 1 and step0 != step1:
            swapped = jnp.swapaxes(block, dims[step0], dims[step1])
            block = jnp.where(core == 0, block, swapped)
        dim = dims[step0]
        mine = jnp.where(core == 0, mine_bit(step0), mine_bit(step1))
        keep = lax.dynamic_index_in_dim(block, mine, axis=dim, keepdims=True)
        send = lax.dynamic_index_in_dim(block, 1 - mine, axis=dim, keepdims=True)
        pairs = []
        for d in range(devices):
            step = step0 if (d // col_count) % 2 == 0 else step1
            pairs.append((d, d ^ mask(step)))
        lanes = send.shape[-1]
        message = jnp.concatenate([send.reshape(-1, lanes), rows], axis=0)
        got = lax.ppermute(message, ("ja", "ia"), pairs)
        block = keep + got[: send.size // lanes].reshape(send.shape)
        rows = rows + got[send.size // lanes :]
    flat = rows.reshape(-1)[: shared.size]
    return block.reshape(rest), flat.reshape(shared.shape)


def with_halo(block, sides, width, periodic):
    for axis, dim in sides:
        count = lax.axis_size(axis)
        forward = [(i, i + 1) for i in range(count - 1)]
        if periodic:
            forward.append((count - 1, 0))
        backward = [(target, source) for source, target in forward]
        low = lax.ppermute(
            lax.slice_in_dim(block, block.shape[dim] - width, None, axis=dim), axis, forward
        )
        high = lax.ppermute(lax.slice_in_dim(block, 0, width, axis=dim), axis, backward)
        block = jnp.concatenate([low, block, high], axis=dim)
    return block


def pick_columns(block, index):
    count = block.shape[1]
    select = (index[:, None] == jnp.arange(count)[None, :]).astype(block.dtype)
    return jnp.einsum("ik,akc->aic", select, block, preferred_element_type=jnp.float32)


def gelu_parts(pre_act):
    cdf = 0.5 * (1.0 + jax.scipy.special.erf(pre_act * 0.7071067811865476))
    dens = jnp.exp(-0.5 * pre_act * pre_act) * 0.3989422804014327
    return (pre_act * cdf, cdf + pre_act * dens)


def on_device(
    field,
    cotangent,
    conv_weight,
    conv_bias,
    norm_gain,
    norm_bias,
    up_weight,
    up_bias,
    down_weight,
    down_bias,
    layer_scale,
    ocean_mask,
    fold_partner,
    row_owner,
    up_projector_copies,
    down_projector_copies,
):
    height, breadth, channels = field.shape
    row_count = lax.axis_size("ja")
    col_count = lax.axis_size("ia")
    row_pos = lax.axis_index("ja")
    col_pos = lax.axis_index("ia")
    at_top = row_pos == row_count - 1
    mirror_local = fold_partner - (col_count - 1 - col_pos) * breadth
    scale = 1.0 / math.sqrt(height * row_count * breadth * col_count)
    top_rows = field[height - 3 :][::-1]
    moved = across_fold(top_rows, "ia")
    fold_in = pick_columns(moved, mirror_local).astype(moved.dtype)
    stacked = with_halo(field, (("ja", 0),), 3, False)
    upper_rows = jnp.where(at_top, fold_in, stacked[height + 3 :])
    extended = jnp.concatenate([stacked[: height + 3], upper_rows], axis=0)
    widened = with_halo(extended, (("ia", 1),), 3, True).astype(jnp.float32)
    copies_both = jnp.stack([up_projector_copies, down_projector_copies])
    mine = col_pos == row_owner[0]
    owned = jnp.where(mine, copies_both, jnp.zeros_like(copies_both))
    for bit in range(min(2, axis_bits("ia"))):
        owned = owned + xor_swap(owned, "ia", bit)
    owned, widened = lax.optimization_barrier((owned, widened))
    conv_out = jnp.zeros((height, breadth, channels), jnp.float32) + conv_bias
    for tap_row in range(K):
        for tap_col in range(K):
            conv_out = (
                conv_out
                + conv_weight[tap_row, tap_col]
                * widened[tap_row : tap_row + height, tap_col : tap_col + breadth]
            )
    hidden_in = conv_out.reshape(-1, channels)
    grad_out = cotangent.reshape(-1, channels).astype(jnp.float32)
    wet_cells = ocean_mask.reshape(-1, 1).astype(jnp.float32)
    mean_val = jnp.mean(hidden_in, axis=-1, keepdims=True)
    centered = hidden_in - mean_val
    variance = jnp.mean(centered * centered, axis=-1, keepdims=True)
    inv_std = 1.0 / jnp.sqrt(variance + epsilon)
    normed = centered * inv_std
    mlp_in = (normed * norm_gain + norm_bias).astype(jnp.bfloat16)
    for bit in range(2, axis_bits("ia")):
        owned = owned + xor_swap(owned, "ia", bit)
    owned, mlp_in = lax.optimization_barrier((owned, mlp_in))
    pre_act = jnp.dot(mlp_in, up_weight, preferred_element_type=jnp.float32) + up_bias
    act_val, slope = gelu_parts(pre_act)
    activated = act_val.astype(jnp.bfloat16)
    full_both = gather_over(owned[None], "ja")
    full_both, activated = lax.optimization_barrier((full_both, activated))
    branch = jnp.dot(activated, down_weight, preferred_element_type=jnp.float32) + down_bias
    out_grad = grad_out * wet_cells * layer_scale
    out_grad_low = out_grad.astype(jnp.bfloat16)
    act_grad = jnp.dot(out_grad_low, down_weight.T, preferred_element_type=jnp.float32)
    pre_grad = (act_grad * slope).astype(jnp.bfloat16)
    in_grad = jnp.dot(pre_grad, up_weight.T, preferred_element_type=jnp.float32)
    scaled_grad = in_grad * norm_gain
    flat_grad = inv_std * (
        scaled_grad
        - jnp.mean(scaled_grad, axis=-1, keepdims=True)
        - normed * jnp.mean(scaled_grad * normed, axis=-1, keepdims=True)
    )
    vec_terms = jnp.stack(
        [
            jnp.sum(flat_grad, 0),
            jnp.sum(in_grad * normed, 0),
            jnp.sum(in_grad, 0),
            jnp.sum(out_grad, 0),
            jnp.sum(grad_out * wet_cells * branch, 0),
        ]
    )
    conv_grad = flat_grad.reshape(height, breadth, channels)
    kernel_terms = lax.conv_general_dilated(
        widened[None],
        conv_grad[:, :, None, :],
        (1, 1),
        "VALID",
        dimension_numbers=("NHWC", "HWIO", "NHWC"),
        feature_group_count=channels,
        precision=lax.Precision.HIGHEST,
    )[0]
    up_proj = full_both[:, 0].reshape(-1, full_both.shape[-1])
    down_proj = full_both[:, 1].reshape(-1, full_both.shape[-1])
    weight_up = jnp.dot(mlp_in.T, pre_grad, preferred_element_type=jnp.float32)
    weight_down = jnp.dot(activated.T, out_grad_low, preferred_element_type=jnp.float32)
    reduced_up = jnp.dot(weight_up.T, up_proj, precision=lax.Precision.HIGHEST)
    reduced_down = jnp.dot(weight_down, down_proj, precision=lax.Precision.HIGHEST)
    devices = row_count * col_count
    hidden, rank = reduced_up.shape
    width = hidden // devices
    shared = jnp.concatenate([vec_terms, kernel_terms.reshape(-1, channels)])
    payload = jnp.concatenate([reduced_up, reduced_down], axis=1).reshape(devices, width, 2 * rank)
    payload, shared, conv_grad = lax.optimization_barrier((payload, shared, conv_grad))
    padded = jnp.pad(conv_grad, ((6, 6), (6, 6), (0, 0)))
    spread = jnp.zeros((height + 6, breadth + 6, channels), jnp.float32)
    for tap_row in range(K):
        for tap_col in range(K):
            spread = (
                spread
                + conv_weight[tap_row, tap_col]
                * padded[
                    6 - tap_row : 6 - tap_row + height + 6, 6 - tap_col : 6 - tap_col + breadth + 6
                ]
            )
    rim_cols = jnp.concatenate([spread[:, :3], spread[:, breadth + 3 :]], axis=1)
    rim_cycle = with_halo(rim_cols.astype(jnp.bfloat16), (("ia", 1),), 3, True).astype(
        rim_cols.dtype
    )
    center = (
        spread[:, 3 : breadth + 3]
        + jnp.pad(rim_cycle[:, :3], ((0, 0), (0, breadth - 3), (0, 0)))
        + jnp.pad(rim_cycle[:, 9:], ((0, 0), (breadth - 3, 0), (0, 0)))
    )
    edge_rows = jnp.concatenate([center[:3], center[height + 3 :]], axis=0)
    edge_cycle = with_halo(edge_rows.astype(jnp.bfloat16), (("ja", 0),), 3, False).astype(
        edge_rows.dtype
    )
    top_grad = center[height + 3 :]
    carried = across_fold(top_grad.astype(jnp.bfloat16), "ia")
    fold_out = pick_columns(carried, mirror_local)
    fold_part = jnp.where(at_top, fold_out[::-1], jnp.zeros_like(fold_out))
    interior = (
        center[3 : height + 3]
        + jnp.pad(edge_cycle[:3], ((0, height - 3), (0, 0), (0, 0)))
        + jnp.pad(edge_cycle[9:] + fold_part, ((height - 3, 0), (0, 0), (0, 0)))
    )
    grad_field = (cotangent.astype(jnp.float32) + interior).astype(jnp.bfloat16)
    mine_chunk, shared = scatter_sum(payload, shared)
    proj_up = mine_chunk[:, :rank].T * scale
    proj_down = mine_chunk[:, rank:] * scale
    vec_total = shared[: vec_terms.shape[0]] * scale
    kernel_total = shared[vec_terms.shape[0] :].reshape(kernel_terms.shape) * scale
    return (grad_field, kernel_total, vec_total, proj_up, proj_down)


def solution(mesh):
    placed = (
        P("ja", "ia", None),
        P("ja", "ia", None),
        P(),
        P(),
        P(),
        P(),
        P(),
        P(),
        P(),
        P(),
        P(),
        P("ja", "ia"),
        P("ia"),
        P("ja"),
        P("ja", "ia"),
        P("ja", "ia"),
    )
    return jax.shard_map(
        on_device,
        mesh=mesh,
        in_specs=placed,
        out_specs=(P("ja", "ia", None), P(), P(), P(None, ("ja", "ia")), P(("ja", "ia"), None)),
        check_vma=False,
    )
```

```python
import math

import jax
import jax.numpy as jnp
from jax import lax
from jax.sharding import PartitionSpec as P

K = 7


epsilon = 1e-06


def across_fold(block, axis):
    count = lax.axis_size(axis)
    return lax.ppermute(block, axis, [(i, count - 1 - i) for i in range(count)])


def xor_swap(block, axis, bit):
    count = lax.axis_size(axis)
    return lax.ppermute(block, axis, [(i, i ^ (1 << bit)) for i in range(count)])


def axis_bits(axis):
    count = lax.axis_size(axis)
    bits = count.bit_length() - 1
    assert 1 << bits == count
    return bits


def sum_over(block, axis):
    for bit in range(axis_bits(axis)):
        block = block + xor_swap(block, axis, bit)
    return block


def gather_over(block, axis):
    pos = lax.axis_index(axis)
    for bit in range(axis_bits(axis)):
        other = xor_swap(block, axis, bit)
        low = (pos >> bit) % 2 == 0
        block = jnp.where(low, jnp.concatenate([block, other]), jnp.concatenate([other, block]))
    return block


def scatter_sum(chunks, shared):
    ja_bits, ia_bits = axis_bits("ja"), axis_bits("ia")
    total = ja_bits + ia_bits
    col_count = lax.axis_size("ia")
    rest = chunks.shape[1:]
    block = chunks.reshape((2,) * total + rest)
    dims = {("ja", b): ja_bits - 1 - b for b in range(ja_bits)}
    dims.update({("ia", b): total - 1 - b for b in range(ia_bits)})
    first = [("ja", b) for b in range(ja_bits)][:1]
    later = [("ja", b) for b in range(1, ja_bits)] + [("ia", b) for b in range(ia_bits)]
    order0 = first + later
    order1 = first + (later[1:2] + later[:1] + later[2:] if len(later) >= 2 else later)
    core = lax.axis_index("ja") % 2
    mask = lambda step: (1 << step[1]) * (col_count if step[0] == "ja" else 1)
    mine_bit = lambda step: (lax.axis_index(step[0]) >> step[1]) % 2
    devices = 1 << total
    lanes = rest[-1]
    count = -(-shared.size // lanes)
    count = -(-count // 8) * 8
    rows = jnp.pad(shared.reshape(-1), (0, count * lanes - shared.size)).reshape(count, lanes)
    for at, (step0, step1) in enumerate(zip(order0, order1)):
        if at == 1 and step0 != step1:
            swapped = jnp.swapaxes(block, dims[step0], dims[step1])
            block = jnp.where(core == 0, block, swapped)
        dim = dims[step0]
        mine = jnp.where(core == 0, mine_bit(step0), mine_bit(step1))
        keep = lax.dynamic_index_in_dim(block, mine, axis=dim, keepdims=True)
        send = lax.dynamic_index_in_dim(block, 1 - mine, axis=dim, keepdims=True)
        pairs = []
        for d in range(devices):
            step = step0 if (d // col_count) % 2 == 0 else step1
            pairs.append((d, d ^ mask(step)))
        lanes = send.shape[-1]
        message = jnp.concatenate([send.reshape(-1, lanes), rows], axis=0)
        got = lax.ppermute(message, ("ja", "ia"), pairs)
        block = keep + got[: send.size // lanes].reshape(send.shape)
        rows = rows + got[send.size // lanes :]
    flat = rows.reshape(-1)[: shared.size]
    return block.reshape(rest), flat.reshape(shared.shape)


def with_halo(block, sides, width, periodic):
    for axis, dim in sides:
        count = lax.axis_size(axis)
        forward = [(i, i + 1) for i in range(count - 1)]
        if periodic:
            forward.append((count - 1, 0))
        backward = [(target, source) for source, target in forward]
        low = lax.ppermute(
            lax.slice_in_dim(block, block.shape[dim] - width, None, axis=dim), axis, forward
        )
        high = lax.ppermute(lax.slice_in_dim(block, 0, width, axis=dim), axis, backward)
        block = jnp.concatenate([low, block, high], axis=dim)
    return block


def pick_columns(block, index):
    count = block.shape[1]
    select = (index[:, None] == jnp.arange(count)[None, :]).astype(block.dtype)
    return jnp.einsum("ik,akc->aic", select, block, preferred_element_type=jnp.float32)


def gelu_parts(pre_act):
    cdf = 0.5 * (1.0 + jax.scipy.special.erf(pre_act * 0.7071067811865476))
    dens = jnp.exp(-0.5 * pre_act * pre_act) * 0.3989422804014327
    return (pre_act * cdf, cdf + pre_act * dens)


def on_device(
    field,
    cotangent,
    conv_weight,
    conv_bias,
    norm_gain,
    norm_bias,
    up_weight,
    up_bias,
    down_weight,
    down_bias,
    layer_scale,
    ocean_mask,
    fold_partner,
    row_owner,
    up_projector_copies,
    down_projector_copies,
):
    height, breadth, channels = field.shape
    row_count = lax.axis_size("ja")
    col_count = lax.axis_size("ia")
    row_pos = lax.axis_index("ja")
    col_pos = lax.axis_index("ia")
    at_top = row_pos == row_count - 1
    mirror_local = fold_partner - (col_count - 1 - col_pos) * breadth
    scale = 1.0 / math.sqrt(height * row_count * breadth * col_count)
    top_rows = field[height - 3 :][::-1]
    moved = across_fold(top_rows, "ia")
    fold_in = pick_columns(moved, mirror_local).astype(moved.dtype)
    stacked = with_halo(field, (("ja", 0),), 3, False)
    upper_rows = jnp.where(at_top, fold_in, stacked[height + 3 :])
    extended = jnp.concatenate([stacked[: height + 3], upper_rows], axis=0)
    widened = with_halo(extended, (("ia", 1),), 3, True).astype(jnp.float32)
    copies_both = jnp.stack([up_projector_copies, down_projector_copies])
    mine = col_pos == row_owner[0]
    owned = jnp.where(mine, copies_both, jnp.zeros_like(copies_both))
    for bit in range(min(2, axis_bits("ia"))):
        owned = owned + xor_swap(owned, "ia", bit)
    owned, widened = lax.optimization_barrier((owned, widened))
    conv_out = jnp.zeros((height, breadth, channels), jnp.float32) + conv_bias
    for tap_row in range(K):
        for tap_col in range(K):
            conv_out = (
                conv_out
                + conv_weight[tap_row, tap_col]
                * widened[tap_row : tap_row + height, tap_col : tap_col + breadth]
            )
    hidden_in = conv_out.reshape(-1, channels)
    grad_out = cotangent.reshape(-1, channels).astype(jnp.float32)
    wet_cells = ocean_mask.reshape(-1, 1).astype(jnp.float32)
    mean_val = jnp.mean(hidden_in, axis=-1, keepdims=True)
    centered = hidden_in - mean_val
    variance = jnp.mean(centered * centered, axis=-1, keepdims=True)
    inv_std = 1.0 / jnp.sqrt(variance + epsilon)
    normed = centered * inv_std
    mlp_in = (normed * norm_gain + norm_bias).astype(jnp.bfloat16)
    for bit in range(2, axis_bits("ia")):
        owned = owned + xor_swap(owned, "ia", bit)
    owned, mlp_in = lax.optimization_barrier((owned, mlp_in))
    pre_act = jnp.dot(mlp_in, up_weight, preferred_element_type=jnp.float32) + up_bias
    act_val, slope = gelu_parts(pre_act)
    activated = act_val.astype(jnp.bfloat16)
    full_both = gather_over(owned[None], "ja")
    full_both, activated = lax.optimization_barrier((full_both, activated))
    branch = jnp.dot(activated, down_weight, preferred_element_type=jnp.float32) + down_bias
    out_grad = grad_out * wet_cells * layer_scale
    out_grad_low = out_grad.astype(jnp.bfloat16)
    act_grad = jnp.dot(out_grad_low, down_weight.T, preferred_element_type=jnp.float32)
    pre_grad = (act_grad * slope).astype(jnp.bfloat16)
    in_grad = jnp.dot(pre_grad, up_weight.T, preferred_element_type=jnp.float32)
    scaled_grad = in_grad * norm_gain
    flat_grad = inv_std * (
        scaled_grad
        - jnp.mean(scaled_grad, axis=-1, keepdims=True)
        - normed * jnp.mean(scaled_grad * normed, axis=-1, keepdims=True)
    )
    vec_terms = jnp.stack(
        [
            jnp.sum(flat_grad, 0),
            jnp.sum(in_grad * normed, 0),
            jnp.sum(in_grad, 0),
            jnp.sum(out_grad, 0),
            jnp.sum(grad_out * wet_cells * branch, 0),
        ]
    )
    conv_grad = flat_grad.reshape(height, breadth, channels)
    kernel_terms = lax.conv_general_dilated(
        widened[None],
        conv_grad[:, :, None, :],
        (1, 1),
        "VALID",
        dimension_numbers=("NHWC", "HWIO", "NHWC"),
        feature_group_count=channels,
        precision=lax.Precision.HIGHEST,
    )[0]
    up_proj = full_both[:, 0].reshape(-1, full_both.shape[-1])
    down_proj = full_both[:, 1].reshape(-1, full_both.shape[-1])
    weight_up = jnp.dot(mlp_in.T, pre_grad, preferred_element_type=jnp.float32)
    weight_down = jnp.dot(activated.T, out_grad_low, preferred_element_type=jnp.float32)
    reduced_up = jnp.dot(weight_up.T, up_proj, precision=lax.Precision.HIGHEST)
    reduced_down = jnp.dot(weight_down, down_proj, precision=lax.Precision.HIGHEST)
    devices = row_count * col_count
    hidden, rank = reduced_up.shape
    width = hidden // devices
    shared = jnp.concatenate([vec_terms, kernel_terms.reshape(-1, channels)])
    payload = jnp.concatenate([reduced_up, reduced_down], axis=1).reshape(devices, width, 2 * rank)
    padded = jnp.pad(conv_grad, ((6, 6), (6, 6), (0, 0)))
    spread = jnp.zeros((height + 6, breadth + 6, channels), jnp.float32)
    for tap_row in range(K):
        for tap_col in range(K):
            spread = (
                spread
                + conv_weight[tap_row, tap_col]
                * padded[
                    6 - tap_row : 6 - tap_row + height + 6, 6 - tap_col : 6 - tap_col + breadth + 6
                ]
            )
    payload, shared, spread = lax.optimization_barrier((payload, shared, spread))
    rim_cols = jnp.concatenate([spread[:, :3], spread[:, breadth + 3 :]], axis=1)
    rim_cycle = with_halo(rim_cols.astype(jnp.bfloat16), (("ia", 1),), 3, True).astype(
        rim_cols.dtype
    )
    center = (
        spread[:, 3 : breadth + 3]
        + jnp.pad(rim_cycle[:, :3], ((0, 0), (0, breadth - 3), (0, 0)))
        + jnp.pad(rim_cycle[:, 9:], ((0, 0), (breadth - 3, 0), (0, 0)))
    )
    edge_rows = jnp.concatenate([center[:3], center[height + 3 :]], axis=0)
    edge_cycle = with_halo(edge_rows.astype(jnp.bfloat16), (("ja", 0),), 3, False).astype(
        edge_rows.dtype
    )
    top_grad = center[height + 3 :]
    carried = across_fold(top_grad.astype(jnp.bfloat16), "ia")
    fold_out = pick_columns(carried, mirror_local)
    fold_part = jnp.where(at_top, fold_out[::-1], jnp.zeros_like(fold_out))
    interior = (
        center[3 : height + 3]
        + jnp.pad(edge_cycle[:3], ((0, height - 3), (0, 0), (0, 0)))
        + jnp.pad(edge_cycle[9:] + fold_part, ((height - 3, 0), (0, 0), (0, 0)))
    )
    grad_field = (cotangent.astype(jnp.float32) + interior).astype(jnp.bfloat16)
    mine_chunk, shared = scatter_sum(payload, shared)
    proj_up = mine_chunk[:, :rank].T * scale
    proj_down = mine_chunk[:, rank:] * scale
    vec_total = shared[: vec_terms.shape[0]] * scale
    kernel_total = shared[vec_terms.shape[0] :].reshape(kernel_terms.shape) * scale
    return (grad_field, kernel_total, vec_total, proj_up, proj_down)


def solution(mesh):
    placed = (
        P("ja", "ia", None),
        P("ja", "ia", None),
        P(),
        P(),
        P(),
        P(),
        P(),
        P(),
        P(),
        P(),
        P(),
        P("ja", "ia"),
        P("ia"),
        P("ja"),
        P("ja", "ia"),
        P("ja", "ia"),
    )
    return jax.shard_map(
        on_device,
        mesh=mesh,
        in_specs=placed,
        out_specs=(P("ja", "ia", None), P(), P(), P(None, ("ja", "ia")), P(("ja", "ia"), None)),
        check_vma=False,
    )
```

```python
import math

import jax
import jax.numpy as jnp
from jax import lax
from jax.sharding import PartitionSpec as P

K = 7


epsilon = 1e-06


def across_fold(block, axis):
    count = lax.axis_size(axis)
    return lax.ppermute(block, axis, [(i, count - 1 - i) for i in range(count)])


def xor_swap(block, axis, bit):
    count = lax.axis_size(axis)
    return lax.ppermute(block, axis, [(i, i ^ (1 << bit)) for i in range(count)])


def axis_bits(axis):
    count = lax.axis_size(axis)
    bits = count.bit_length() - 1
    assert 1 << bits == count
    return bits


def sum_over(block, axis):
    for bit in range(axis_bits(axis)):
        block = block + xor_swap(block, axis, bit)
    return block


def gather_over(block, axis):
    pos = lax.axis_index(axis)
    for bit in range(axis_bits(axis)):
        other = xor_swap(block, axis, bit)
        low = (pos >> bit) % 2 == 0
        block = jnp.where(low, jnp.concatenate([block, other]), jnp.concatenate([other, block]))
    return block


def mesh_steps():
    steps = [("ja", b) for b in range(axis_bits("ja"))]
    return steps + [("ia", b) for b in range(axis_bits("ia"))]


def step_bit(step):
    return (lax.axis_index(step[0]) >> step[1]) % 2


def group_swap(value, group, offset):
    col_count = lax.axis_size("ia")
    devices = lax.axis_size("ja") * col_count
    mask = 0
    for at, (axis, bit) in enumerate(group):
        if (offset >> at) % 2:
            mask ^= (1 << bit) * (col_count if axis == "ja" else 1)
    return lax.ppermute(value, ("ja", "ia"), [(d, d ^ mask) for d in range(devices)])


def group_position(group):
    return sum(step_bit(step) << at for at, step in enumerate(group))


def in_order(own, got, position, size):
    stacked = jnp.stack([own] + got)
    return [lax.dynamic_index_in_dim(stacked, k ^ position, 0, keepdims=False) for k in range(size)]


def group_sum(block, group):
    size = 1 << len(group)
    total = block
    for offset in range(1, size):
        total = total + group_swap(block, group, offset)
    return total


def group_gather(block, group):
    size = 1 << len(group)
    got = [group_swap(block, group, offset) for offset in range(1, size)]
    return jnp.concatenate(in_order(block, got, group_position(group), size))


def scatter_sum(chunks, shared):
    steps = mesh_steps()
    total = len(steps)
    rest = chunks.shape[1:]
    block = chunks.reshape((2,) * total + rest)
    dims = {step: (axis_bits("ja") - 1 - step[1] if step[0] == "ja" else total - 1 - step[1]) for step in steps}
    groups = [steps[:1]] + [steps[1:][at : at + 2] for at in range(0, total - 1, 2)]
    lanes = rest[-1]
    count = -(-shared.size // lanes)
    count = -(-count // 8) * 8
    rows = jnp.pad(shared.reshape(-1), (0, count * lanes - shared.size)).reshape(count, lanes)
    for group in groups:
        size = 1 << len(group)
        bits = [step_bit(step) for step in group]

        def pick(offset):
            out = block
            for at, step in enumerate(group):
                want = bits[at] ^ ((offset >> at) % 2)
                out = lax.dynamic_index_in_dim(out, want, axis=dims[step], keepdims=True)
            return out

        summed = pick(0)
        got_rows = []
        for offset in range(1, size):
            send = pick(offset)
            held = send.size // lanes
            got = group_swap(jnp.concatenate([send.reshape(-1, lanes), rows]), group, offset)
            summed = summed + got[:held].reshape(send.shape)
            got_rows.append(got[held:])
        members = in_order(rows, got_rows, group_position(group), size)
        rows = members[0]
        for value in members[1:]:
            rows = rows + value
        block = summed
    flat = rows.reshape(-1)[: shared.size]
    return block.reshape(rest), flat.reshape(shared.shape)


def with_halo(block, sides, width, periodic):
    for axis, dim in sides:
        count = lax.axis_size(axis)
        forward = [(i, i + 1) for i in range(count - 1)]
        if periodic:
            forward.append((count - 1, 0))
        backward = [(target, source) for source, target in forward]
        low = lax.ppermute(
            lax.slice_in_dim(block, block.shape[dim] - width, None, axis=dim), axis, forward
        )
        high = lax.ppermute(lax.slice_in_dim(block, 0, width, axis=dim), axis, backward)
        block = jnp.concatenate([low, block, high], axis=dim)
    return block


def pick_columns(block, index):
    count = block.shape[1]
    select = (index[:, None] == jnp.arange(count)[None, :]).astype(block.dtype)
    return jnp.einsum("ik,akc->aic", select, block, preferred_element_type=jnp.float32)


def gelu_parts(pre_act):
    cdf = 0.5 * (1.0 + jax.scipy.special.erf(pre_act * 0.7071067811865476))
    dens = jnp.exp(-0.5 * pre_act * pre_act) * 0.3989422804014327
    return (pre_act * cdf, cdf + pre_act * dens)


def on_device(
    field,
    cotangent,
    conv_weight,
    conv_bias,
    norm_gain,
    norm_bias,
    up_weight,
    up_bias,
    down_weight,
    down_bias,
    layer_scale,
    ocean_mask,
    fold_partner,
    row_owner,
    up_projector_copies,
    down_projector_copies,
):
    height, breadth, channels = field.shape
    row_count = lax.axis_size("ja")
    col_count = lax.axis_size("ia")
    row_pos = lax.axis_index("ja")
    col_pos = lax.axis_index("ia")
    at_top = row_pos == row_count - 1
    mirror_local = fold_partner - (col_count - 1 - col_pos) * breadth
    scale = 1.0 / math.sqrt(height * row_count * breadth * col_count)
    top_rows = field[height - 3 :][::-1]
    moved = across_fold(top_rows, "ia")
    fold_in = pick_columns(moved, mirror_local).astype(moved.dtype)
    stacked = with_halo(field, (("ja", 0),), 3, False)
    upper_rows = jnp.where(at_top, fold_in, stacked[height + 3 :])
    extended = jnp.concatenate([stacked[: height + 3], upper_rows], axis=0)
    widened = with_halo(extended, (("ia", 1),), 3, True).astype(jnp.float32)
    copies_both = jnp.stack([up_projector_copies, down_projector_copies])
    mine = col_pos == row_owner[0]
    owned = jnp.where(mine, copies_both, jnp.zeros_like(copies_both))
    ia_steps = [("ia", b) for b in range(axis_bits("ia"))]
    owned = group_sum(owned, ia_steps[:2])
    owned, widened = lax.optimization_barrier((owned, widened))
    conv_out = jnp.zeros((height, breadth, channels), jnp.float32) + conv_bias
    for tap_row in range(K):
        for tap_col in range(K):
            conv_out = (
                conv_out
                + conv_weight[tap_row, tap_col]
                * widened[tap_row : tap_row + height, tap_col : tap_col + breadth]
            )
    hidden_in = conv_out.reshape(-1, channels)
    grad_out = cotangent.reshape(-1, channels).astype(jnp.float32)
    wet_cells = ocean_mask.reshape(-1, 1).astype(jnp.float32)
    mean_val = jnp.mean(hidden_in, axis=-1, keepdims=True)
    centered = hidden_in - mean_val
    variance = jnp.mean(centered * centered, axis=-1, keepdims=True)
    inv_std = 1.0 / jnp.sqrt(variance + epsilon)
    normed = centered * inv_std
    mlp_in = (normed * norm_gain + norm_bias).astype(jnp.bfloat16)
    for at in range(2, len(ia_steps), 2):
        owned = group_sum(owned, ia_steps[at : at + 2])
    owned, mlp_in = lax.optimization_barrier((owned, mlp_in))
    pre_act = jnp.dot(mlp_in, up_weight, preferred_element_type=jnp.float32) + up_bias
    act_val, slope = gelu_parts(pre_act)
    activated = act_val.astype(jnp.bfloat16)
    full_both = owned[None]
    ja_steps = [("ja", b) for b in range(axis_bits("ja"))]
    for at in range(0, len(ja_steps), 2):
        full_both = group_gather(full_both, ja_steps[at : at + 2])
    full_both, activated = lax.optimization_barrier((full_both, activated))
    branch = jnp.dot(activated, down_weight, preferred_element_type=jnp.float32) + down_bias
    out_grad = grad_out * wet_cells * layer_scale
    out_grad_low = out_grad.astype(jnp.bfloat16)
    act_grad = jnp.dot(out_grad_low, down_weight.T, preferred_element_type=jnp.float32)
    pre_grad = (act_grad * slope).astype(jnp.bfloat16)
    in_grad = jnp.dot(pre_grad, up_weight.T, preferred_element_type=jnp.float32)
    scaled_grad = in_grad * norm_gain
    flat_grad = inv_std * (
        scaled_grad
        - jnp.mean(scaled_grad, axis=-1, keepdims=True)
        - normed * jnp.mean(scaled_grad * normed, axis=-1, keepdims=True)
    )
    vec_terms = jnp.stack(
        [
            jnp.sum(flat_grad, 0),
            jnp.sum(in_grad * normed, 0),
            jnp.sum(in_grad, 0),
            jnp.sum(out_grad, 0),
            jnp.sum(grad_out * wet_cells * branch, 0),
        ]
    )
    conv_grad = flat_grad.reshape(height, breadth, channels)
    kernel_terms = lax.conv_general_dilated(
        widened[None],
        conv_grad[:, :, None, :],
        (1, 1),
        "VALID",
        dimension_numbers=("NHWC", "HWIO", "NHWC"),
        feature_group_count=channels,
        precision=lax.Precision.HIGHEST,
    )[0]
    up_proj = full_both[:, 0].reshape(-1, full_both.shape[-1])
    down_proj = full_both[:, 1].reshape(-1, full_both.shape[-1])
    weight_up = jnp.dot(mlp_in.T, pre_grad, preferred_element_type=jnp.float32)
    weight_down = jnp.dot(activated.T, out_grad_low, preferred_element_type=jnp.float32)
    reduced_up = jnp.dot(weight_up.T, up_proj, precision=lax.Precision.HIGHEST)
    reduced_down = jnp.dot(weight_down, down_proj, precision=lax.Precision.HIGHEST)
    devices = row_count * col_count
    hidden, rank = reduced_up.shape
    width = hidden // devices
    shared = jnp.concatenate([vec_terms, kernel_terms.reshape(-1, channels)])
    payload = jnp.concatenate([reduced_up, reduced_down], axis=1).reshape(devices, width, 2 * rank)
    padded = jnp.pad(conv_grad, ((6, 6), (6, 6), (0, 0)))
    spread = jnp.zeros((height + 6, breadth + 6, channels), jnp.float32)
    for tap_row in range(K):
        for tap_col in range(K):
            spread = (
                spread
                + conv_weight[tap_row, tap_col]
                * padded[
                    6 - tap_row : 6 - tap_row + height + 6, 6 - tap_col : 6 - tap_col + breadth + 6
                ]
            )
    payload, shared, spread = lax.optimization_barrier((payload, shared, spread))
    rim_cols = jnp.concatenate([spread[:, :3], spread[:, breadth + 3 :]], axis=1)
    rim_cycle = with_halo(rim_cols.astype(jnp.bfloat16), (("ia", 1),), 3, True).astype(
        rim_cols.dtype
    )
    center = (
        spread[:, 3 : breadth + 3]
        + jnp.pad(rim_cycle[:, :3], ((0, 0), (0, breadth - 3), (0, 0)))
        + jnp.pad(rim_cycle[:, 9:], ((0, 0), (breadth - 3, 0), (0, 0)))
    )
    edge_rows = jnp.concatenate([center[:3], center[height + 3 :]], axis=0)
    edge_cycle = with_halo(edge_rows.astype(jnp.bfloat16), (("ja", 0),), 3, False).astype(
        edge_rows.dtype
    )
    top_grad = center[height + 3 :]
    carried = across_fold(top_grad.astype(jnp.bfloat16), "ia")
    fold_out = pick_columns(carried, mirror_local)
    fold_part = jnp.where(at_top, fold_out[::-1], jnp.zeros_like(fold_out))
    interior = (
        center[3 : height + 3]
        + jnp.pad(edge_cycle[:3], ((0, height - 3), (0, 0), (0, 0)))
        + jnp.pad(edge_cycle[9:] + fold_part, ((height - 3, 0), (0, 0), (0, 0)))
    )
    grad_field = (cotangent.astype(jnp.float32) + interior).astype(jnp.bfloat16)
    mine_chunk, shared = scatter_sum(payload, shared)
    proj_up = mine_chunk[:, :rank].T * scale
    proj_down = mine_chunk[:, rank:] * scale
    vec_total = shared[: vec_terms.shape[0]] * scale
    kernel_total = shared[vec_terms.shape[0] :].reshape(kernel_terms.shape) * scale
    return (grad_field, kernel_total, vec_total, proj_up, proj_down)


def solution(mesh):
    placed = (
        P("ja", "ia", None),
        P("ja", "ia", None),
        P(),
        P(),
        P(),
        P(),
        P(),
        P(),
        P(),
        P(),
        P(),
        P("ja", "ia"),
        P("ia"),
        P("ja"),
        P("ja", "ia"),
        P("ja", "ia"),
    )
    return jax.shard_map(
        on_device,
        mesh=mesh,
        in_specs=placed,
        out_specs=(P("ja", "ia", None), P(), P(), P(None, ("ja", "ia")), P(("ja", "ia"), None)),
        check_vma=False,
    )
```

```python
import math

import jax
import jax.numpy as jnp
from jax import lax
from jax.sharding import PartitionSpec as P

K = 7


epsilon = 1e-06


def across_fold(block, axis):
    count = lax.axis_size(axis)
    return lax.ppermute(block, axis, [(i, count - 1 - i) for i in range(count)])


def xor_swap(block, axis, bit):
    count = lax.axis_size(axis)
    return lax.ppermute(block, axis, [(i, i ^ (1 << bit)) for i in range(count)])


def axis_bits(axis):
    count = lax.axis_size(axis)
    bits = count.bit_length() - 1
    assert 1 << bits == count
    return bits


def sum_over(block, axis):
    for bit in range(axis_bits(axis)):
        block = block + xor_swap(block, axis, bit)
    return block


def gather_over(block, axis):
    pos = lax.axis_index(axis)
    for bit in range(axis_bits(axis)):
        other = xor_swap(block, axis, bit)
        low = (pos >> bit) % 2 == 0
        block = jnp.where(low, jnp.concatenate([block, other]), jnp.concatenate([other, block]))
    return block


def scatter_sum(chunks, shared):
    ja_bits, ia_bits = axis_bits("ja"), axis_bits("ia")
    total = ja_bits + ia_bits
    col_count = lax.axis_size("ia")
    rest = chunks.shape[1:]
    block = chunks.reshape((2,) * total + rest)
    dims = {("ja", b): ja_bits - 1 - b for b in range(ja_bits)}
    dims.update({("ia", b): total - 1 - b for b in range(ia_bits)})
    first = [("ja", b) for b in range(ja_bits)][:1]
    later = [("ja", b) for b in range(1, ja_bits)] + [("ia", b) for b in range(ia_bits)]
    order0 = first + later
    order1 = first + (later[1:2] + later[:1] + later[2:] if len(later) >= 2 else later)
    core = lax.axis_index("ja") % 2
    mask = lambda step: (1 << step[1]) * (col_count if step[0] == "ja" else 1)
    mine_bit = lambda step: (lax.axis_index(step[0]) >> step[1]) % 2
    devices = 1 << total
    lanes = rest[-1]
    count = -(-shared.size // lanes)
    count = -(-count // 8) * 8
    rows = jnp.pad(shared.reshape(-1), (0, count * lanes - shared.size)).reshape(count, lanes)
    for at, (step0, step1) in enumerate(zip(order0, order1)):
        if at == 1 and step0 != step1:
            swapped = jnp.swapaxes(block, dims[step0], dims[step1])
            block = jnp.where(core == 0, block, swapped)
        dim = dims[step0]
        mine = jnp.where(core == 0, mine_bit(step0), mine_bit(step1))
        keep = lax.dynamic_index_in_dim(block, mine, axis=dim, keepdims=True)
        send = lax.dynamic_index_in_dim(block, 1 - mine, axis=dim, keepdims=True)
        pairs = []
        for d in range(devices):
            step = step0 if (d // col_count) % 2 == 0 else step1
            pairs.append((d, d ^ mask(step)))
        lanes = send.shape[-1]
        message = jnp.concatenate([send.reshape(-1, lanes), rows], axis=0)
        got = lax.ppermute(message, ("ja", "ia"), pairs)
        block = keep + got[: send.size // lanes].reshape(send.shape)
        rows = rows + got[send.size // lanes :]
    flat = rows.reshape(-1)[: shared.size]
    return block.reshape(rest), flat.reshape(shared.shape)


def with_halo(block, sides, width, periodic):
    for axis, dim in sides:
        count = lax.axis_size(axis)
        forward = [(i, i + 1) for i in range(count - 1)]
        if periodic:
            forward.append((count - 1, 0))
        backward = [(target, source) for source, target in forward]
        low = lax.ppermute(
            lax.slice_in_dim(block, block.shape[dim] - width, None, axis=dim), axis, forward
        )
        high = lax.ppermute(lax.slice_in_dim(block, 0, width, axis=dim), axis, backward)
        block = jnp.concatenate([low, block, high], axis=dim)
    return block


def pick_columns(block, index):
    count = block.shape[1]
    select = (index[:, None] == jnp.arange(count)[None, :]).astype(block.dtype)
    return jnp.einsum("ik,akc->aic", select, block, preferred_element_type=jnp.float32)


def gelu_parts(pre_act):
    cdf = 0.5 * (1.0 + jax.scipy.special.erf(pre_act * 0.7071067811865476))
    dens = jnp.exp(-0.5 * pre_act * pre_act) * 0.3989422804014327
    return (pre_act * cdf, cdf + pre_act * dens)


def on_device(
    field,
    cotangent,
    conv_weight,
    conv_bias,
    norm_gain,
    norm_bias,
    up_weight,
    up_bias,
    down_weight,
    down_bias,
    layer_scale,
    ocean_mask,
    fold_partner,
    row_owner,
    up_projector_copies,
    down_projector_copies,
):
    height, breadth, channels = field.shape
    row_count = lax.axis_size("ja")
    col_count = lax.axis_size("ia")
    row_pos = lax.axis_index("ja")
    col_pos = lax.axis_index("ia")
    at_top = row_pos == row_count - 1
    mirror_local = fold_partner - (col_count - 1 - col_pos) * breadth
    scale = 1.0 / math.sqrt(height * row_count * breadth * col_count)
    top_rows = field[height - 3 :][::-1]
    moved = across_fold(top_rows, "ia")
    fold_in = pick_columns(moved, mirror_local).astype(moved.dtype)
    stacked = with_halo(field, (("ja", 0),), 3, False)
    upper_rows = jnp.where(at_top, fold_in, stacked[height + 3 :])
    extended = jnp.concatenate([stacked[: height + 3], upper_rows], axis=0)
    widened = with_halo(extended, (("ia", 1),), 3, True).astype(jnp.float32)
    copies_both = jnp.stack([up_projector_copies, down_projector_copies])
    mine = col_pos == row_owner[0]
    owned = jnp.where(mine, copies_both, jnp.zeros_like(copies_both))
    for bit in range(min(2, axis_bits("ia"))):
        owned = owned + xor_swap(owned, "ia", bit)
    owned, widened = lax.optimization_barrier((owned, widened))
    conv_out = jnp.zeros((height, breadth, channels), jnp.float32) + conv_bias
    for tap_row in range(K):
        for tap_col in range(K):
            conv_out = (
                conv_out
                + conv_weight[tap_row, tap_col]
                * widened[tap_row : tap_row + height, tap_col : tap_col + breadth]
            )
    hidden_in = conv_out.reshape(-1, channels)
    grad_out = cotangent.reshape(-1, channels).astype(jnp.float32)
    wet_cells = ocean_mask.reshape(-1, 1).astype(jnp.float32)
    mean_val = jnp.mean(hidden_in, axis=-1, keepdims=True)
    centered = hidden_in - mean_val
    variance = jnp.mean(centered * centered, axis=-1, keepdims=True)
    inv_std = 1.0 / jnp.sqrt(variance + epsilon)
    normed = centered * inv_std
    mlp_in = (normed * norm_gain + norm_bias).astype(jnp.bfloat16)
    for bit in range(2, axis_bits("ia")):
        owned = owned + xor_swap(owned, "ia", bit)
    owned, mlp_in = lax.optimization_barrier((owned, mlp_in))
    pre_act = jnp.dot(mlp_in, up_weight, preferred_element_type=jnp.float32) + up_bias
    act_val, slope = gelu_parts(pre_act)
    activated = act_val.astype(jnp.bfloat16)
    full_both = gather_over(owned[None], "ja")
    branch = jnp.dot(activated, down_weight, preferred_element_type=jnp.float32) + down_bias
    out_grad = grad_out * wet_cells * layer_scale
    out_grad_low = out_grad.astype(jnp.bfloat16)
    act_grad = jnp.dot(out_grad_low, down_weight.T, preferred_element_type=jnp.float32)
    pre_grad = (act_grad * slope).astype(jnp.bfloat16)
    in_grad = jnp.dot(pre_grad, up_weight.T, preferred_element_type=jnp.float32)
    scaled_grad = in_grad * norm_gain
    flat_grad = inv_std * (
        scaled_grad
        - jnp.mean(scaled_grad, axis=-1, keepdims=True)
        - normed * jnp.mean(scaled_grad * normed, axis=-1, keepdims=True)
    )
    vec_terms = jnp.stack(
        [
            jnp.sum(flat_grad, 0),
            jnp.sum(in_grad * normed, 0),
            jnp.sum(in_grad, 0),
            jnp.sum(out_grad, 0),
            jnp.sum(grad_out * wet_cells * branch, 0),
        ]
    )
    conv_grad = flat_grad.reshape(height, breadth, channels)
    kernel_terms = lax.conv_general_dilated(
        widened[None],
        conv_grad[:, :, None, :],
        (1, 1),
        "VALID",
        dimension_numbers=("NHWC", "HWIO", "NHWC"),
        feature_group_count=channels,
        precision=lax.Precision.HIGHEST,
    )[0]
    up_proj = full_both[:, 0].reshape(-1, full_both.shape[-1])
    down_proj = full_both[:, 1].reshape(-1, full_both.shape[-1])
    weight_up = jnp.dot(mlp_in.T, pre_grad, preferred_element_type=jnp.float32)
    weight_down = jnp.dot(activated.T, out_grad_low, preferred_element_type=jnp.float32)
    reduced_up = jnp.dot(weight_up.T, up_proj, precision=lax.Precision.HIGHEST)
    reduced_down = jnp.dot(weight_down, down_proj, precision=lax.Precision.HIGHEST)
    devices = row_count * col_count
    hidden, rank = reduced_up.shape
    width = hidden // devices
    shared = jnp.concatenate([vec_terms, kernel_terms.reshape(-1, channels)])
    payload = jnp.concatenate([reduced_up, reduced_down], axis=1).reshape(devices, width, 2 * rank)
    padded = jnp.pad(conv_grad, ((6, 6), (6, 6), (0, 0)))
    spread = jnp.zeros((height + 6, breadth + 6, channels), jnp.float32)
    for tap_row in range(K):
        for tap_col in range(K):
            spread = (
                spread
                + conv_weight[tap_row, tap_col]
                * padded[
                    6 - tap_row : 6 - tap_row + height + 6, 6 - tap_col : 6 - tap_col + breadth + 6
                ]
            )
    payload, shared, spread = lax.optimization_barrier((payload, shared, spread))
    rim_cols = jnp.concatenate([spread[:, :3], spread[:, breadth + 3 :]], axis=1)
    rim_cycle = with_halo(rim_cols.astype(jnp.bfloat16), (("ia", 1),), 3, True).astype(
        rim_cols.dtype
    )
    center = (
        spread[:, 3 : breadth + 3]
        + jnp.pad(rim_cycle[:, :3], ((0, 0), (0, breadth - 3), (0, 0)))
        + jnp.pad(rim_cycle[:, 9:], ((0, 0), (breadth - 3, 0), (0, 0)))
    )
    edge_rows = jnp.concatenate([center[:3], center[height + 3 :]], axis=0)
    edge_cycle = with_halo(edge_rows.astype(jnp.bfloat16), (("ja", 0),), 3, False).astype(
        edge_rows.dtype
    )
    top_grad = center[height + 3 :]
    carried = across_fold(top_grad.astype(jnp.bfloat16), "ia")
    fold_out = pick_columns(carried, mirror_local)
    fold_part = jnp.where(at_top, fold_out[::-1], jnp.zeros_like(fold_out))
    interior = (
        center[3 : height + 3]
        + jnp.pad(edge_cycle[:3], ((0, height - 3), (0, 0), (0, 0)))
        + jnp.pad(edge_cycle[9:] + fold_part, ((height - 3, 0), (0, 0), (0, 0)))
    )
    grad_field = (cotangent.astype(jnp.float32) + interior).astype(jnp.bfloat16)
    mine_chunk, shared = scatter_sum(payload, shared)
    proj_up = mine_chunk[:, :rank].T * scale
    proj_down = mine_chunk[:, rank:] * scale
    vec_total = shared[: vec_terms.shape[0]] * scale
    kernel_total = shared[vec_terms.shape[0] :].reshape(kernel_terms.shape) * scale
    return (grad_field, kernel_total, vec_total, proj_up, proj_down)


def solution(mesh):
    placed = (
        P("ja", "ia", None),
        P("ja", "ia", None),
        P(),
        P(),
        P(),
        P(),
        P(),
        P(),
        P(),
        P(),
        P(),
        P("ja", "ia"),
        P("ia"),
        P("ja"),
        P("ja", "ia"),
        P("ja", "ia"),
    )
    return jax.shard_map(
        on_device,
        mesh=mesh,
        in_specs=placed,
        out_specs=(P("ja", "ia", None), P(), P(), P(None, ("ja", "ia")), P(("ja", "ia"), None)),
        check_vma=False,
    )
```

```python
import math

import jax
import jax.numpy as jnp
from jax import lax
from jax.sharding import PartitionSpec as P

K = 7


epsilon = 1e-06


def across_fold(block, axis):
    count = lax.axis_size(axis)
    return lax.ppermute(block, axis, [(i, count - 1 - i) for i in range(count)])


def xor_swap(block, axis, bit):
    count = lax.axis_size(axis)
    return lax.ppermute(block, axis, [(i, i ^ (1 << bit)) for i in range(count)])


def axis_bits(axis):
    count = lax.axis_size(axis)
    bits = count.bit_length() - 1
    assert 1 << bits == count
    return bits


def sum_over(block, axis):
    for bit in range(axis_bits(axis)):
        block = block + xor_swap(block, axis, bit)
    return block


def gather_over(block, axis):
    pos = lax.axis_index(axis)
    for bit in range(axis_bits(axis)):
        other = xor_swap(block, axis, bit)
        low = (pos >> bit) % 2 == 0
        block = jnp.where(low, jnp.concatenate([block, other]), jnp.concatenate([other, block]))
    return block


def scatter_sum(parts, shared):
    ja_bits, ia_bits = axis_bits("ja"), axis_bits("ia")
    total = ja_bits + ia_bits
    col_count = lax.axis_size("ia")
    rest = parts[0].shape[1:]
    blocks = [part.reshape((2,) * total + rest) for part in parts]
    dims = {("ja", b): ja_bits - 1 - b for b in range(ja_bits)}
    dims.update({("ia", b): total - 1 - b for b in range(ia_bits)})
    first = [("ja", b) for b in range(ja_bits)][:1]
    later = [("ja", b) for b in range(1, ja_bits)] + [("ia", b) for b in range(ia_bits)]
    order0 = first + later
    order1 = first + (later[1:2] + later[:1] + later[2:] if len(later) >= 2 else later)
    core = lax.axis_index("ja") % 2
    mask = lambda step: (1 << step[1]) * (col_count if step[0] == "ja" else 1)
    mine_bit = lambda step: (lax.axis_index(step[0]) >> step[1]) % 2
    devices = 1 << total
    lanes = rest[-1]
    count = -(-shared.size // lanes)
    count = -(-count // 8) * 8
    rows = jnp.pad(shared.reshape(-1), (0, count * lanes - shared.size)).reshape(count, lanes)
    for at, (step0, step1) in enumerate(zip(order0, order1)):
        if at == 1 and step0 != step1:
            blocks = [
                jnp.where(core == 0, block, jnp.swapaxes(block, dims[step0], dims[step1]))
                for block in blocks
            ]
        dim = dims[step0]
        mine = jnp.where(core == 0, mine_bit(step0), mine_bit(step1))
        keeps = [lax.dynamic_index_in_dim(block, mine, axis=dim, keepdims=True) for block in blocks]
        sends = [lax.dynamic_index_in_dim(block, 1 - mine, axis=dim, keepdims=True) for block in blocks]
        pairs = []
        for d in range(devices):
            step = step0 if (d // col_count) % 2 == 0 else step1
            pairs.append((d, d ^ mask(step)))
        message = jnp.concatenate([send.reshape(-1, lanes) for send in sends] + [rows], axis=0)
        got = lax.ppermute(message, ("ja", "ia"), pairs)
        start = 0
        for at, (keep, send) in enumerate(zip(keeps, sends)):
            held = send.size // lanes
            blocks[at] = keep + got[start : start + held].reshape(send.shape)
            start += held
        rows = rows + got[start:]
    flat = rows.reshape(-1)[: shared.size]
    return [block.reshape(rest) for block in blocks], flat.reshape(shared.shape)


def with_halo(block, sides, width, periodic):
    for axis, dim in sides:
        count = lax.axis_size(axis)
        forward = [(i, i + 1) for i in range(count - 1)]
        if periodic:
            forward.append((count - 1, 0))
        backward = [(target, source) for source, target in forward]
        low = lax.ppermute(
            lax.slice_in_dim(block, block.shape[dim] - width, None, axis=dim), axis, forward
        )
        high = lax.ppermute(lax.slice_in_dim(block, 0, width, axis=dim), axis, backward)
        block = jnp.concatenate([low, block, high], axis=dim)
    return block


def pick_columns(block, index):
    count = block.shape[1]
    select = (index[:, None] == jnp.arange(count)[None, :]).astype(block.dtype)
    return jnp.einsum("ik,akc->aic", select, block, preferred_element_type=jnp.float32)


def gelu_parts(pre_act):
    cdf = 0.5 * (1.0 + jax.scipy.special.erf(pre_act * 0.7071067811865476))
    dens = jnp.exp(-0.5 * pre_act * pre_act) * 0.3989422804014327
    return (pre_act * cdf, cdf + pre_act * dens)


def on_device(
    field,
    cotangent,
    conv_weight,
    conv_bias,
    norm_gain,
    norm_bias,
    up_weight,
    up_bias,
    down_weight,
    down_bias,
    layer_scale,
    ocean_mask,
    fold_partner,
    row_owner,
    up_projector_copies,
    down_projector_copies,
):
    height, breadth, channels = field.shape
    row_count = lax.axis_size("ja")
    col_count = lax.axis_size("ia")
    row_pos = lax.axis_index("ja")
    col_pos = lax.axis_index("ia")
    at_top = row_pos == row_count - 1
    mirror_local = fold_partner - (col_count - 1 - col_pos) * breadth
    scale = 1.0 / math.sqrt(height * row_count * breadth * col_count)
    top_rows = field[height - 3 :][::-1]
    moved = across_fold(top_rows, "ia")
    fold_in = pick_columns(moved, mirror_local).astype(moved.dtype)
    stacked = with_halo(field, (("ja", 0),), 3, False)
    upper_rows = jnp.where(at_top, fold_in, stacked[height + 3 :])
    extended = jnp.concatenate([stacked[: height + 3], upper_rows], axis=0)
    widened = with_halo(extended, (("ia", 1),), 3, True).astype(jnp.float32)
    copies_both = jnp.stack([up_projector_copies, down_projector_copies])
    mine = col_pos == row_owner[0]
    owned = jnp.where(mine, copies_both, jnp.zeros_like(copies_both))
    for bit in range(min(2, axis_bits("ia"))):
        owned = owned + xor_swap(owned, "ia", bit)
    owned, widened = lax.optimization_barrier((owned, widened))
    conv_out = jnp.zeros((height, breadth, channels), jnp.float32) + conv_bias
    for tap_row in range(K):
        for tap_col in range(K):
            conv_out = (
                conv_out
                + conv_weight[tap_row, tap_col]
                * widened[tap_row : tap_row + height, tap_col : tap_col + breadth]
            )
    hidden_in = conv_out.reshape(-1, channels)
    grad_out = cotangent.reshape(-1, channels).astype(jnp.float32)
    wet_cells = ocean_mask.reshape(-1, 1).astype(jnp.float32)
    mean_val = jnp.mean(hidden_in, axis=-1, keepdims=True)
    centered = hidden_in - mean_val
    variance = jnp.mean(centered * centered, axis=-1, keepdims=True)
    inv_std = 1.0 / jnp.sqrt(variance + epsilon)
    normed = centered * inv_std
    mlp_in = (normed * norm_gain + norm_bias).astype(jnp.bfloat16)
    for bit in range(2, axis_bits("ia")):
        owned = owned + xor_swap(owned, "ia", bit)
    owned, mlp_in = lax.optimization_barrier((owned, mlp_in))
    pre_act = jnp.dot(mlp_in, up_weight, preferred_element_type=jnp.float32) + up_bias
    act_val, slope = gelu_parts(pre_act)
    activated = act_val.astype(jnp.bfloat16)
    full_both = gather_over(owned[None], "ja")
    full_both, activated = lax.optimization_barrier((full_both, activated))
    branch = jnp.dot(activated, down_weight, preferred_element_type=jnp.float32) + down_bias
    out_grad = grad_out * wet_cells * layer_scale
    out_grad_low = out_grad.astype(jnp.bfloat16)
    act_grad = jnp.dot(out_grad_low, down_weight.T, preferred_element_type=jnp.float32)
    pre_grad = (act_grad * slope).astype(jnp.bfloat16)
    in_grad = jnp.dot(pre_grad, up_weight.T, preferred_element_type=jnp.float32)
    scaled_grad = in_grad * norm_gain
    flat_grad = inv_std * (
        scaled_grad
        - jnp.mean(scaled_grad, axis=-1, keepdims=True)
        - normed * jnp.mean(scaled_grad * normed, axis=-1, keepdims=True)
    )
    vec_terms = jnp.stack(
        [
            jnp.sum(flat_grad, 0),
            jnp.sum(in_grad * normed, 0),
            jnp.sum(in_grad, 0),
            jnp.sum(out_grad, 0),
            jnp.sum(grad_out * wet_cells * branch, 0),
        ]
    )
    conv_grad = flat_grad.reshape(height, breadth, channels)
    kernel_terms = lax.conv_general_dilated(
        widened[None],
        conv_grad[:, :, None, :],
        (1, 1),
        "VALID",
        dimension_numbers=("NHWC", "HWIO", "NHWC"),
        feature_group_count=channels,
        precision=lax.Precision.HIGHEST,
    )[0]
    up_proj = full_both[:, 0].reshape(-1, full_both.shape[-1])
    down_proj = full_both[:, 1].reshape(-1, full_both.shape[-1])
    weight_up = jnp.dot(mlp_in.T, pre_grad, preferred_element_type=jnp.float32)
    weight_down = jnp.dot(activated.T, out_grad_low, preferred_element_type=jnp.float32)
    reduced_up = jnp.dot(weight_up.T, up_proj, precision=lax.Precision.HIGHEST)
    reduced_down = jnp.dot(weight_down, down_proj, precision=lax.Precision.HIGHEST)
    devices = row_count * col_count
    hidden, rank = reduced_up.shape
    width = hidden // devices
    shared = jnp.concatenate([vec_terms, kernel_terms.reshape(-1, channels)])
    payload = (reduced_up.reshape(devices, width, rank), reduced_down.reshape(devices, width, rank))
    padded = jnp.pad(conv_grad, ((6, 6), (6, 6), (0, 0)))
    spread = jnp.zeros((height + 6, breadth + 6, channels), jnp.float32)
    for tap_row in range(K):
        for tap_col in range(K):
            spread = (
                spread
                + conv_weight[tap_row, tap_col]
                * padded[
                    6 - tap_row : 6 - tap_row + height + 6, 6 - tap_col : 6 - tap_col + breadth + 6
                ]
            )
    payload, shared, spread = lax.optimization_barrier((payload, shared, spread))
    rim_cols = jnp.concatenate([spread[:, :3], spread[:, breadth + 3 :]], axis=1)
    rim_cycle = with_halo(rim_cols.astype(jnp.bfloat16), (("ia", 1),), 3, True).astype(
        rim_cols.dtype
    )
    center = (
        spread[:, 3 : breadth + 3]
        + jnp.pad(rim_cycle[:, :3], ((0, 0), (0, breadth - 3), (0, 0)))
        + jnp.pad(rim_cycle[:, 9:], ((0, 0), (breadth - 3, 0), (0, 0)))
    )
    edge_rows = jnp.concatenate([center[:3], center[height + 3 :]], axis=0)
    edge_cycle = with_halo(edge_rows.astype(jnp.bfloat16), (("ja", 0),), 3, False).astype(
        edge_rows.dtype
    )
    top_grad = center[height + 3 :]
    carried = across_fold(top_grad.astype(jnp.bfloat16), "ia")
    fold_out = pick_columns(carried, mirror_local)
    fold_part = jnp.where(at_top, fold_out[::-1], jnp.zeros_like(fold_out))
    interior = (
        center[3 : height + 3]
        + jnp.pad(edge_cycle[:3], ((0, height - 3), (0, 0), (0, 0)))
        + jnp.pad(edge_cycle[9:] + fold_part, ((height - 3, 0), (0, 0), (0, 0)))
    )
    grad_field = (cotangent.astype(jnp.float32) + interior).astype(jnp.bfloat16)
    (mine_up, mine_down), shared = scatter_sum(payload, shared)
    proj_up = mine_up.T * scale
    proj_down = mine_down * scale
    vec_total = shared[: vec_terms.shape[0]] * scale
    kernel_total = shared[vec_terms.shape[0] :].reshape(kernel_terms.shape) * scale
    return (grad_field, kernel_total, vec_total, proj_up, proj_down)


def solution(mesh):
    placed = (
        P("ja", "ia", None),
        P("ja", "ia", None),
        P(),
        P(),
        P(),
        P(),
        P(),
        P(),
        P(),
        P(),
        P(),
        P("ja", "ia"),
        P("ia"),
        P("ja"),
        P("ja", "ia"),
        P("ja", "ia"),
    )
    return jax.shard_map(
        on_device,
        mesh=mesh,
        in_specs=placed,
        out_specs=(P("ja", "ia", None), P(), P(), P(None, ("ja", "ia")), P(("ja", "ia"), None)),
        check_vma=False,
    )
```

```python
import math

import jax
import jax.numpy as jnp
from jax import lax
from jax.sharding import PartitionSpec as P

K = 7


epsilon = 1e-06


def across_fold(block, axis):
    count = lax.axis_size(axis)
    return lax.ppermute(block, axis, [(i, count - 1 - i) for i in range(count)])


def xor_swap(block, axis, bit):
    count = lax.axis_size(axis)
    return lax.ppermute(block, axis, [(i, i ^ (1 << bit)) for i in range(count)])


def axis_bits(axis):
    count = lax.axis_size(axis)
    bits = count.bit_length() - 1
    assert 1 << bits == count
    return bits


def sum_over(block, axis):
    for bit in range(axis_bits(axis)):
        block = block + xor_swap(block, axis, bit)
    return block


def gather_over(block, axis):
    pos = lax.axis_index(axis)
    for bit in range(axis_bits(axis)):
        other = xor_swap(block, axis, bit)
        low = (pos >> bit) % 2 == 0
        block = jnp.where(low, jnp.concatenate([block, other]), jnp.concatenate([other, block]))
    return block


def scatter_sum(chunks, shared):
    ja_bits, ia_bits = axis_bits("ja"), axis_bits("ia")
    total = ja_bits + ia_bits
    col_count = lax.axis_size("ia")
    rest = chunks.shape[1:]
    block = chunks.reshape((2,) * total + rest)
    dims = {("ja", b): ja_bits - 1 - b for b in range(ja_bits)}
    dims.update({("ia", b): total - 1 - b for b in range(ia_bits)})
    first = [("ja", b) for b in range(ja_bits)][:1]
    later = [("ja", b) for b in range(1, ja_bits)] + [("ia", b) for b in range(ia_bits)]
    order0 = first + later
    order1 = first + (later[1:2] + later[:1] + later[2:] if len(later) >= 2 else later)
    core = lax.axis_index("ja") % 2
    mask = lambda step: (1 << step[1]) * (col_count if step[0] == "ja" else 1)
    mine_bit = lambda step: (lax.axis_index(step[0]) >> step[1]) % 2
    devices = 1 << total
    lanes = rest[-1]
    count = -(-shared.size // lanes)
    count = -(-count // 8) * 8
    rows = jnp.pad(shared.reshape(-1), (0, count * lanes - shared.size)).reshape(count, lanes)
    for at, (step0, step1) in enumerate(zip(order0, order1)):
        if at == 1 and step0 != step1:
            swapped = jnp.swapaxes(block, dims[step0], dims[step1])
            block = jnp.where(core == 0, block, swapped)
        dim = dims[step0]
        mine = jnp.where(core == 0, mine_bit(step0), mine_bit(step1))
        keep = lax.dynamic_index_in_dim(block, mine, axis=dim, keepdims=True)
        send = lax.dynamic_index_in_dim(block, 1 - mine, axis=dim, keepdims=True)
        pairs = []
        for d in range(devices):
            step = step0 if (d // col_count) % 2 == 0 else step1
            pairs.append((d, d ^ mask(step)))
        lanes = send.shape[-1]
        held = send.size // lanes
        balanced = order0[1] != order1[1]
        if balanced and at == 1:
            message = jnp.concatenate([send.reshape(-1, lanes), rows], axis=0)
            got = lax.ppermute(message, ("ja", "ia"), pairs)
            block = keep + got[:held].reshape(send.shape)
            near = got[held:]
        elif balanced and at == 2:
            message = jnp.concatenate([send.reshape(-1, lanes), rows, near], axis=0)
            got = lax.ppermute(message, ("ja", "ia"), pairs)
            block = keep + got[:held].reshape(send.shape)
            far = got[held : held + count]
            corner = got[held + count :]
            pieces = jnp.stack(
                [rows, jnp.where(core == 0, near, far), jnp.where(core == 0, far, near), corner]
            )
            place = mine_bit(order0[1]) + 2 * mine_bit(order0[2])
            rows = lax.dynamic_index_in_dim(pieces, place, 0, keepdims=False)
            for k in range(1, 4):
                rows = rows + lax.dynamic_index_in_dim(pieces, k ^ place, 0, keepdims=False)
        else:
            message = jnp.concatenate([send.reshape(-1, lanes), rows], axis=0)
            got = lax.ppermute(message, ("ja", "ia"), pairs)
            block = keep + got[:held].reshape(send.shape)
            rows = rows + got[held:]
    flat = rows.reshape(-1)[: shared.size]
    return block.reshape(rest), flat.reshape(shared.shape)


def with_halo(block, sides, width, periodic):
    for axis, dim in sides:
        count = lax.axis_size(axis)
        forward = [(i, i + 1) for i in range(count - 1)]
        if periodic:
            forward.append((count - 1, 0))
        backward = [(target, source) for source, target in forward]
        low = lax.ppermute(
            lax.slice_in_dim(block, block.shape[dim] - width, None, axis=dim), axis, forward
        )
        high = lax.ppermute(lax.slice_in_dim(block, 0, width, axis=dim), axis, backward)
        block = jnp.concatenate([low, block, high], axis=dim)
    return block


def pick_columns(block, index):
    count = block.shape[1]
    select = (index[:, None] == jnp.arange(count)[None, :]).astype(block.dtype)
    return jnp.einsum("ik,akc->aic", select, block, preferred_element_type=jnp.float32)


def gelu_parts(pre_act):
    cdf = 0.5 * (1.0 + jax.scipy.special.erf(pre_act * 0.7071067811865476))
    dens = jnp.exp(-0.5 * pre_act * pre_act) * 0.3989422804014327
    return (pre_act * cdf, cdf + pre_act * dens)


def on_device(
    field,
    cotangent,
    conv_weight,
    conv_bias,
    norm_gain,
    norm_bias,
    up_weight,
    up_bias,
    down_weight,
    down_bias,
    layer_scale,
    ocean_mask,
    fold_partner,
    row_owner,
    up_projector_copies,
    down_projector_copies,
):
    height, breadth, channels = field.shape
    row_count = lax.axis_size("ja")
    col_count = lax.axis_size("ia")
    row_pos = lax.axis_index("ja")
    col_pos = lax.axis_index("ia")
    at_top = row_pos == row_count - 1
    mirror_local = fold_partner - (col_count - 1 - col_pos) * breadth
    scale = 1.0 / math.sqrt(height * row_count * breadth * col_count)
    top_rows = field[height - 3 :][::-1]
    moved = across_fold(top_rows, "ia")
    fold_in = pick_columns(moved, mirror_local).astype(moved.dtype)
    stacked = with_halo(field, (("ja", 0),), 3, False)
    upper_rows = jnp.where(at_top, fold_in, stacked[height + 3 :])
    extended = jnp.concatenate([stacked[: height + 3], upper_rows], axis=0)
    widened = with_halo(extended, (("ia", 1),), 3, True).astype(jnp.float32)
    copies_both = jnp.stack([up_projector_copies, down_projector_copies])
    mine = col_pos == row_owner[0]
    owned = jnp.where(mine, copies_both, jnp.zeros_like(copies_both))
    for bit in range(min(2, axis_bits("ia"))):
        owned = owned + xor_swap(owned, "ia", bit)
    owned, widened = lax.optimization_barrier((owned, widened))
    conv_out = jnp.zeros((height, breadth, channels), jnp.float32) + conv_bias
    for tap_row in range(K):
        for tap_col in range(K):
            conv_out = (
                conv_out
                + conv_weight[tap_row, tap_col]
                * widened[tap_row : tap_row + height, tap_col : tap_col + breadth]
            )
    hidden_in = conv_out.reshape(-1, channels)
    grad_out = cotangent.reshape(-1, channels).astype(jnp.float32)
    wet_cells = ocean_mask.reshape(-1, 1).astype(jnp.float32)
    mean_val = jnp.mean(hidden_in, axis=-1, keepdims=True)
    centered = hidden_in - mean_val
    variance = jnp.mean(centered * centered, axis=-1, keepdims=True)
    inv_std = 1.0 / jnp.sqrt(variance + epsilon)
    normed = centered * inv_std
    mlp_in = (normed * norm_gain + norm_bias).astype(jnp.bfloat16)
    for bit in range(2, axis_bits("ia")):
        owned = owned + xor_swap(owned, "ia", bit)
    owned, mlp_in = lax.optimization_barrier((owned, mlp_in))
    pre_act = jnp.dot(mlp_in, up_weight, preferred_element_type=jnp.float32) + up_bias
    act_val, slope = gelu_parts(pre_act)
    activated = act_val.astype(jnp.bfloat16)
    full_both = gather_over(owned[None], "ja")
    full_both, activated = lax.optimization_barrier((full_both, activated))
    branch = jnp.dot(activated, down_weight, preferred_element_type=jnp.float32) + down_bias
    out_grad = grad_out * wet_cells * layer_scale
    out_grad_low = out_grad.astype(jnp.bfloat16)
    act_grad = jnp.dot(out_grad_low, down_weight.T, preferred_element_type=jnp.float32)
    pre_grad = (act_grad * slope).astype(jnp.bfloat16)
    in_grad = jnp.dot(pre_grad, up_weight.T, preferred_element_type=jnp.float32)
    scaled_grad = in_grad * norm_gain
    flat_grad = inv_std * (
        scaled_grad
        - jnp.mean(scaled_grad, axis=-1, keepdims=True)
        - normed * jnp.mean(scaled_grad * normed, axis=-1, keepdims=True)
    )
    vec_terms = jnp.stack(
        [
            jnp.sum(flat_grad, 0),
            jnp.sum(in_grad * normed, 0),
            jnp.sum(in_grad, 0),
            jnp.sum(out_grad, 0),
            jnp.sum(grad_out * wet_cells * branch, 0),
        ]
    )
    conv_grad = flat_grad.reshape(height, breadth, channels)
    kernel_terms = lax.conv_general_dilated(
        widened[None],
        conv_grad[:, :, None, :],
        (1, 1),
        "VALID",
        dimension_numbers=("NHWC", "HWIO", "NHWC"),
        feature_group_count=channels,
        precision=lax.Precision.HIGHEST,
    )[0]
    up_proj = full_both[:, 0].reshape(-1, full_both.shape[-1])
    down_proj = full_both[:, 1].reshape(-1, full_both.shape[-1])
    weight_up = jnp.dot(mlp_in.T, pre_grad, preferred_element_type=jnp.float32)
    weight_down = jnp.dot(activated.T, out_grad_low, preferred_element_type=jnp.float32)
    reduced_up = jnp.dot(weight_up.T, up_proj, precision=lax.Precision.HIGHEST)
    reduced_down = jnp.dot(weight_down, down_proj, precision=lax.Precision.HIGHEST)
    devices = row_count * col_count
    hidden, rank = reduced_up.shape
    width = hidden // devices
    shared = jnp.concatenate([vec_terms, kernel_terms.reshape(-1, channels)])
    payload = jnp.concatenate([reduced_up, reduced_down], axis=1).reshape(devices, width, 2 * rank)
    padded = jnp.pad(conv_grad, ((6, 6), (6, 6), (0, 0)))
    spread = jnp.zeros((height + 6, breadth + 6, channels), jnp.float32)
    for tap_row in range(K):
        for tap_col in range(K):
            spread = (
                spread
                + conv_weight[tap_row, tap_col]
                * padded[
                    6 - tap_row : 6 - tap_row + height + 6, 6 - tap_col : 6 - tap_col + breadth + 6
                ]
            )
    payload, shared, spread = lax.optimization_barrier((payload, shared, spread))
    rim_cols = jnp.concatenate([spread[:, :3], spread[:, breadth + 3 :]], axis=1)
    rim_cycle = with_halo(rim_cols.astype(jnp.bfloat16), (("ia", 1),), 3, True).astype(
        rim_cols.dtype
    )
    center = (
        spread[:, 3 : breadth + 3]
        + jnp.pad(rim_cycle[:, :3], ((0, 0), (0, breadth - 3), (0, 0)))
        + jnp.pad(rim_cycle[:, 9:], ((0, 0), (breadth - 3, 0), (0, 0)))
    )
    edge_rows = jnp.concatenate([center[:3], center[height + 3 :]], axis=0)
    edge_cycle = with_halo(edge_rows.astype(jnp.bfloat16), (("ja", 0),), 3, False).astype(
        edge_rows.dtype
    )
    top_grad = center[height + 3 :]
    carried = across_fold(top_grad.astype(jnp.bfloat16), "ia")
    fold_out = pick_columns(carried, mirror_local)
    fold_part = jnp.where(at_top, fold_out[::-1], jnp.zeros_like(fold_out))
    interior = (
        center[3 : height + 3]
        + jnp.pad(edge_cycle[:3], ((0, height - 3), (0, 0), (0, 0)))
        + jnp.pad(edge_cycle[9:] + fold_part, ((height - 3, 0), (0, 0), (0, 0)))
    )
    grad_field = (cotangent.astype(jnp.float32) + interior).astype(jnp.bfloat16)
    mine_chunk, shared = scatter_sum(payload, shared)
    proj_up = mine_chunk[:, :rank].T * scale
    proj_down = mine_chunk[:, rank:] * scale
    vec_total = shared[: vec_terms.shape[0]] * scale
    kernel_total = shared[vec_terms.shape[0] :].reshape(kernel_terms.shape) * scale
    return (grad_field, kernel_total, vec_total, proj_up, proj_down)


def solution(mesh):
    placed = (
        P("ja", "ia", None),
        P("ja", "ia", None),
        P(),
        P(),
        P(),
        P(),
        P(),
        P(),
        P(),
        P(),
        P(),
        P("ja", "ia"),
        P("ia"),
        P("ja"),
        P("ja", "ia"),
        P("ja", "ia"),
    )
    return jax.shard_map(
        on_device,
        mesh=mesh,
        in_specs=placed,
        out_specs=(P("ja", "ia", None), P(), P(), P(None, ("ja", "ia")), P(("ja", "ia"), None)),
        check_vma=False,
    )
```

```python
import math

import jax
import jax.numpy as jnp
from jax import lax
from jax.sharding import PartitionSpec as P

K = 7


epsilon = 1e-06


def across_fold(block, axis):
    count = lax.axis_size(axis)
    return lax.ppermute(block, axis, [(i, count - 1 - i) for i in range(count)])


def xor_swap(block, axis, bit):
    count = lax.axis_size(axis)
    return lax.ppermute(block, axis, [(i, i ^ (1 << bit)) for i in range(count)])


def axis_bits(axis):
    count = lax.axis_size(axis)
    bits = count.bit_length() - 1
    assert 1 << bits == count
    return bits


def sum_over(block, axis):
    for bit in range(axis_bits(axis)):
        block = block + xor_swap(block, axis, bit)
    return block


def gather_over(block, axis):
    pos = lax.axis_index(axis)
    for bit in range(axis_bits(axis)):
        other = xor_swap(block, axis, bit)
        low = (pos >> bit) % 2 == 0
        block = jnp.where(low, jnp.concatenate([block, other]), jnp.concatenate([other, block]))
    return block


def scatter_sum(chunks, shared):
    ja_bits, ia_bits = axis_bits("ja"), axis_bits("ia")
    total = ja_bits + ia_bits
    col_count = lax.axis_size("ia")
    rest = chunks.shape[1:]
    block = chunks.reshape((2,) * total + rest)
    dims = {("ja", b): ja_bits - 1 - b for b in range(ja_bits)}
    dims.update({("ia", b): total - 1 - b for b in range(ia_bits)})
    first = [("ja", b) for b in range(ja_bits)][:1]
    ia_order = list(range(min(1, ia_bits))) + list(range(ia_bits - 1, 0, -1))
    later = [("ja", b) for b in range(1, ja_bits)] + [("ia", b) for b in ia_order]
    order0 = first + later
    order1 = first + (later[1:2] + later[:1] + later[2:] if len(later) >= 2 else later)
    core = lax.axis_index("ja") % 2
    mask = lambda step: (1 << step[1]) * (col_count if step[0] == "ja" else 1)
    mine_bit = lambda step: (lax.axis_index(step[0]) >> step[1]) % 2
    devices = 1 << total
    lanes = rest[-1]
    count = -(-shared.size // lanes)
    count = -(-count // 8) * 8
    rows = jnp.pad(shared.reshape(-1), (0, count * lanes - shared.size)).reshape(count, lanes)
    for at, (step0, step1) in enumerate(zip(order0, order1)):
        if at == 1 and step0 != step1:
            swapped = jnp.swapaxes(block, dims[step0], dims[step1])
            block = jnp.where(core == 0, block, swapped)
        dim = dims[step0]
        mine = jnp.where(core == 0, mine_bit(step0), mine_bit(step1))
        keep = lax.dynamic_index_in_dim(block, mine, axis=dim, keepdims=True)
        send = lax.dynamic_index_in_dim(block, 1 - mine, axis=dim, keepdims=True)
        pairs = []
        for d in range(devices):
            step = step0 if (d // col_count) % 2 == 0 else step1
            pairs.append((d, d ^ mask(step)))
        lanes = send.shape[-1]
        message = jnp.concatenate([send.reshape(-1, lanes), rows], axis=0)
        got = lax.ppermute(message, ("ja", "ia"), pairs)
        block = keep + got[: send.size // lanes].reshape(send.shape)
        rows = rows + got[send.size // lanes :]
    flat = rows.reshape(-1)[: shared.size]
    return block.reshape(rest), flat.reshape(shared.shape)


def with_halo(block, sides, width, periodic):
    for axis, dim in sides:
        count = lax.axis_size(axis)
        forward = [(i, i + 1) for i in range(count - 1)]
        if periodic:
            forward.append((count - 1, 0))
        backward = [(target, source) for source, target in forward]
        low = lax.ppermute(
            lax.slice_in_dim(block, block.shape[dim] - width, None, axis=dim), axis, forward
        )
        high = lax.ppermute(lax.slice_in_dim(block, 0, width, axis=dim), axis, backward)
        block = jnp.concatenate([low, block, high], axis=dim)
    return block


def pick_columns(block, index):
    count = block.shape[1]
    select = (index[:, None] == jnp.arange(count)[None, :]).astype(block.dtype)
    return jnp.einsum("ik,akc->aic", select, block, preferred_element_type=jnp.float32)


def gelu_parts(pre_act):
    cdf = 0.5 * (1.0 + jax.scipy.special.erf(pre_act * 0.7071067811865476))
    dens = jnp.exp(-0.5 * pre_act * pre_act) * 0.3989422804014327
    return (pre_act * cdf, cdf + pre_act * dens)


def on_device(
    field,
    cotangent,
    conv_weight,
    conv_bias,
    norm_gain,
    norm_bias,
    up_weight,
    up_bias,
    down_weight,
    down_bias,
    layer_scale,
    ocean_mask,
    fold_partner,
    row_owner,
    up_projector_copies,
    down_projector_copies,
):
    height, breadth, channels = field.shape
    row_count = lax.axis_size("ja")
    col_count = lax.axis_size("ia")
    row_pos = lax.axis_index("ja")
    col_pos = lax.axis_index("ia")
    at_top = row_pos == row_count - 1
    mirror_local = fold_partner - (col_count - 1 - col_pos) * breadth
    scale = 1.0 / math.sqrt(height * row_count * breadth * col_count)
    top_rows = field[height - 3 :][::-1]
    moved = across_fold(top_rows, "ia")
    fold_in = pick_columns(moved, mirror_local).astype(moved.dtype)
    stacked = with_halo(field, (("ja", 0),), 3, False)
    upper_rows = jnp.where(at_top, fold_in, stacked[height + 3 :])
    extended = jnp.concatenate([stacked[: height + 3], upper_rows], axis=0)
    widened = with_halo(extended, (("ia", 1),), 3, True).astype(jnp.float32)
    copies_both = jnp.stack([up_projector_copies, down_projector_copies])
    mine = col_pos == row_owner[0]
    owned = jnp.where(mine, copies_both, jnp.zeros_like(copies_both))
    for bit in range(min(2, axis_bits("ia"))):
        owned = owned + xor_swap(owned, "ia", bit)
    owned, widened = lax.optimization_barrier((owned, widened))
    conv_out = jnp.zeros((height, breadth, channels), jnp.float32) + conv_bias
    for tap_row in range(K):
        for tap_col in range(K):
            conv_out = (
                conv_out
                + conv_weight[tap_row, tap_col]
                * widened[tap_row : tap_row + height, tap_col : tap_col + breadth]
            )
    hidden_in = conv_out.reshape(-1, channels)
    grad_out = cotangent.reshape(-1, channels).astype(jnp.float32)
    wet_cells = ocean_mask.reshape(-1, 1).astype(jnp.float32)
    mean_val = jnp.mean(hidden_in, axis=-1, keepdims=True)
    centered = hidden_in - mean_val
    variance = jnp.mean(centered * centered, axis=-1, keepdims=True)
    inv_std = 1.0 / jnp.sqrt(variance + epsilon)
    normed = centered * inv_std
    mlp_in = (normed * norm_gain + norm_bias).astype(jnp.bfloat16)
    for bit in range(2, axis_bits("ia")):
        owned = owned + xor_swap(owned, "ia", bit)
    owned, mlp_in = lax.optimization_barrier((owned, mlp_in))
    pre_act = jnp.dot(mlp_in, up_weight, preferred_element_type=jnp.float32) + up_bias
    act_val, slope = gelu_parts(pre_act)
    activated = act_val.astype(jnp.bfloat16)
    full_both = gather_over(owned[None], "ja")
    full_both, activated = lax.optimization_barrier((full_both, activated))
    branch = jnp.dot(activated, down_weight, preferred_element_type=jnp.float32) + down_bias
    out_grad = grad_out * wet_cells * layer_scale
    out_grad_low = out_grad.astype(jnp.bfloat16)
    act_grad = jnp.dot(out_grad_low, down_weight.T, preferred_element_type=jnp.float32)
    pre_grad = (act_grad * slope).astype(jnp.bfloat16)
    in_grad = jnp.dot(pre_grad, up_weight.T, preferred_element_type=jnp.float32)
    scaled_grad = in_grad * norm_gain
    flat_grad = inv_std * (
        scaled_grad
        - jnp.mean(scaled_grad, axis=-1, keepdims=True)
        - normed * jnp.mean(scaled_grad * normed, axis=-1, keepdims=True)
    )
    vec_terms = jnp.stack(
        [
            jnp.sum(flat_grad, 0),
            jnp.sum(in_grad * normed, 0),
            jnp.sum(in_grad, 0),
            jnp.sum(out_grad, 0),
            jnp.sum(grad_out * wet_cells * branch, 0),
        ]
    )
    conv_grad = flat_grad.reshape(height, breadth, channels)
    kernel_terms = lax.conv_general_dilated(
        widened[None],
        conv_grad[:, :, None, :],
        (1, 1),
        "VALID",
        dimension_numbers=("NHWC", "HWIO", "NHWC"),
        feature_group_count=channels,
        precision=lax.Precision.HIGHEST,
    )[0]
    up_proj = full_both[:, 0].reshape(-1, full_both.shape[-1])
    down_proj = full_both[:, 1].reshape(-1, full_both.shape[-1])
    weight_up = jnp.dot(mlp_in.T, pre_grad, preferred_element_type=jnp.float32)
    weight_down = jnp.dot(activated.T, out_grad_low, preferred_element_type=jnp.float32)
    reduced_up = jnp.dot(weight_up.T, up_proj, precision=lax.Precision.HIGHEST)
    reduced_down = jnp.dot(weight_down, down_proj, precision=lax.Precision.HIGHEST)
    devices = row_count * col_count
    hidden, rank = reduced_up.shape
    width = hidden // devices
    shared = jnp.concatenate([vec_terms, kernel_terms.reshape(-1, channels)])
    payload = jnp.concatenate([reduced_up, reduced_down], axis=1).reshape(devices, width, 2 * rank)
    padded = jnp.pad(conv_grad, ((6, 6), (6, 6), (0, 0)))
    spread = jnp.zeros((height + 6, breadth + 6, channels), jnp.float32)
    for tap_row in range(K):
        for tap_col in range(K):
            spread = (
                spread
                + conv_weight[tap_row, tap_col]
                * padded[
                    6 - tap_row : 6 - tap_row + height + 6, 6 - tap_col : 6 - tap_col + breadth + 6
                ]
            )
    payload, shared, spread = lax.optimization_barrier((payload, shared, spread))
    rim_cols = jnp.concatenate([spread[:, :3], spread[:, breadth + 3 :]], axis=1)
    rim_cycle = with_halo(rim_cols.astype(jnp.bfloat16), (("ia", 1),), 3, True).astype(
        rim_cols.dtype
    )
    center = (
        spread[:, 3 : breadth + 3]
        + jnp.pad(rim_cycle[:, :3], ((0, 0), (0, breadth - 3), (0, 0)))
        + jnp.pad(rim_cycle[:, 9:], ((0, 0), (breadth - 3, 0), (0, 0)))
    )
    edge_rows = jnp.concatenate([center[:3], center[height + 3 :]], axis=0)
    edge_cycle = with_halo(edge_rows.astype(jnp.bfloat16), (("ja", 0),), 3, False).astype(
        edge_rows.dtype
    )
    top_grad = center[height + 3 :]
    carried = across_fold(top_grad.astype(jnp.bfloat16), "ia")
    fold_out = pick_columns(carried, mirror_local)
    fold_part = jnp.where(at_top, fold_out[::-1], jnp.zeros_like(fold_out))
    interior = (
        center[3 : height + 3]
        + jnp.pad(edge_cycle[:3], ((0, height - 3), (0, 0), (0, 0)))
        + jnp.pad(edge_cycle[9:] + fold_part, ((height - 3, 0), (0, 0), (0, 0)))
    )
    grad_field = (cotangent.astype(jnp.float32) + interior).astype(jnp.bfloat16)
    mine_chunk, shared = scatter_sum(payload, shared)
    proj_up = mine_chunk[:, :rank].T * scale
    proj_down = mine_chunk[:, rank:] * scale
    vec_total = shared[: vec_terms.shape[0]] * scale
    kernel_total = shared[vec_terms.shape[0] :].reshape(kernel_terms.shape) * scale
    return (grad_field, kernel_total, vec_total, proj_up, proj_down)


def solution(mesh):
    placed = (
        P("ja", "ia", None),
        P("ja", "ia", None),
        P(),
        P(),
        P(),
        P(),
        P(),
        P(),
        P(),
        P(),
        P(),
        P("ja", "ia"),
        P("ia"),
        P("ja"),
        P("ja", "ia"),
        P("ja", "ia"),
    )
    return jax.shard_map(
        on_device,
        mesh=mesh,
        in_specs=placed,
        out_specs=(P("ja", "ia", None), P(), P(), P(None, ("ja", "ia")), P(("ja", "ia"), None)),
        check_vma=False,
    )
```

```python
import math

import jax
import jax.numpy as jnp
from jax import lax
from jax.sharding import PartitionSpec as P

K = 7


epsilon = 1e-06


def across_fold(block, axis):
    count = lax.axis_size(axis)
    return lax.ppermute(block, axis, [(i, count - 1 - i) for i in range(count)])


def xor_swap(block, axis, bit):
    count = lax.axis_size(axis)
    return lax.ppermute(block, axis, [(i, i ^ (1 << bit)) for i in range(count)])


def axis_bits(axis):
    count = lax.axis_size(axis)
    bits = count.bit_length() - 1
    assert 1 << bits == count
    return bits


def sum_over(block, axis):
    for bit in range(axis_bits(axis)):
        block = block + xor_swap(block, axis, bit)
    return block


def gather_over(block, axis):
    pos = lax.axis_index(axis)
    for bit in range(axis_bits(axis)):
        other = xor_swap(block, axis, bit)
        low = (pos >> bit) % 2 == 0
        block = jnp.where(low, jnp.concatenate([block, other]), jnp.concatenate([other, block]))
    return block


def scatter_sum(chunks, shared):
    ja_bits, ia_bits = axis_bits("ja"), axis_bits("ia")
    total = ja_bits + ia_bits
    col_count = lax.axis_size("ia")
    rest = chunks.shape[1:]
    block = chunks.reshape((2,) * total + rest)
    dims = {("ja", b): ja_bits - 1 - b for b in range(ja_bits)}
    dims.update({("ia", b): total - 1 - b for b in range(ia_bits)})
    first = [("ja", b) for b in range(ja_bits)][:1]
    later = [("ja", b) for b in range(1, ja_bits)] + [("ia", b) for b in range(ia_bits)]
    order0 = first + later
    order1 = first + (later[1:2] + later[:1] + later[3:4] + later[2:3] + later[4:] if len(later) >= 4 else later)
    core = lax.axis_index("ja") % 2
    mask = lambda step: (1 << step[1]) * (col_count if step[0] == "ja" else 1)
    mine_bit = lambda step: (lax.axis_index(step[0]) >> step[1]) % 2
    devices = 1 << total
    lanes = rest[-1]
    count = -(-shared.size // lanes)
    count = -(-count // 8) * 8
    rows = jnp.pad(shared.reshape(-1), (0, count * lanes - shared.size)).reshape(count, lanes)
    for at, (step0, step1) in enumerate(zip(order0, order1)):
        if at in (1, 3) and step0 != step1:
            swapped = jnp.swapaxes(block, dims[step0], dims[step1])
            block = jnp.where(core == 0, block, swapped)
        dim = dims[step0]
        mine = jnp.where(core == 0, mine_bit(step0), mine_bit(step1))
        keep = lax.dynamic_index_in_dim(block, mine, axis=dim, keepdims=True)
        send = lax.dynamic_index_in_dim(block, 1 - mine, axis=dim, keepdims=True)
        pairs = []
        for d in range(devices):
            step = step0 if (d // col_count) % 2 == 0 else step1
            pairs.append((d, d ^ mask(step)))
        lanes = send.shape[-1]
        message = jnp.concatenate([send.reshape(-1, lanes), rows], axis=0)
        got = lax.ppermute(message, ("ja", "ia"), pairs)
        block = keep + got[: send.size // lanes].reshape(send.shape)
        rows = rows + got[send.size // lanes :]
    flat = rows.reshape(-1)[: shared.size]
    return block.reshape(rest), flat.reshape(shared.shape)


def with_halo(block, sides, width, periodic):
    for axis, dim in sides:
        count = lax.axis_size(axis)
        forward = [(i, i + 1) for i in range(count - 1)]
        if periodic:
            forward.append((count - 1, 0))
        backward = [(target, source) for source, target in forward]
        low = lax.ppermute(
            lax.slice_in_dim(block, block.shape[dim] - width, None, axis=dim), axis, forward
        )
        high = lax.ppermute(lax.slice_in_dim(block, 0, width, axis=dim), axis, backward)
        block = jnp.concatenate([low, block, high], axis=dim)
    return block


def pick_columns(block, index):
    count = block.shape[1]
    select = (index[:, None] == jnp.arange(count)[None, :]).astype(block.dtype)
    return jnp.einsum("ik,akc->aic", select, block, preferred_element_type=jnp.float32)


def gelu_parts(pre_act):
    cdf = 0.5 * (1.0 + jax.scipy.special.erf(pre_act * 0.7071067811865476))
    dens = jnp.exp(-0.5 * pre_act * pre_act) * 0.3989422804014327
    return (pre_act * cdf, cdf + pre_act * dens)


def on_device(
    field,
    cotangent,
    conv_weight,
    conv_bias,
    norm_gain,
    norm_bias,
    up_weight,
    up_bias,
    down_weight,
    down_bias,
    layer_scale,
    ocean_mask,
    fold_partner,
    row_owner,
    up_projector_copies,
    down_projector_copies,
):
    height, breadth, channels = field.shape
    row_count = lax.axis_size("ja")
    col_count = lax.axis_size("ia")
    row_pos = lax.axis_index("ja")
    col_pos = lax.axis_index("ia")
    at_top = row_pos == row_count - 1
    mirror_local = fold_partner - (col_count - 1 - col_pos) * breadth
    scale = 1.0 / math.sqrt(height * row_count * breadth * col_count)
    top_rows = field[height - 3 :][::-1]
    moved = across_fold(top_rows, "ia")
    fold_in = pick_columns(moved, mirror_local).astype(moved.dtype)
    stacked = with_halo(field, (("ja", 0),), 3, False)
    upper_rows = jnp.where(at_top, fold_in, stacked[height + 3 :])
    extended = jnp.concatenate([stacked[: height + 3], upper_rows], axis=0)
    widened = with_halo(extended, (("ia", 1),), 3, True).astype(jnp.float32)
    copies_both = jnp.stack([up_projector_copies, down_projector_copies])
    mine = col_pos == row_owner[0]
    owned = jnp.where(mine, copies_both, jnp.zeros_like(copies_both))
    for bit in range(min(2, axis_bits("ia"))):
        owned = owned + xor_swap(owned, "ia", bit)
    owned, widened = lax.optimization_barrier((owned, widened))
    conv_out = jnp.zeros((height, breadth, channels), jnp.float32) + conv_bias
    for tap_row in range(K):
        for tap_col in range(K):
            conv_out = (
                conv_out
                + conv_weight[tap_row, tap_col]
                * widened[tap_row : tap_row + height, tap_col : tap_col + breadth]
            )
    hidden_in = conv_out.reshape(-1, channels)
    grad_out = cotangent.reshape(-1, channels).astype(jnp.float32)
    wet_cells = ocean_mask.reshape(-1, 1).astype(jnp.float32)
    mean_val = jnp.mean(hidden_in, axis=-1, keepdims=True)
    centered = hidden_in - mean_val
    variance = jnp.mean(centered * centered, axis=-1, keepdims=True)
    inv_std = 1.0 / jnp.sqrt(variance + epsilon)
    normed = centered * inv_std
    mlp_in = (normed * norm_gain + norm_bias).astype(jnp.bfloat16)
    for bit in range(2, axis_bits("ia")):
        owned = owned + xor_swap(owned, "ia", bit)
    owned, mlp_in = lax.optimization_barrier((owned, mlp_in))
    pre_act = jnp.dot(mlp_in, up_weight, preferred_element_type=jnp.float32) + up_bias
    act_val, slope = gelu_parts(pre_act)
    activated = act_val.astype(jnp.bfloat16)
    full_both = gather_over(owned[None], "ja")
    full_both, activated = lax.optimization_barrier((full_both, activated))
    branch = jnp.dot(activated, down_weight, preferred_element_type=jnp.float32) + down_bias
    out_grad = grad_out * wet_cells * layer_scale
    out_grad_low = out_grad.astype(jnp.bfloat16)
    act_grad = jnp.dot(out_grad_low, down_weight.T, preferred_element_type=jnp.float32)
    pre_grad = (act_grad * slope).astype(jnp.bfloat16)
    in_grad = jnp.dot(pre_grad, up_weight.T, preferred_element_type=jnp.float32)
    scaled_grad = in_grad * norm_gain
    flat_grad = inv_std * (
        scaled_grad
        - jnp.mean(scaled_grad, axis=-1, keepdims=True)
        - normed * jnp.mean(scaled_grad * normed, axis=-1, keepdims=True)
    )
    vec_terms = jnp.stack(
        [
            jnp.sum(flat_grad, 0),
            jnp.sum(in_grad * normed, 0),
            jnp.sum(in_grad, 0),
            jnp.sum(out_grad, 0),
            jnp.sum(grad_out * wet_cells * branch, 0),
        ]
    )
    conv_grad = flat_grad.reshape(height, breadth, channels)
    kernel_terms = lax.conv_general_dilated(
        widened[None],
        conv_grad[:, :, None, :],
        (1, 1),
        "VALID",
        dimension_numbers=("NHWC", "HWIO", "NHWC"),
        feature_group_count=channels,
        precision=lax.Precision.HIGHEST,
    )[0]
    up_proj = full_both[:, 0].reshape(-1, full_both.shape[-1])
    down_proj = full_both[:, 1].reshape(-1, full_both.shape[-1])
    weight_up = jnp.dot(mlp_in.T, pre_grad, preferred_element_type=jnp.float32)
    weight_down = jnp.dot(activated.T, out_grad_low, preferred_element_type=jnp.float32)
    reduced_up = jnp.dot(weight_up.T, up_proj, precision=lax.Precision.HIGHEST)
    reduced_down = jnp.dot(weight_down, down_proj, precision=lax.Precision.HIGHEST)
    devices = row_count * col_count
    hidden, rank = reduced_up.shape
    width = hidden // devices
    shared = jnp.concatenate([vec_terms, kernel_terms.reshape(-1, channels)])
    payload = jnp.concatenate([reduced_up, reduced_down], axis=1).reshape(devices, width, 2 * rank)
    padded = jnp.pad(conv_grad, ((6, 6), (6, 6), (0, 0)))
    spread = jnp.zeros((height + 6, breadth + 6, channels), jnp.float32)
    for tap_row in range(K):
        for tap_col in range(K):
            spread = (
                spread
                + conv_weight[tap_row, tap_col]
                * padded[
                    6 - tap_row : 6 - tap_row + height + 6, 6 - tap_col : 6 - tap_col + breadth + 6
                ]
            )
    payload, shared, spread = lax.optimization_barrier((payload, shared, spread))
    rim_cols = jnp.concatenate([spread[:, :3], spread[:, breadth + 3 :]], axis=1)
    rim_cycle = with_halo(rim_cols.astype(jnp.bfloat16), (("ia", 1),), 3, True).astype(
        rim_cols.dtype
    )
    center = (
        spread[:, 3 : breadth + 3]
        + jnp.pad(rim_cycle[:, :3], ((0, 0), (0, breadth - 3), (0, 0)))
        + jnp.pad(rim_cycle[:, 9:], ((0, 0), (breadth - 3, 0), (0, 0)))
    )
    edge_rows = jnp.concatenate([center[:3], center[height + 3 :]], axis=0)
    edge_cycle = with_halo(edge_rows.astype(jnp.bfloat16), (("ja", 0),), 3, False).astype(
        edge_rows.dtype
    )
    top_grad = center[height + 3 :]
    carried = across_fold(top_grad.astype(jnp.bfloat16), "ia")
    fold_out = pick_columns(carried, mirror_local)
    fold_part = jnp.where(at_top, fold_out[::-1], jnp.zeros_like(fold_out))
    interior = (
        center[3 : height + 3]
        + jnp.pad(edge_cycle[:3], ((0, height - 3), (0, 0), (0, 0)))
        + jnp.pad(edge_cycle[9:] + fold_part, ((height - 3, 0), (0, 0), (0, 0)))
    )
    grad_field = (cotangent.astype(jnp.float32) + interior).astype(jnp.bfloat16)
    mine_chunk, shared = scatter_sum(payload, shared)
    proj_up = mine_chunk[:, :rank].T * scale
    proj_down = mine_chunk[:, rank:] * scale
    vec_total = shared[: vec_terms.shape[0]] * scale
    kernel_total = shared[vec_terms.shape[0] :].reshape(kernel_terms.shape) * scale
    return (grad_field, kernel_total, vec_total, proj_up, proj_down)


def solution(mesh):
    placed = (
        P("ja", "ia", None),
        P("ja", "ia", None),
        P(),
        P(),
        P(),
        P(),
        P(),
        P(),
        P(),
        P(),
        P(),
        P("ja", "ia"),
        P("ia"),
        P("ja"),
        P("ja", "ia"),
        P("ja", "ia"),
    )
    return jax.shard_map(
        on_device,
        mesh=mesh,
        in_specs=placed,
        out_specs=(P("ja", "ia", None), P(), P(), P(None, ("ja", "ia")), P(("ja", "ia"), None)),
        check_vma=False,
    )
```

```python
import math

import jax
import jax.numpy as jnp
from jax import lax
from jax.sharding import PartitionSpec as P

K = 7


epsilon = 1e-06


def across_fold(block, axis):
    count = lax.axis_size(axis)
    return lax.ppermute(block, axis, [(i, count - 1 - i) for i in range(count)])


def xor_swap(block, axis, bit):
    count = lax.axis_size(axis)
    return lax.ppermute(block, axis, [(i, i ^ (1 << bit)) for i in range(count)])


def axis_bits(axis):
    count = lax.axis_size(axis)
    bits = count.bit_length() - 1
    assert 1 << bits == count
    return bits


def sum_over(block, axis):
    for bit in range(axis_bits(axis)):
        block = block + xor_swap(block, axis, bit)
    return block


def gather_over(block, axis):
    pos = lax.axis_index(axis)
    for bit in range(axis_bits(axis)):
        other = xor_swap(block, axis, bit)
        low = (pos >> bit) % 2 == 0
        block = jnp.where(low, jnp.concatenate([block, other]), jnp.concatenate([other, block]))
    return block


def scatter_sum(chunks, shared):
    ja_bits, ia_bits = axis_bits("ja"), axis_bits("ia")
    total = ja_bits + ia_bits
    col_count = lax.axis_size("ia")
    rest = chunks.shape[1:]
    block = chunks.reshape((2,) * total + rest)
    dims = {("ja", b): ja_bits - 1 - b for b in range(ja_bits)}
    dims.update({("ia", b): total - 1 - b for b in range(ia_bits)})
    first = [("ja", b) for b in range(ja_bits)][:1]
    later = [("ja", b) for b in range(1, ja_bits)] + [("ia", b) for b in range(ia_bits)]
    order0 = first + later
    order1 = first + (later[1:2] + later[:1] + later[3:4] + later[2:3] + later[4:] if len(later) >= 4 else later)
    core = lax.axis_index("ja") % 2
    mask = lambda step: (1 << step[1]) * (col_count if step[0] == "ja" else 1)
    mine_bit = lambda step: (lax.axis_index(step[0]) >> step[1]) % 2
    devices = 1 << total
    lanes = rest[-1]
    count = -(-shared.size // lanes)
    count = -(-count // 8) * 8
    rows = jnp.pad(shared.reshape(-1), (0, count * lanes - shared.size)).reshape(count, lanes)
    for at, (step0, step1) in enumerate(zip(order0, order1)):
        if at in (1, 3) and step0 != step1:
            swapped = jnp.swapaxes(block, dims[step0], dims[step1])
            block = jnp.where(core == 0, block, swapped)
        dim = dims[step0]
        mine = jnp.where(core == 0, mine_bit(step0), mine_bit(step1))
        keep = lax.dynamic_index_in_dim(block, mine, axis=dim, keepdims=True)
        send = lax.dynamic_index_in_dim(block, 1 - mine, axis=dim, keepdims=True)
        pairs = []
        for d in range(devices):
            step = step0 if (d // col_count) % 2 == 0 else step1
            pairs.append((d, d ^ mask(step)))
        lanes = send.shape[-1]
        message = jnp.concatenate([send.reshape(-1, lanes), rows], axis=0)
        got = lax.ppermute(message, ("ja", "ia"), pairs)
        block = keep + got[: send.size // lanes].reshape(send.shape)
        rows = rows + got[send.size // lanes :]
    flat = rows.reshape(-1)[: shared.size]
    return block.reshape(rest), flat.reshape(shared.shape)


def with_halo(block, sides, width, periodic):
    for axis, dim in sides:
        count = lax.axis_size(axis)
        forward = [(i, i + 1) for i in range(count - 1)]
        if periodic:
            forward.append((count - 1, 0))
        backward = [(target, source) for source, target in forward]
        low = lax.ppermute(
            lax.slice_in_dim(block, block.shape[dim] - width, None, axis=dim), axis, forward
        )
        high = lax.ppermute(lax.slice_in_dim(block, 0, width, axis=dim), axis, backward)
        block = jnp.concatenate([low, block, high], axis=dim)
    return block


def pick_columns(block, index):
    count = block.shape[1]
    select = (index[:, None] == jnp.arange(count)[None, :]).astype(block.dtype)
    return jnp.einsum("ik,akc->aic", select, block, preferred_element_type=jnp.float32)


def gelu_parts(pre_act):
    cdf = 0.5 * (1.0 + jax.scipy.special.erf(pre_act * 0.7071067811865476))
    dens = jnp.exp(-0.5 * pre_act * pre_act) * 0.3989422804014327
    return (pre_act * cdf, cdf + pre_act * dens)


def on_device(
    field,
    cotangent,
    conv_weight,
    conv_bias,
    norm_gain,
    norm_bias,
    up_weight,
    up_bias,
    down_weight,
    down_bias,
    layer_scale,
    ocean_mask,
    fold_partner,
    row_owner,
    up_projector_copies,
    down_projector_copies,
):
    height, breadth, channels = field.shape
    row_count = lax.axis_size("ja")
    col_count = lax.axis_size("ia")
    row_pos = lax.axis_index("ja")
    col_pos = lax.axis_index("ia")
    at_top = row_pos == row_count - 1
    mirror_local = fold_partner - (col_count - 1 - col_pos) * breadth
    scale = 1.0 / math.sqrt(height * row_count * breadth * col_count)
    top_rows = field[height - 3 :][::-1]
    moved = across_fold(top_rows, "ia")
    fold_in = pick_columns(moved, mirror_local).astype(moved.dtype)
    stacked = with_halo(field, (("ja", 0),), 3, False)
    upper_rows = jnp.where(at_top, fold_in, stacked[height + 3 :])
    extended = jnp.concatenate([stacked[: height + 3], upper_rows], axis=0)
    widened = with_halo(extended, (("ia", 1),), 3, True).astype(jnp.float32)
    copies_both = jnp.stack([up_projector_copies, down_projector_copies])
    mine = col_pos == row_owner[0]
    owned = jnp.where(mine, copies_both, jnp.zeros_like(copies_both))
    early = list(range(min(2, axis_bits("ia"))))
    devices = row_count * col_count
    for at in range(len(early)):
        pairs = []
        for d in range(devices):
            bit = early[at] if (d // col_count) % 2 == 0 else early[len(early) - 1 - at]
            pairs.append((d, d ^ (1 << bit)))
        owned = owned + lax.ppermute(owned, ("ja", "ia"), pairs)
    owned, widened = lax.optimization_barrier((owned, widened))
    conv_out = jnp.zeros((height, breadth, channels), jnp.float32) + conv_bias
    for tap_row in range(K):
        for tap_col in range(K):
            conv_out = (
                conv_out
                + conv_weight[tap_row, tap_col]
                * widened[tap_row : tap_row + height, tap_col : tap_col + breadth]
            )
    hidden_in = conv_out.reshape(-1, channels)
    grad_out = cotangent.reshape(-1, channels).astype(jnp.float32)
    wet_cells = ocean_mask.reshape(-1, 1).astype(jnp.float32)
    mean_val = jnp.mean(hidden_in, axis=-1, keepdims=True)
    centered = hidden_in - mean_val
    variance = jnp.mean(centered * centered, axis=-1, keepdims=True)
    inv_std = 1.0 / jnp.sqrt(variance + epsilon)
    normed = centered * inv_std
    mlp_in = (normed * norm_gain + norm_bias).astype(jnp.bfloat16)
    for bit in range(2, axis_bits("ia")):
        owned = owned + xor_swap(owned, "ia", bit)
    owned, mlp_in = lax.optimization_barrier((owned, mlp_in))
    pre_act = jnp.dot(mlp_in, up_weight, preferred_element_type=jnp.float32) + up_bias
    act_val, slope = gelu_parts(pre_act)
    activated = act_val.astype(jnp.bfloat16)
    full_both = gather_over(owned[None], "ja")
    full_both, activated = lax.optimization_barrier((full_both, activated))
    branch = jnp.dot(activated, down_weight, preferred_element_type=jnp.float32) + down_bias
    out_grad = grad_out * wet_cells * layer_scale
    out_grad_low = out_grad.astype(jnp.bfloat16)
    act_grad = jnp.dot(out_grad_low, down_weight.T, preferred_element_type=jnp.float32)
    pre_grad = (act_grad * slope).astype(jnp.bfloat16)
    in_grad = jnp.dot(pre_grad, up_weight.T, preferred_element_type=jnp.float32)
    scaled_grad = in_grad * norm_gain
    flat_grad = inv_std * (
        scaled_grad
        - jnp.mean(scaled_grad, axis=-1, keepdims=True)
        - normed * jnp.mean(scaled_grad * normed, axis=-1, keepdims=True)
    )
    vec_terms = jnp.stack(
        [
            jnp.sum(flat_grad, 0),
            jnp.sum(in_grad * normed, 0),
            jnp.sum(in_grad, 0),
            jnp.sum(out_grad, 0),
            jnp.sum(grad_out * wet_cells * branch, 0),
        ]
    )
    conv_grad = flat_grad.reshape(height, breadth, channels)
    kernel_terms = lax.conv_general_dilated(
        widened[None],
        conv_grad[:, :, None, :],
        (1, 1),
        "VALID",
        dimension_numbers=("NHWC", "HWIO", "NHWC"),
        feature_group_count=channels,
        precision=lax.Precision.HIGHEST,
    )[0]
    up_proj = full_both[:, 0].reshape(-1, full_both.shape[-1])
    down_proj = full_both[:, 1].reshape(-1, full_both.shape[-1])
    weight_up = jnp.dot(mlp_in.T, pre_grad, preferred_element_type=jnp.float32)
    weight_down = jnp.dot(activated.T, out_grad_low, preferred_element_type=jnp.float32)
    reduced_up = jnp.dot(weight_up.T, up_proj, precision=lax.Precision.HIGHEST)
    reduced_down = jnp.dot(weight_down, down_proj, precision=lax.Precision.HIGHEST)
    devices = row_count * col_count
    hidden, rank = reduced_up.shape
    width = hidden // devices
    shared = jnp.concatenate([vec_terms, kernel_terms.reshape(-1, channels)])
    payload = jnp.concatenate([reduced_up, reduced_down], axis=1).reshape(devices, width, 2 * rank)
    padded = jnp.pad(conv_grad, ((6, 6), (6, 6), (0, 0)))
    spread = jnp.zeros((height + 6, breadth + 6, channels), jnp.float32)
    for tap_row in range(K):
        for tap_col in range(K):
            spread = (
                spread
                + conv_weight[tap_row, tap_col]
                * padded[
                    6 - tap_row : 6 - tap_row + height + 6, 6 - tap_col : 6 - tap_col + breadth + 6
                ]
            )
    payload, shared, spread = lax.optimization_barrier((payload, shared, spread))
    rim_cols = jnp.concatenate([spread[:, :3], spread[:, breadth + 3 :]], axis=1)
    rim_cycle = with_halo(rim_cols.astype(jnp.bfloat16), (("ia", 1),), 3, True).astype(
        rim_cols.dtype
    )
    center = (
        spread[:, 3 : breadth + 3]
        + jnp.pad(rim_cycle[:, :3], ((0, 0), (0, breadth - 3), (0, 0)))
        + jnp.pad(rim_cycle[:, 9:], ((0, 0), (breadth - 3, 0), (0, 0)))
    )
    edge_rows = jnp.concatenate([center[:3], center[height + 3 :]], axis=0)
    edge_cycle = with_halo(edge_rows.astype(jnp.bfloat16), (("ja", 0),), 3, False).astype(
        edge_rows.dtype
    )
    top_grad = center[height + 3 :]
    carried = across_fold(top_grad.astype(jnp.bfloat16), "ia")
    fold_out = pick_columns(carried, mirror_local)
    fold_part = jnp.where(at_top, fold_out[::-1], jnp.zeros_like(fold_out))
    interior = (
        center[3 : height + 3]
        + jnp.pad(edge_cycle[:3], ((0, height - 3), (0, 0), (0, 0)))
        + jnp.pad(edge_cycle[9:] + fold_part, ((height - 3, 0), (0, 0), (0, 0)))
    )
    grad_field = (cotangent.astype(jnp.float32) + interior).astype(jnp.bfloat16)
    mine_chunk, shared = scatter_sum(payload, shared)
    proj_up = mine_chunk[:, :rank].T * scale
    proj_down = mine_chunk[:, rank:] * scale
    vec_total = shared[: vec_terms.shape[0]] * scale
    kernel_total = shared[vec_terms.shape[0] :].reshape(kernel_terms.shape) * scale
    return (grad_field, kernel_total, vec_total, proj_up, proj_down)


def solution(mesh):
    placed = (
        P("ja", "ia", None),
        P("ja", "ia", None),
        P(),
        P(),
        P(),
        P(),
        P(),
        P(),
        P(),
        P(),
        P(),
        P("ja", "ia"),
        P("ia"),
        P("ja"),
        P("ja", "ia"),
        P("ja", "ia"),
    )
    return jax.shard_map(
        on_device,
        mesh=mesh,
        in_specs=placed,
        out_specs=(P("ja", "ia", None), P(), P(), P(None, ("ja", "ia")), P(("ja", "ia"), None)),
        check_vma=False,
    )
```

```python
import math

import jax
import jax.numpy as jnp
from jax import lax
from jax.sharding import PartitionSpec as P

K = 7


epsilon = 1e-06


def across_fold(block, axis):
    count = lax.axis_size(axis)
    return lax.ppermute(block, axis, [(i, count - 1 - i) for i in range(count)])


def xor_swap(block, axis, bit):
    count = lax.axis_size(axis)
    return lax.ppermute(block, axis, [(i, i ^ (1 << bit)) for i in range(count)])


def axis_bits(axis):
    count = lax.axis_size(axis)
    bits = count.bit_length() - 1
    assert 1 << bits == count
    return bits


def sum_over(block, axis):
    for bit in range(axis_bits(axis)):
        block = block + xor_swap(block, axis, bit)
    return block


def gather_over(block, axis):
    pos = lax.axis_index(axis)
    for bit in range(axis_bits(axis)):
        other = xor_swap(block, axis, bit)
        low = (pos >> bit) % 2 == 0
        block = jnp.where(low, jnp.concatenate([block, other]), jnp.concatenate([other, block]))
    return block


def scatter_sum(chunks, shared):
    ja_bits, ia_bits = axis_bits("ja"), axis_bits("ia")
    total = ja_bits + ia_bits
    col_count = lax.axis_size("ia")
    rest = chunks.shape[1:]
    block = chunks.reshape((2,) * total + rest)
    dims = {("ja", b): ja_bits - 1 - b for b in range(ja_bits)}
    dims.update({("ia", b): total - 1 - b for b in range(ia_bits)})
    first = [("ja", b) for b in range(ja_bits)][:1]
    later = [("ja", b) for b in range(1, ja_bits)] + [("ia", b) for b in range(ia_bits)]
    order0 = first + later
    order1 = first + (later[1:2] + later[:1] + later[3:4] + later[2:3] + later[4:] if len(later) >= 4 else later)
    core = lax.axis_index("ja") % 2
    mask = lambda step: (1 << step[1]) * (col_count if step[0] == "ja" else 1)
    mine_bit = lambda step: (lax.axis_index(step[0]) >> step[1]) % 2
    devices = 1 << total
    lanes = rest[-1]
    count = -(-shared.size // lanes)
    count = -(-count // 8) * 8
    rows = jnp.pad(shared.reshape(-1), (0, count * lanes - shared.size)).reshape(count, lanes)
    for at, (step0, step1) in enumerate(zip(order0, order1)):
        if at in (1, 3) and step0 != step1:
            swapped = jnp.swapaxes(block, dims[step0], dims[step1])
            block = jnp.where(core == 0, block, swapped)
        dim = dims[step0]
        mine = jnp.where(core == 0, mine_bit(step0), mine_bit(step1))
        keep = lax.dynamic_index_in_dim(block, mine, axis=dim, keepdims=True)
        send = lax.dynamic_index_in_dim(block, 1 - mine, axis=dim, keepdims=True)
        pairs = []
        for d in range(devices):
            step = step0 if (d // col_count) % 2 == 0 else step1
            pairs.append((d, d ^ mask(step)))
        lanes = send.shape[-1]
        message = jnp.concatenate([send.reshape(-1, lanes), rows], axis=0)
        got = lax.ppermute(message, ("ja", "ia"), pairs)
        block = keep + got[: send.size // lanes].reshape(send.shape)
        rows = rows + got[send.size // lanes :]
    flat = rows.reshape(-1)[: shared.size]
    return block.reshape(rest), flat.reshape(shared.shape)


def with_halo(block, sides, width, periodic):
    for axis, dim in sides:
        count = lax.axis_size(axis)
        forward = [(i, i + 1) for i in range(count - 1)]
        if periodic:
            forward.append((count - 1, 0))
        backward = [(target, source) for source, target in forward]
        low = lax.ppermute(
            lax.slice_in_dim(block, block.shape[dim] - width, None, axis=dim), axis, forward
        )
        high = lax.ppermute(lax.slice_in_dim(block, 0, width, axis=dim), axis, backward)
        block = jnp.concatenate([low, block, high], axis=dim)
    return block


def pick_columns(block, index):
    count = block.shape[1]
    select = (index[:, None] == jnp.arange(count)[None, :]).astype(block.dtype)
    return jnp.einsum("ik,akc->aic", select, block, preferred_element_type=jnp.float32)


def gelu_parts(pre_act):
    cdf = 0.5 * (1.0 + jax.scipy.special.erf(pre_act * 0.7071067811865476))
    dens = jnp.exp(-0.5 * pre_act * pre_act) * 0.3989422804014327
    return (pre_act * cdf, cdf + pre_act * dens)


def on_device(
    field,
    cotangent,
    conv_weight,
    conv_bias,
    norm_gain,
    norm_bias,
    up_weight,
    up_bias,
    down_weight,
    down_bias,
    layer_scale,
    ocean_mask,
    fold_partner,
    row_owner,
    up_projector_copies,
    down_projector_copies,
):
    height, breadth, channels = field.shape
    row_count = lax.axis_size("ja")
    col_count = lax.axis_size("ia")
    row_pos = lax.axis_index("ja")
    col_pos = lax.axis_index("ia")
    at_top = row_pos == row_count - 1
    mirror_local = fold_partner - (col_count - 1 - col_pos) * breadth
    scale = 1.0 / math.sqrt(height * row_count * breadth * col_count)
    top_rows = field[height - 3 :][::-1]
    moved = across_fold(top_rows, "ia")
    fold_in = pick_columns(moved, mirror_local).astype(moved.dtype)
    stacked = with_halo(field, (("ja", 0),), 3, False)
    upper_rows = jnp.where(at_top, fold_in, stacked[height + 3 :])
    extended = jnp.concatenate([stacked[: height + 3], upper_rows], axis=0)
    widened = with_halo(extended, (("ia", 1),), 3, True).astype(jnp.float32)
    copies_both = jnp.stack([up_projector_copies, down_projector_copies])
    mine = col_pos == row_owner[0]
    owned = jnp.where(mine, copies_both, jnp.zeros_like(copies_both))
    for bit in range(min(2, axis_bits("ia"))):
        owned = owned + xor_swap(owned, "ia", bit)
    conv_out = jnp.zeros((height, breadth, channels), jnp.float32) + conv_bias
    for tap_row in range(K):
        for tap_col in range(K):
            conv_out = (
                conv_out
                + conv_weight[tap_row, tap_col]
                * widened[tap_row : tap_row + height, tap_col : tap_col + breadth]
            )
    hidden_in = conv_out.reshape(-1, channels)
    grad_out = cotangent.reshape(-1, channels).astype(jnp.float32)
    wet_cells = ocean_mask.reshape(-1, 1).astype(jnp.float32)
    mean_val = jnp.mean(hidden_in, axis=-1, keepdims=True)
    centered = hidden_in - mean_val
    variance = jnp.mean(centered * centered, axis=-1, keepdims=True)
    inv_std = 1.0 / jnp.sqrt(variance + epsilon)
    normed = centered * inv_std
    mlp_in = (normed * norm_gain + norm_bias).astype(jnp.bfloat16)
    for bit in range(2, axis_bits("ia")):
        owned = owned + xor_swap(owned, "ia", bit)
    pre_act = jnp.dot(mlp_in, up_weight, preferred_element_type=jnp.float32) + up_bias
    act_val, slope = gelu_parts(pre_act)
    activated = act_val.astype(jnp.bfloat16)
    full_both = gather_over(owned[None], "ja")
    full_both, activated = lax.optimization_barrier((full_both, activated))
    branch = jnp.dot(activated, down_weight, preferred_element_type=jnp.float32) + down_bias
    out_grad = grad_out * wet_cells * layer_scale
    out_grad_low = out_grad.astype(jnp.bfloat16)
    act_grad = jnp.dot(out_grad_low, down_weight.T, preferred_element_type=jnp.float32)
    pre_grad = (act_grad * slope).astype(jnp.bfloat16)
    in_grad = jnp.dot(pre_grad, up_weight.T, preferred_element_type=jnp.float32)
    scaled_grad = in_grad * norm_gain
    flat_grad = inv_std * (
        scaled_grad
        - jnp.mean(scaled_grad, axis=-1, keepdims=True)
        - normed * jnp.mean(scaled_grad * normed, axis=-1, keepdims=True)
    )
    vec_terms = jnp.stack(
        [
            jnp.sum(flat_grad, 0),
            jnp.sum(in_grad * normed, 0),
            jnp.sum(in_grad, 0),
            jnp.sum(out_grad, 0),
            jnp.sum(grad_out * wet_cells * branch, 0),
        ]
    )
    conv_grad = flat_grad.reshape(height, breadth, channels)
    kernel_terms = lax.conv_general_dilated(
        widened[None],
        conv_grad[:, :, None, :],
        (1, 1),
        "VALID",
        dimension_numbers=("NHWC", "HWIO", "NHWC"),
        feature_group_count=channels,
        precision=lax.Precision.HIGHEST,
    )[0]
    up_proj = full_both[:, 0].reshape(-1, full_both.shape[-1])
    down_proj = full_both[:, 1].reshape(-1, full_both.shape[-1])
    weight_up = jnp.dot(mlp_in.T, pre_grad, preferred_element_type=jnp.float32)
    weight_down = jnp.dot(activated.T, out_grad_low, preferred_element_type=jnp.float32)
    reduced_up = jnp.dot(weight_up.T, up_proj, precision=lax.Precision.HIGHEST)
    reduced_down = jnp.dot(weight_down, down_proj, precision=lax.Precision.HIGHEST)
    devices = row_count * col_count
    hidden, rank = reduced_up.shape
    width = hidden // devices
    shared = jnp.concatenate([vec_terms, kernel_terms.reshape(-1, channels)])
    payload = jnp.concatenate([reduced_up, reduced_down], axis=1).reshape(devices, width, 2 * rank)
    padded = jnp.pad(conv_grad, ((6, 6), (6, 6), (0, 0)))
    spread = jnp.zeros((height + 6, breadth + 6, channels), jnp.float32)
    for tap_row in range(K):
        for tap_col in range(K):
            spread = (
                spread
                + conv_weight[tap_row, tap_col]
                * padded[
                    6 - tap_row : 6 - tap_row + height + 6, 6 - tap_col : 6 - tap_col + breadth + 6
                ]
            )
    payload, shared, spread = lax.optimization_barrier((payload, shared, spread))
    rim_cols = jnp.concatenate([spread[:, :3], spread[:, breadth + 3 :]], axis=1)
    rim_cycle = with_halo(rim_cols.astype(jnp.bfloat16), (("ia", 1),), 3, True).astype(
        rim_cols.dtype
    )
    center = (
        spread[:, 3 : breadth + 3]
        + jnp.pad(rim_cycle[:, :3], ((0, 0), (0, breadth - 3), (0, 0)))
        + jnp.pad(rim_cycle[:, 9:], ((0, 0), (breadth - 3, 0), (0, 0)))
    )
    edge_rows = jnp.concatenate([center[:3], center[height + 3 :]], axis=0)
    edge_cycle = with_halo(edge_rows.astype(jnp.bfloat16), (("ja", 0),), 3, False).astype(
        edge_rows.dtype
    )
    top_grad = center[height + 3 :]
    carried = across_fold(top_grad.astype(jnp.bfloat16), "ia")
    fold_out = pick_columns(carried, mirror_local)
    fold_part = jnp.where(at_top, fold_out[::-1], jnp.zeros_like(fold_out))
    interior = (
        center[3 : height + 3]
        + jnp.pad(edge_cycle[:3], ((0, height - 3), (0, 0), (0, 0)))
        + jnp.pad(edge_cycle[9:] + fold_part, ((height - 3, 0), (0, 0), (0, 0)))
    )
    grad_field = (cotangent.astype(jnp.float32) + interior).astype(jnp.bfloat16)
    mine_chunk, shared = scatter_sum(payload, shared)
    proj_up = mine_chunk[:, :rank].T * scale
    proj_down = mine_chunk[:, rank:] * scale
    vec_total = shared[: vec_terms.shape[0]] * scale
    kernel_total = shared[vec_terms.shape[0] :].reshape(kernel_terms.shape) * scale
    return (grad_field, kernel_total, vec_total, proj_up, proj_down)


def solution(mesh):
    placed = (
        P("ja", "ia", None),
        P("ja", "ia", None),
        P(),
        P(),
        P(),
        P(),
        P(),
        P(),
        P(),
        P(),
        P(),
        P("ja", "ia"),
        P("ia"),
        P("ja"),
        P("ja", "ia"),
        P("ja", "ia"),
    )
    return jax.shard_map(
        on_device,
        mesh=mesh,
        in_specs=placed,
        out_specs=(P("ja", "ia", None), P(), P(), P(None, ("ja", "ia")), P(("ja", "ia"), None)),
        check_vma=False,
    )
```

```python
import math

import jax
import jax.numpy as jnp
from jax import lax
from jax.sharding import PartitionSpec as P

K = 7


epsilon = 1e-06


def across_fold(block, axis):
    count = lax.axis_size(axis)
    return lax.ppermute(block, axis, [(i, count - 1 - i) for i in range(count)])


def xor_swap(block, axis, bit):
    count = lax.axis_size(axis)
    return lax.ppermute(block, axis, [(i, i ^ (1 << bit)) for i in range(count)])


def axis_bits(axis):
    count = lax.axis_size(axis)
    bits = count.bit_length() - 1
    assert 1 << bits == count
    return bits


def sum_over(block, axis):
    for bit in range(axis_bits(axis)):
        block = block + xor_swap(block, axis, bit)
    return block


def gather_over(block, axis):
    pos = lax.axis_index(axis)
    for bit in range(axis_bits(axis)):
        other = xor_swap(block, axis, bit)
        low = (pos >> bit) % 2 == 0
        block = jnp.where(low, jnp.concatenate([block, other]), jnp.concatenate([other, block]))
    return block


def scatter_sum(chunks, shared):
    ja_bits, ia_bits = axis_bits("ja"), axis_bits("ia")
    total = ja_bits + ia_bits
    col_count = lax.axis_size("ia")
    rest = chunks.shape[1:]
    block = chunks.reshape((2,) * total + rest)
    dims = {("ja", b): ja_bits - 1 - b for b in range(ja_bits)}
    dims.update({("ia", b): total - 1 - b for b in range(ia_bits)})
    first = [("ja", b) for b in range(ja_bits)][:1]
    later = [("ja", b) for b in range(1, ja_bits)] + [("ia", b) for b in range(ia_bits)]
    order0 = first + later
    order1 = first + (later[1:2] + later[:1] + later[3:4] + later[2:3] + later[4:] if len(later) >= 4 else later)
    core = lax.axis_index("ja") % 2
    mask = lambda step: (1 << step[1]) * (col_count if step[0] == "ja" else 1)
    mine_bit = lambda step: (lax.axis_index(step[0]) >> step[1]) % 2
    devices = 1 << total
    lanes = rest[-1]
    count = -(-shared.size // lanes)
    count = -(-count // 8) * 8
    rows = jnp.pad(shared.reshape(-1), (0, count * lanes - shared.size)).reshape(count, lanes)
    for at, (step0, step1) in enumerate(zip(order0, order1)):
        if at in (1, 3) and step0 != step1:
            swapped = jnp.swapaxes(block, dims[step0], dims[step1])
            block = jnp.where(core == 0, block, swapped)
        dim = dims[step0]
        mine = jnp.where(core == 0, mine_bit(step0), mine_bit(step1))
        keep = lax.dynamic_index_in_dim(block, mine, axis=dim, keepdims=True)
        send = lax.dynamic_index_in_dim(block, 1 - mine, axis=dim, keepdims=True)
        pairs = []
        for d in range(devices):
            step = step0 if (d // col_count) % 2 == 0 else step1
            pairs.append((d, d ^ mask(step)))
        lanes = send.shape[-1]
        message = jnp.concatenate([send.reshape(-1, lanes), rows], axis=0)
        got = lax.ppermute(message, ("ja", "ia"), pairs)
        block = keep + got[: send.size // lanes].reshape(send.shape)
        rows = rows + got[send.size // lanes :]
    flat = rows.reshape(-1)[: shared.size]
    return block.reshape(rest), flat.reshape(shared.shape)


def with_halo(block, sides, width, periodic):
    for axis, dim in sides:
        count = lax.axis_size(axis)
        forward = [(i, i + 1) for i in range(count - 1)]
        if periodic:
            forward.append((count - 1, 0))
        backward = [(target, source) for source, target in forward]
        low = lax.ppermute(
            lax.slice_in_dim(block, block.shape[dim] - width, None, axis=dim), axis, forward
        )
        high = lax.ppermute(lax.slice_in_dim(block, 0, width, axis=dim), axis, backward)
        block = jnp.concatenate([low, block, high], axis=dim)
    return block


def pick_columns(block, index):
    count = block.shape[1]
    select = (index[:, None] == jnp.arange(count)[None, :]).astype(block.dtype)
    return jnp.einsum("ik,akc->aic", select, block, preferred_element_type=jnp.float32)


def gelu_parts(pre_act):
    cdf = 0.5 * (1.0 + jax.scipy.special.erf(pre_act * 0.7071067811865476))
    dens = jnp.exp(-0.5 * pre_act * pre_act) * 0.3989422804014327
    return (pre_act * cdf, cdf + pre_act * dens)


def on_device(
    field,
    cotangent,
    conv_weight,
    conv_bias,
    norm_gain,
    norm_bias,
    up_weight,
    up_bias,
    down_weight,
    down_bias,
    layer_scale,
    ocean_mask,
    fold_partner,
    row_owner,
    up_projector_copies,
    down_projector_copies,
):
    height, breadth, channels = field.shape
    row_count = lax.axis_size("ja")
    col_count = lax.axis_size("ia")
    row_pos = lax.axis_index("ja")
    col_pos = lax.axis_index("ia")
    at_top = row_pos == row_count - 1
    mirror_local = fold_partner - (col_count - 1 - col_pos) * breadth
    scale = 1.0 / math.sqrt(height * row_count * breadth * col_count)
    top_rows = field[height - 3 :][::-1]
    moved = across_fold(top_rows, "ia")
    fold_in = pick_columns(moved, mirror_local).astype(moved.dtype)
    stacked = with_halo(field, (("ja", 0),), 3, False)
    upper_rows = jnp.where(at_top, fold_in, stacked[height + 3 :])
    extended = jnp.concatenate([stacked[: height + 3], upper_rows], axis=0)
    widened = with_halo(extended, (("ia", 1),), 3, True).astype(jnp.float32)
    copies_both = jnp.stack([up_projector_copies, down_projector_copies])
    mine = col_pos == row_owner[0]
    owned = jnp.where(mine, copies_both, jnp.zeros_like(copies_both))
    for bit in range(min(2, axis_bits("ia"))):
        owned = owned + xor_swap(owned, "ia", bit)
    conv_out = jnp.zeros((height, breadth, channels), jnp.float32) + conv_bias
    for tap_row in range(K):
        for tap_col in range(K):
            conv_out = (
                conv_out
                + conv_weight[tap_row, tap_col]
                * widened[tap_row : tap_row + height, tap_col : tap_col + breadth]
            )
    hidden_in = conv_out.reshape(-1, channels)
    grad_out = cotangent.reshape(-1, channels).astype(jnp.float32)
    wet_cells = ocean_mask.reshape(-1, 1).astype(jnp.float32)
    mean_val = jnp.mean(hidden_in, axis=-1, keepdims=True)
    centered = hidden_in - mean_val
    variance = jnp.mean(centered * centered, axis=-1, keepdims=True)
    inv_std = 1.0 / jnp.sqrt(variance + epsilon)
    normed = centered * inv_std
    mlp_in = (normed * norm_gain + norm_bias).astype(jnp.bfloat16)
    for bit in range(2, axis_bits("ia")):
        owned = owned + xor_swap(owned, "ia", bit)
    pre_act = jnp.dot(mlp_in, up_weight, preferred_element_type=jnp.float32) + up_bias
    act_val, slope = gelu_parts(pre_act)
    activated = act_val.astype(jnp.bfloat16)
    full_both = gather_over(owned[None], "ja")
    branch = jnp.dot(activated, down_weight, preferred_element_type=jnp.float32) + down_bias
    out_grad = grad_out * wet_cells * layer_scale
    out_grad_low = out_grad.astype(jnp.bfloat16)
    act_grad = jnp.dot(out_grad_low, down_weight.T, preferred_element_type=jnp.float32)
    pre_grad = (act_grad * slope).astype(jnp.bfloat16)
    in_grad = jnp.dot(pre_grad, up_weight.T, preferred_element_type=jnp.float32)
    scaled_grad = in_grad * norm_gain
    flat_grad = inv_std * (
        scaled_grad
        - jnp.mean(scaled_grad, axis=-1, keepdims=True)
        - normed * jnp.mean(scaled_grad * normed, axis=-1, keepdims=True)
    )
    vec_terms = jnp.stack(
        [
            jnp.sum(flat_grad, 0),
            jnp.sum(in_grad * normed, 0),
            jnp.sum(in_grad, 0),
            jnp.sum(out_grad, 0),
            jnp.sum(grad_out * wet_cells * branch, 0),
        ]
    )
    conv_grad = flat_grad.reshape(height, breadth, channels)
    kernel_terms = lax.conv_general_dilated(
        widened[None],
        conv_grad[:, :, None, :],
        (1, 1),
        "VALID",
        dimension_numbers=("NHWC", "HWIO", "NHWC"),
        feature_group_count=channels,
        precision=lax.Precision.HIGHEST,
    )[0]
    up_proj = full_both[:, 0].reshape(-1, full_both.shape[-1])
    down_proj = full_both[:, 1].reshape(-1, full_both.shape[-1])
    weight_up = jnp.dot(mlp_in.T, pre_grad, preferred_element_type=jnp.float32)
    weight_down = jnp.dot(activated.T, out_grad_low, preferred_element_type=jnp.float32)
    reduced_up = jnp.dot(weight_up.T, up_proj, precision=lax.Precision.HIGHEST)
    reduced_down = jnp.dot(weight_down, down_proj, precision=lax.Precision.HIGHEST)
    devices = row_count * col_count
    hidden, rank = reduced_up.shape
    width = hidden // devices
    shared = jnp.concatenate([vec_terms, kernel_terms.reshape(-1, channels)])
    payload = jnp.concatenate([reduced_up, reduced_down], axis=1).reshape(devices, width, 2 * rank)
    padded = jnp.pad(conv_grad, ((6, 6), (6, 6), (0, 0)))
    spread = jnp.zeros((height + 6, breadth + 6, channels), jnp.float32)
    for tap_row in range(K):
        for tap_col in range(K):
            spread = (
                spread
                + conv_weight[tap_row, tap_col]
                * padded[
                    6 - tap_row : 6 - tap_row + height + 6, 6 - tap_col : 6 - tap_col + breadth + 6
                ]
            )
    payload, shared, spread = lax.optimization_barrier((payload, shared, spread))
    rim_cols = jnp.concatenate([spread[:, :3], spread[:, breadth + 3 :]], axis=1)
    rim_cycle = with_halo(rim_cols.astype(jnp.bfloat16), (("ia", 1),), 3, True).astype(
        rim_cols.dtype
    )
    center = (
        spread[:, 3 : breadth + 3]
        + jnp.pad(rim_cycle[:, :3], ((0, 0), (0, breadth - 3), (0, 0)))
        + jnp.pad(rim_cycle[:, 9:], ((0, 0), (breadth - 3, 0), (0, 0)))
    )
    edge_rows = jnp.concatenate([center[:3], center[height + 3 :]], axis=0)
    edge_cycle = with_halo(edge_rows.astype(jnp.bfloat16), (("ja", 0),), 3, False).astype(
        edge_rows.dtype
    )
    top_grad = center[height + 3 :]
    carried = across_fold(top_grad.astype(jnp.bfloat16), "ia")
    fold_out = pick_columns(carried, mirror_local)
    fold_part = jnp.where(at_top, fold_out[::-1], jnp.zeros_like(fold_out))
    interior = (
        center[3 : height + 3]
        + jnp.pad(edge_cycle[:3], ((0, height - 3), (0, 0), (0, 0)))
        + jnp.pad(edge_cycle[9:] + fold_part, ((height - 3, 0), (0, 0), (0, 0)))
    )
    grad_field = (cotangent.astype(jnp.float32) + interior).astype(jnp.bfloat16)
    mine_chunk, shared = scatter_sum(payload, shared)
    proj_up = mine_chunk[:, :rank].T * scale
    proj_down = mine_chunk[:, rank:] * scale
    vec_total = shared[: vec_terms.shape[0]] * scale
    kernel_total = shared[vec_terms.shape[0] :].reshape(kernel_terms.shape) * scale
    return (grad_field, kernel_total, vec_total, proj_up, proj_down)


def solution(mesh):
    placed = (
        P("ja", "ia", None),
        P("ja", "ia", None),
        P(),
        P(),
        P(),
        P(),
        P(),
        P(),
        P(),
        P(),
        P(),
        P("ja", "ia"),
        P("ia"),
        P("ja"),
        P("ja", "ia"),
        P("ja", "ia"),
    )
    return jax.shard_map(
        on_device,
        mesh=mesh,
        in_specs=placed,
        out_specs=(P("ja", "ia", None), P(), P(), P(None, ("ja", "ia")), P(("ja", "ia"), None)),
        check_vma=False,
    )
```
